512 devices in a mesh: seq: 64 (over y, z_hi, x, core), head: 8 (over z_lo).
Axes of the slice: x: 4, y: 4, z: 16 (z_hi: 2, z_lo: 8; z = z_hi * 8 + z_lo), core: 2. Of those that a mesh axis runs over, the one named last changes fastest.
Arguments:
- cross_q: bfloat16 [512, 2048], P('seq', 'head'), may hold values from -20 to 20
- cross_out: bfloat16 [512, 2048], P('seq', 'head'), may hold values from -0.59765625 to 0.59765625
- cross_grad: bfloat16 [512, 2048], P('seq', 'head'), may hold values from -1800 to 1800
- prefix_k: bfloat16 [8192, 2048], P('seq', 'head'), may hold values from -6 to 6
- prefix_v: bfloat16 [8192, 2048], P('seq', 'head'), may hold values from -6 to 6
- pad_counts: int32 [64], P('seq'), may hold values from 0 to 64, as said below
- self_q: bfloat16 [512, 2048], P(('seq', 'head')), may hold values from -20 to 20
- self_k: bfloat16 [512, 2048], P(('seq', 'head')), may hold values from -6 to 6
- self_v: bfloat16 [512, 2048], P(('seq', 'head')), may hold values from -6 to 6
- self_grad: bfloat16 [512, 2048], P(('seq', 'head')), may hold values from -12 to 12
Outputs:
- cross_dq: bfloat16 [512, 2048], P('seq', 'head')
- prefix_dk: bfloat16 [8192, 2048], P('seq', 'head')
- prefix_dv: bfloat16 [8192, 2048], P('seq', 'head')
- self_dq: bfloat16 [512, 2048], P('seq', 'head')
- self_dk: bfloat16 [512, 2048], P('seq', 'head')
- self_dv: bfloat16 [512, 2048], P('seq', 'head')
The draws below stay inside these ranges and needn't reach their ends.
Inputs may be any that keep to these rules, and one draw needn't show every extreme that they name: `pad_counts`: every shard keeps at least 64 valid tokens; some shard has exactly 64 padded tokens.
All inputs are finite; a program needn't handle non-finite values.
Results may differ from the reference program's by a relative error of at most 0.0086.
Values may be sent and summed in bfloat16 or wider, within the bound.
No kernel may reach another device: no remote copies, remote signals or barrier semaphores. Data moves between devices by JAX's collectives and lax.ppermute only.
A program may use at most 64 MiB of HBM per device.

```python
import jax
import jax.numpy as jnp
from jax import lax

HEADS = 16
HEAD_DIM = 128
D = 2048
TOK_DEV = 128
PREFIX = 8192
LAT = 512
SHARDS = 64
PAD_MAX = 64


def drawn_rows(key, offset, row_count, spread_scale):
    base_rows = jax.random.normal(jax.random.fold_in(key, offset), (row_count, D), jnp.float32)
    return jnp.clip(base_rows, -6.0, 6.0) * spread_scale


def draw_cross_q(key, part):
    query_rows = drawn_rows(key, 21, LAT, 1.5)
    return query_rows.astype(jnp.bfloat16)


def draw_prefix_k(key, part):
    key_rows = drawn_rows(key, 31, PREFIX, 1.0)
    return key_rows.astype(jnp.bfloat16)


def draw_self_q(key, part):
    query_rows = drawn_rows(key, 41, LAT, 1.5)
    return query_rows.astype(jnp.bfloat16)


def draw_self_k(key, part):
    key_rows = drawn_rows(key, 61, LAT, 1.0)
    return key_rows.astype(jnp.bfloat16)


def draw_pad_counts(key, part):
    counts = jax.random.randint(jax.random.fold_in(key, 51), (SHARDS,), 0, PAD_MAX + 1)
    chosen = jax.random.randint(jax.random.fold_in(key, 52), (), 0, SHARDS)
    return jnp.where(jnp.arange(SHARDS) == chosen, PAD_MAX, counts).astype(jnp.int32)


def steps_of(key, shape, shards, low, top_value):
    def one(position, shards_of):
        steps = jax.random.uniform(jax.random.fold_in(jax.random.fold_in(key, 6), position), (shards_of,), jnp.float32, low / len(shards), top_value / len(shards))
        return jnp.repeat(jnp.exp(steps), shape[position] // shards_of).reshape((-1,) + (1,) * (len(shape) - position - 1))

    gain = one(*shards[0])
    for cut in shards[1:]:
        gain = gain * one(*cut)
    return gain


def normal_values(own_key, extent, scale, most, pieces=(), held_as=jnp.bfloat16):
    gain = steps_of(own_key, extent, pieces, -0.22, 0.18) if pieces else 1.0
    array = jax.random.normal(own_key, extent, jnp.float32) * scale * gain
    return jnp.minimum(jnp.maximum(array, -most), most).astype(held_as)


def setup_inputs(seed: int = 0) -> dict:
    key_of = jax.random.split(jax.random.key(seed), 11)
    return {
        "cross_q": draw_cross_q(jax.random.fold_in(key_of[10], 71), 0),
        "cross_out": normal_values(key_of[1], (LAT, D), 0.1, 0.59765625, ((0, 64), (1, 8))),
        "cross_grad": normal_values(key_of[2], (LAT, D), 300.0, 1800.0, ((0, 64), (1, 8))),
        "prefix_k": draw_prefix_k(jax.random.fold_in(key_of[10], 71), 0),
        "prefix_v": normal_values(key_of[4], (PREFIX, D), 1.0, 6.0, ((0, 64), (1, 8))),
        "pad_counts": draw_pad_counts(jax.random.fold_in(key_of[10], 71), 0),
        "self_q": draw_self_q(jax.random.fold_in(key_of[10], 71), 0),
        "self_k": draw_self_k(jax.random.fold_in(key_of[10], 71), 0),
        "self_v": normal_values(key_of[8], (LAT, D), 1.0, 6.0, ((0, 512),)),
        "self_grad": normal_values(key_of[9], (LAT, D), 2.0, 12.0, ((0, 512),)),
    }


def column_block(matrix, head_index):
    return lax.dynamic_slice_in_dim(matrix, head_index * HEAD_DIM, HEAD_DIM, 1)

def scores_grad(weights, grad_rows, value_rows, row_dot, score_scale):
    grad_probs = jnp.dot(grad_rows, value_rows.T, preferred_element_type=jnp.float32)
    return (weights * (grad_probs - row_dot) * score_scale).astype(jnp.bfloat16)

def join_heads(stacked):
    return jnp.transpose(stacked, (1, 0, 2)).reshape(stacked.shape[1], HEADS * HEAD_DIM)

def reference(cross_q, cross_out, cross_grad, prefix_k, prefix_v, pad_counts, self_q, self_k, self_v, self_grad):
    score_scale = HEAD_DIM ** (-0.5)
    positions = jnp.arange(PREFIX, dtype=jnp.int32)
    shard_pad = jnp.repeat(pad_counts, TOK_DEV, total_repeat_length=PREFIX)
    valid_keys = positions % TOK_DEV < TOK_DEV - shard_pad
    products = cross_grad.astype(jnp.float32) * cross_out.astype(jnp.float32)
    row_dots = lax.optimization_barrier(jnp.sum(products.reshape(LAT, HEADS, HEAD_DIM), axis=2)).astype(jnp.bfloat16)
    row_dots = lax.optimization_barrier(row_dots).astype(jnp.float32)

    def cross_head(head_index):
        queries = column_block(cross_q, head_index)
        key_rows = column_block(prefix_k, head_index)
        value_rows = column_block(prefix_v, head_index)
        grad_rows = column_block(cross_grad, head_index)
        scores = jnp.dot(queries, key_rows.T, preferred_element_type=jnp.float32) * score_scale
        scores = jnp.where(valid_keys[None, :], scores, -jnp.inf)
        log_total = jax.nn.logsumexp(scores, axis=1, keepdims=True)
        weights = jnp.exp(scores - log_total)
        grad_values = jnp.dot(weights.astype(jnp.bfloat16).T, grad_rows, preferred_element_type=jnp.float32)
        row_dot = lax.dynamic_slice_in_dim(row_dots, head_index, 1, 1)
        grad_scores = scores_grad(weights, grad_rows, value_rows, row_dot, score_scale)
        grad_queries = jnp.dot(grad_scores, key_rows, preferred_element_type=jnp.float32)
        grad_keys = jnp.dot(grad_scores.T, queries, preferred_element_type=jnp.float32)
        return (grad_queries.astype(jnp.bfloat16), grad_keys.astype(jnp.bfloat16), grad_values.astype(jnp.bfloat16))
    latent_ids = jnp.arange(LAT, dtype=jnp.int32)
    causal = latent_ids[:, None] >= latent_ids[None, :]

    def self_head(head_index):
        queries = column_block(self_q, head_index)
        key_rows = column_block(self_k, head_index)
        value_rows = column_block(self_v, head_index)
        grad_rows = column_block(self_grad, head_index)
        scores = jnp.dot(queries, key_rows.T, preferred_element_type=jnp.float32) * score_scale
        scores = jnp.where(causal, scores, -jnp.inf)
        log_total = jax.nn.logsumexp(scores, axis=1, keepdims=True)
        weights = jnp.exp(scores - log_total)
        weight_half = weights.astype(jnp.bfloat16)
        self_out = jnp.dot(weight_half, value_rows, preferred_element_type=jnp.float32)
        row_dot = lax.optimization_barrier(jnp.sum(grad_rows.astype(jnp.float32) * self_out, axis=1, keepdims=True))
        grad_scores = scores_grad(weights, grad_rows, value_rows, row_dot, score_scale)
        grad_queries = jnp.dot(grad_scores, key_rows, preferred_element_type=jnp.float32)
        grad_keys = jnp.dot(grad_scores.T, queries, preferred_element_type=jnp.float32)
        grad_values = jnp.dot(weight_half.T, grad_rows, preferred_element_type=jnp.float32)
        return (grad_queries.astype(jnp.bfloat16), grad_keys.astype(jnp.bfloat16), grad_values.astype(jnp.bfloat16))
    head_range = jnp.arange(HEADS, dtype=jnp.int32)
    cross_dq, prefix_dk, prefix_dv = lax.map(cross_head, head_range)
    self_dq, self_dk, self_dv = lax.map(self_head, head_range)
    return (join_heads(cross_dq), join_heads(prefix_dk), join_heads(prefix_dv), join_heads(self_dq), join_heads(self_dk), join_heads(self_dv))
```

```python
import jax
import jax.numpy as jnp
from jax import lax
from jax.sharding import PartitionSpec as P

HEAD_DIM = 128


def in_one_piece(arrays, axis, dim, along):
    ends, at = ([], 0)
    for a in arrays[:-1]:
        at += a.shape[along]
        ends.append(at)
    both = jnp.concatenate(arrays, axis=along)
    return tuple(jnp.split(lax.all_gather(both, axis, axis=dim, tiled=True), ends, axis=along))


def from_everyone(x, axis):
    copies = jnp.broadcast_to(x, (lax.axis_size(axis), *x.shape))
    return lax.all_to_all(copies, axis, split_axis=0, concat_axis=0, tiled=True)


def all_in_one(x, axis):
    leaves = jax.tree.leaves(x)
    order = sorted(range(len(leaves)), key=lambda k: -leaves[k].size)
    width = (1, *leaves[order[0]].shape)[-1]
    lines = [
        jnp.pad(leaves[k].reshape(-1), (0, -leaves[k].size % width)).reshape(-1, width)
        for k in order
    ]
    both, at, found = (from_everyone(jnp.concatenate(lines), axis), 0, {})
    for k, line in zip(order, lines):
        section = both[:, at : at + len(line)].reshape(len(both), -1)
        found[k] = section[:, : leaves[k].size].reshape(-1, *leaves[k].shape)
        at += len(line)
    numbers = iter(range(len(leaves)))
    return jax.tree.map(lambda _: found[next(numbers)], x)


def joined_by_halves(pieces, combine):
    while len(jax.tree.leaves(pieces)[0]) > 1:
        pieces = jax.vmap(combine)(
            *(jax.tree.map(lambda part: part[side::2], pieces) for side in (0, 1))
        )
    return jax.tree.map(lambda part: part[0], pieces)


def merged(x, axis, combine):
    pieces = all_in_one(x, axis)
    return joined_by_halves(pieces, combine)


def split_up(x, dim, size):
    before, after = (x.shape[:dim], x.shape[dim + 1 :])
    return jnp.moveaxis(x.reshape(*before, size, -1, *after), dim, 0)


def sum_at_owner(x, axis, dim):
    size = lax.axis_size(axis)
    parts = lax.all_to_all(split_up(x, dim, size), axis, 0, 0, tiled=True)
    return jnp.sum(parts, axis=0)


def joined_along(parts, dim):
    lengths = list(parts.shape[1:])
    lengths[dim] *= parts.shape[0]
    return jnp.moveaxis(parts, 0, dim).reshape(lengths)


def gathered_copies(x, axis, dim):
    return joined_along(from_everyone(x, axis), dim)


def merge_stats(left_stats, right_stats):
    row_max = jnp.maximum(left_stats[0], right_stats[0])
    row_sum = left_stats[1] * jnp.exp(left_stats[0] - row_max) + right_stats[1] * jnp.exp(
        right_stats[0] - row_max
    )
    return (row_max, row_sum)


def head_scores(queries, key_rows, score_scale):
    return (
        jnp.einsum("qhd,khd->hqk", queries, key_rows, preferred_element_type=jnp.float32)
        * score_scale
    )


def scores_grad(weights, grad_rows, value_rows, row_dot, score_scale):
    grad_probs = jnp.einsum(
        "qhd,khd->hqk", grad_rows, value_rows, preferred_element_type=jnp.float32
    )
    return (weights * (grad_probs - jnp.transpose(row_dot)[:, :, None]) * score_scale).astype(
        jnp.bfloat16
    )


def contract_rows(left_rows, right_rows):
    return jnp.einsum("hqk,qhd->khd", left_rows, right_rows, preferred_element_type=jnp.float32)


def contract_cols(left_rows, right_rows):
    return jnp.einsum("hqk,khd->qhd", left_rows, right_rows, preferred_element_type=jnp.float32)


SEQ_PARTS = ("c", "x", "zh", "y")


def gather_seq(x, dim):
    for axis in SEQ_PARTS:
        x = lax.all_gather(x, axis, axis=dim, tiled=True)
    return x


def merged_seq(row_max, row_sum):
    for axis in SEQ_PARTS:
        both = lax.all_gather(jnp.stack([row_max, row_sum]), axis)
        top = jnp.max(both[:, 0], axis=0)
        row_sum = jnp.sum(both[:, 1] * jnp.exp(both[:, 0] - top), axis=0)
        row_max = top
    return row_max, row_sum


def shards(
    cross_q,
    cross_out,
    cross_grad,
    prefix_k,
    prefix_v,
    pad_counts,
    self_q,
    self_k,
    self_v,
    self_grad,
):
    score_scale = HEAD_DIM ** (-0.5)
    own_rows, feature_width = cross_q.shape
    local_heads = feature_width // HEAD_DIM
    tokens = prefix_k.shape[0]
    grad_own = cross_grad.reshape(own_rows, local_heads, HEAD_DIM).astype(jnp.float32)
    out_own = cross_out.reshape(own_rows, local_heads, HEAD_DIM).astype(jnp.float32)
    row_dot = jnp.sum(grad_own * out_own, axis=2).astype(jnp.bfloat16)
    stacked = jnp.stack([self_q, self_k, self_v, self_grad])
    regrouped = lax.all_to_all(stacked, "zl", split_axis=2, concat_axis=1, tiled=True)
    block_rows = regrouped.shape[1]
    self_cols = jnp.transpose(regrouped, (1, 0, 2)).reshape(block_rows, -1)
    pieces = (cross_q, cross_grad, row_dot, self_cols)
    ends, at = [], 0
    for piece in pieces[:-1]:
        at += piece.shape[1]
        ends.append(at)
    gathered = gather_seq(jnp.concatenate(pieces, axis=1), 0)
    query_all, grad_all, dots_all, self_all = jnp.split(gathered, ends, axis=1)
    latents = query_all.shape[0]
    query_heads = query_all.reshape(latents, local_heads, HEAD_DIM)
    grad_heads = grad_all.reshape(latents, local_heads, HEAD_DIM)
    key_heads = prefix_k.reshape(tokens, local_heads, HEAD_DIM)
    value_heads = prefix_v.reshape(tokens, local_heads, HEAD_DIM)
    valid_keys = jnp.arange(tokens) < tokens - pad_counts[0]
    scores = head_scores(query_heads, key_heads, score_scale)
    scores = jnp.where(valid_keys[None, None, :], scores, -jnp.inf)
    row_max = jnp.max(scores, axis=2)
    row_sum = jnp.sum(jnp.exp(scores - row_max[:, :, None]), axis=2)
    row_maxes, row_sums = merged_seq(row_max, row_sum)
    log_total = row_maxes + jnp.log(row_sums)
    row_dots = dots_all.astype(jnp.float32)
    weights = jnp.exp(scores - log_total[:, :, None])
    prefix_dv = (
        contract_rows(weights.astype(jnp.bfloat16), grad_heads)
        .reshape(tokens, feature_width)
        .astype(jnp.bfloat16)
    )
    grad_scores = scores_grad(weights, grad_heads, value_heads, row_dots, score_scale)
    prefix_dk = (
        contract_rows(grad_scores, query_heads).reshape(tokens, feature_width).astype(jnp.bfloat16)
    )
    partial_value = contract_cols(grad_scores, key_heads).reshape(latents, feature_width)
    cross_dq = sum_at_owner(partial_value, SEQ_AXES, 0).astype(jnp.bfloat16)
    everything = jnp.transpose(self_all.reshape(latents, 4, feature_width), (1, 0, 2))
    row_start = lax.axis_index(SEQ_AXES) * block_rows
    all_rows = everything.shape[1]
    query_every = everything[0].reshape(all_rows, local_heads, HEAD_DIM)
    key_every = everything[1].reshape(all_rows, local_heads, HEAD_DIM)
    value_every = everything[2].reshape(all_rows, local_heads, HEAD_DIM)
    grad_every = everything[3].reshape(all_rows, local_heads, HEAD_DIM)
    row_ids = jnp.arange(all_rows)
    causal_full = row_ids[:, None] >= row_ids[None, :]
    full_scores = head_scores(query_every, key_every, score_scale)
    full_scores = jnp.where(causal_full[None, :, :], full_scores, -jnp.inf)
    full_lse = jax.nn.logsumexp(full_scores, axis=2)
    full_weights = jnp.exp(full_scores - full_lse[:, :, None])
    full_half = full_weights.astype(jnp.bfloat16)
    full_out = contract_cols(full_half, value_every)
    full_dot = jnp.sum(grad_every.astype(jnp.float32) * full_out, axis=2)
    full_gs = scores_grad(full_weights, grad_every, value_every, full_dot, score_scale)
    query_part = lax.dynamic_slice_in_dim(full_gs, row_start, block_rows, 1)
    self_dq = (
        contract_cols(query_part, key_every).reshape(block_rows, feature_width).astype(jnp.bfloat16)
    )
    key_part = lax.dynamic_slice_in_dim(full_gs, row_start, block_rows, 2)
    half_part = lax.dynamic_slice_in_dim(full_half, row_start, block_rows, 2)
    self_dk = (
        contract_rows(key_part, query_every).reshape(block_rows, feature_width).astype(jnp.bfloat16)
    )
    self_dv = (
        contract_rows(half_part, grad_every).reshape(block_rows, feature_width).astype(jnp.bfloat16)
    )
    return (cross_dq, prefix_dk, prefix_dv, self_dq, self_dk, self_dv)


SEQ_AXES = ("y", "zh", "x", "c")


def solution(mesh):
    sizes = dict(mesh.shape)
    split = mesh.devices.reshape(4, 2, 4, 2, sizes["head"])
    mesh = jax.sharding.Mesh(split, (*SEQ_AXES, "zl"))
    in_specs = (
        P(SEQ_AXES, "zl"),
        P(SEQ_AXES, "zl"),
        P(SEQ_AXES, "zl"),
        P(SEQ_AXES, "zl"),
        P(SEQ_AXES, "zl"),
        P(SEQ_AXES),
        P((*SEQ_AXES, "zl"), None),
        P((*SEQ_AXES, "zl"), None),
        P((*SEQ_AXES, "zl"), None),
        P((*SEQ_AXES, "zl"), None),
    )
    out_specs = (
        P(SEQ_AXES, "zl"),
        P(SEQ_AXES, "zl"),
        P(SEQ_AXES, "zl"),
        P(SEQ_AXES, "zl"),
        P(SEQ_AXES, "zl"),
        P(SEQ_AXES, "zl"),
    )
    return jax.shard_map(shards, mesh=mesh, in_specs=in_specs, out_specs=out_specs, check_vma=False)
```

```python
import jax
import jax.numpy as jnp
from jax import lax
from jax.sharding import PartitionSpec as P

HEAD_DIM = 128


def in_one_piece(arrays, axis, dim, along):
    ends, at = ([], 0)
    for a in arrays[:-1]:
        at += a.shape[along]
        ends.append(at)
    both = jnp.concatenate(arrays, axis=along)
    return tuple(jnp.split(lax.all_gather(both, axis, axis=dim, tiled=True), ends, axis=along))


def from_everyone(x, axis):
    copies = jnp.broadcast_to(x, (lax.axis_size(axis), *x.shape))
    return lax.all_to_all(copies, axis, split_axis=0, concat_axis=0, tiled=True)


def all_in_one(x, axis):
    leaves = jax.tree.leaves(x)
    order = sorted(range(len(leaves)), key=lambda k: -leaves[k].size)
    width = (1, *leaves[order[0]].shape)[-1]
    lines = [
        jnp.pad(leaves[k].reshape(-1), (0, -leaves[k].size % width)).reshape(-1, width)
        for k in order
    ]
    both, at, found = (from_everyone(jnp.concatenate(lines), axis), 0, {})
    for k, line in zip(order, lines):
        section = both[:, at : at + len(line)].reshape(len(both), -1)
        found[k] = section[:, : leaves[k].size].reshape(-1, *leaves[k].shape)
        at += len(line)
    numbers = iter(range(len(leaves)))
    return jax.tree.map(lambda _: found[next(numbers)], x)


def joined_by_halves(pieces, combine):
    while len(jax.tree.leaves(pieces)[0]) > 1:
        pieces = jax.vmap(combine)(
            *(jax.tree.map(lambda part: part[side::2], pieces) for side in (0, 1))
        )
    return jax.tree.map(lambda part: part[0], pieces)


def merged(x, axis, combine):
    pieces = all_in_one(x, axis)
    return joined_by_halves(pieces, combine)


def split_up(x, dim, size):
    before, after = (x.shape[:dim], x.shape[dim + 1 :])
    return jnp.moveaxis(x.reshape(*before, size, -1, *after), dim, 0)


def sum_at_owner(x, axis, dim):
    size = lax.axis_size(axis)
    parts = lax.all_to_all(split_up(x, dim, size), axis, 0, 0, tiled=True)
    return jnp.sum(parts, axis=0)


def joined_along(parts, dim):
    lengths = list(parts.shape[1:])
    lengths[dim] *= parts.shape[0]
    return jnp.moveaxis(parts, 0, dim).reshape(lengths)


def gathered_copies(x, axis, dim):
    return joined_along(from_everyone(x, axis), dim)


def merge_stats(left_stats, right_stats):
    row_max = jnp.maximum(left_stats[0], right_stats[0])
    row_sum = left_stats[1] * jnp.exp(left_stats[0] - row_max) + right_stats[1] * jnp.exp(
        right_stats[0] - row_max
    )
    return (row_max, row_sum)


def head_scores(queries, key_rows, score_scale):
    return (
        jnp.einsum("qhd,khd->hqk", queries, key_rows, preferred_element_type=jnp.float32)
        * score_scale
    )


def scores_grad(weights, grad_rows, value_rows, row_dot, score_scale):
    grad_probs = jnp.einsum(
        "qhd,khd->hqk", grad_rows, value_rows, preferred_element_type=jnp.float32
    )
    return (weights * (grad_probs - jnp.transpose(row_dot)[:, :, None]) * score_scale).astype(
        jnp.bfloat16
    )


def contract_rows(left_rows, right_rows):
    return jnp.einsum("hqk,qhd->khd", left_rows, right_rows, preferred_element_type=jnp.float32)


def contract_cols(left_rows, right_rows):
    return jnp.einsum("hqk,khd->qhd", left_rows, right_rows, preferred_element_type=jnp.float32)


SEQ_PARTS = ("c", "x", "zh", "y")


def gather_seq(x, dim):
    for axis in SEQ_PARTS:
        x = lax.all_gather(x, axis, axis=dim, tiled=True)
    return x


def merged_seq(row_max, row_sum):
    for axis in SEQ_PARTS:
        both = lax.all_gather(jnp.stack([row_max, row_sum]), axis)
        top = jnp.max(both[:, 0], axis=0)
        row_sum = jnp.sum(both[:, 1] * jnp.exp(both[:, 0] - top), axis=0)
        row_max = top
    return row_max, row_sum


def shards(
    cross_q,
    cross_out,
    cross_grad,
    prefix_k,
    prefix_v,
    pad_counts,
    self_q,
    self_k,
    self_v,
    self_grad,
):
    score_scale = HEAD_DIM ** (-0.5)
    own_rows, feature_width = cross_q.shape
    local_heads = feature_width // HEAD_DIM
    tokens = prefix_k.shape[0]
    grad_own = cross_grad.reshape(own_rows, local_heads, HEAD_DIM).astype(jnp.float32)
    out_own = cross_out.reshape(own_rows, local_heads, HEAD_DIM).astype(jnp.float32)
    row_dot = jnp.sum(grad_own * out_own, axis=2).astype(jnp.bfloat16)
    head_groups = lax.axis_size("zl")
    stacked = jnp.stack([self_q, self_k, self_v, self_grad]).reshape(4, head_groups, feature_width)
    regrouped = lax.all_to_all(
        jnp.transpose(stacked, (1, 0, 2)), "zl", split_axis=0, concat_axis=0, tiled=True
    )
    block_rows = regrouped.shape[0]
    self_cols = regrouped.reshape(block_rows, -1)
    pieces = (cross_q, cross_grad, row_dot, self_cols)
    ends, at = [], 0
    for piece in pieces[:-1]:
        at += piece.shape[1]
        ends.append(at)
    gathered = gather_seq(jnp.concatenate(pieces, axis=1), 0)
    query_all, grad_all, dots_all, self_all = jnp.split(gathered, ends, axis=1)
    latents = query_all.shape[0]
    query_heads = query_all.reshape(latents, local_heads, HEAD_DIM)
    grad_heads = grad_all.reshape(latents, local_heads, HEAD_DIM)
    key_heads = prefix_k.reshape(tokens, local_heads, HEAD_DIM)
    value_heads = prefix_v.reshape(tokens, local_heads, HEAD_DIM)
    valid_keys = jnp.arange(tokens) < tokens - pad_counts[0]
    scores = head_scores(query_heads, key_heads, score_scale)
    scores = jnp.where(valid_keys[None, None, :], scores, -jnp.inf)
    row_max = jnp.max(scores, axis=2)
    row_sum = jnp.sum(jnp.exp(scores - row_max[:, :, None]), axis=2)
    row_maxes, row_sums = merged_seq(row_max, row_sum)
    log_total = row_maxes + jnp.log(row_sums)
    row_dots = dots_all.astype(jnp.float32)
    weights = jnp.exp(scores - log_total[:, :, None])
    prefix_dv = (
        contract_rows(weights.astype(jnp.bfloat16), grad_heads)
        .reshape(tokens, feature_width)
        .astype(jnp.bfloat16)
    )
    grad_scores = scores_grad(weights, grad_heads, value_heads, row_dots, score_scale)
    prefix_dk = (
        contract_rows(grad_scores, query_heads).reshape(tokens, feature_width).astype(jnp.bfloat16)
    )
    partial_value = contract_cols(grad_scores, key_heads).reshape(latents, feature_width)
    cross_dq = sum_at_owner(partial_value, SEQ_AXES, 0).astype(jnp.bfloat16)
    everything = jnp.transpose(self_all.reshape(latents, 4, feature_width), (1, 0, 2))
    row_start = lax.axis_index(SEQ_AXES) * block_rows
    all_rows = everything.shape[1]
    query_every = everything[0].reshape(all_rows, local_heads, HEAD_DIM)
    key_every = everything[1].reshape(all_rows, local_heads, HEAD_DIM)
    value_every = everything[2].reshape(all_rows, local_heads, HEAD_DIM)
    grad_every = everything[3].reshape(all_rows, local_heads, HEAD_DIM)
    row_ids = jnp.arange(all_rows)
    causal_full = row_ids[:, None] >= row_ids[None, :]
    full_scores = head_scores(query_every, key_every, score_scale)
    full_scores = jnp.where(causal_full[None, :, :], full_scores, -jnp.inf)
    full_lse = jax.nn.logsumexp(full_scores, axis=2)
    full_weights = jnp.exp(full_scores - full_lse[:, :, None])
    full_half = full_weights.astype(jnp.bfloat16)
    full_out = contract_cols(full_half, value_every)
    full_dot = jnp.sum(grad_every.astype(jnp.float32) * full_out, axis=2)
    full_gs = scores_grad(full_weights, grad_every, value_every, full_dot, score_scale)
    query_part = lax.dynamic_slice_in_dim(full_gs, row_start, block_rows, 1)
    self_dq = (
        contract_cols(query_part, key_every).reshape(block_rows, feature_width).astype(jnp.bfloat16)
    )
    key_part = lax.dynamic_slice_in_dim(full_gs, row_start, block_rows, 2)
    half_part = lax.dynamic_slice_in_dim(full_half, row_start, block_rows, 2)
    self_dk = (
        contract_rows(key_part, query_every).reshape(block_rows, feature_width).astype(jnp.bfloat16)
    )
    self_dv = (
        contract_rows(half_part, grad_every).reshape(block_rows, feature_width).astype(jnp.bfloat16)
    )
    return (cross_dq, prefix_dk, prefix_dv, self_dq, self_dk, self_dv)


SEQ_AXES = ("y", "zh", "x", "c")


def solution(mesh):
    sizes = dict(mesh.shape)
    split = mesh.devices.reshape(4, 2, 4, 2, sizes["head"])
    mesh = jax.sharding.Mesh(split, (*SEQ_AXES, "zl"))
    in_specs = (
        P(SEQ_AXES, "zl"),
        P(SEQ_AXES, "zl"),
        P(SEQ_AXES, "zl"),
        P(SEQ_AXES, "zl"),
        P(SEQ_AXES, "zl"),
        P(SEQ_AXES),
        P((*SEQ_AXES, "zl"), None),
        P((*SEQ_AXES, "zl"), None),
        P((*SEQ_AXES, "zl"), None),
        P((*SEQ_AXES, "zl"), None),
    )
    out_specs = (
        P(SEQ_AXES, "zl"),
        P(SEQ_AXES, "zl"),
        P(SEQ_AXES, "zl"),
        P(SEQ_AXES, "zl"),
        P(SEQ_AXES, "zl"),
        P(SEQ_AXES, "zl"),
    )
    return jax.shard_map(shards, mesh=mesh, in_specs=in_specs, out_specs=out_specs, check_vma=False)
```

```python
import jax
import jax.numpy as jnp
from jax import lax
from jax.sharding import PartitionSpec as P

HEAD_DIM = 128


def in_one_piece(arrays, axis, dim, along):
    ends, at = ([], 0)
    for a in arrays[:-1]:
        at += a.shape[along]
        ends.append(at)
    both = jnp.concatenate(arrays, axis=along)
    return tuple(jnp.split(lax.all_gather(both, axis, axis=dim, tiled=True), ends, axis=along))


def from_everyone(x, axis):
    copies = jnp.broadcast_to(x, (lax.axis_size(axis), *x.shape))
    return lax.all_to_all(copies, axis, split_axis=0, concat_axis=0, tiled=True)


def all_in_one(x, axis):
    leaves = jax.tree.leaves(x)
    order = sorted(range(len(leaves)), key=lambda k: -leaves[k].size)
    width = (1, *leaves[order[0]].shape)[-1]
    lines = [
        jnp.pad(leaves[k].reshape(-1), (0, -leaves[k].size % width)).reshape(-1, width)
        for k in order
    ]
    both, at, found = (from_everyone(jnp.concatenate(lines), axis), 0, {})
    for k, line in zip(order, lines):
        section = both[:, at : at + len(line)].reshape(len(both), -1)
        found[k] = section[:, : leaves[k].size].reshape(-1, *leaves[k].shape)
        at += len(line)
    numbers = iter(range(len(leaves)))
    return jax.tree.map(lambda _: found[next(numbers)], x)


def joined_by_halves(pieces, combine):
    while len(jax.tree.leaves(pieces)[0]) > 1:
        pieces = jax.vmap(combine)(
            *(jax.tree.map(lambda part: part[side::2], pieces) for side in (0, 1))
        )
    return jax.tree.map(lambda part: part[0], pieces)


def merged(x, axis, combine):
    pieces = all_in_one(x, axis)
    return joined_by_halves(pieces, combine)


def split_up(x, dim, size):
    before, after = (x.shape[:dim], x.shape[dim + 1 :])
    return jnp.moveaxis(x.reshape(*before, size, -1, *after), dim, 0)


def sum_at_owner(x, axis, dim):
    size = lax.axis_size(axis)
    parts = lax.all_to_all(split_up(x, dim, size), axis, 0, 0, tiled=True)
    return jnp.sum(parts, axis=0)


def joined_along(parts, dim):
    lengths = list(parts.shape[1:])
    lengths[dim] *= parts.shape[0]
    return jnp.moveaxis(parts, 0, dim).reshape(lengths)


def gathered_copies(x, axis, dim):
    return joined_along(from_everyone(x, axis), dim)


def merge_stats(left_stats, right_stats):
    row_max = jnp.maximum(left_stats[0], right_stats[0])
    row_sum = left_stats[1] * jnp.exp(left_stats[0] - row_max) + right_stats[1] * jnp.exp(
        right_stats[0] - row_max
    )
    return (row_max, row_sum)


def head_scores(queries, key_rows, score_scale):
    return (
        jnp.einsum("qhd,khd->hqk", queries, key_rows, preferred_element_type=jnp.float32)
        * score_scale
    )


def scores_grad(weights, grad_rows, value_rows, row_dot, score_scale):
    grad_probs = jnp.einsum(
        "qhd,khd->hqk", grad_rows, value_rows, preferred_element_type=jnp.float32
    )
    return (weights * (grad_probs - jnp.transpose(row_dot)[:, :, None]) * score_scale).astype(
        jnp.bfloat16
    )


def contract_rows(left_rows, right_rows):
    return jnp.einsum("hqk,qhd->khd", left_rows, right_rows, preferred_element_type=jnp.float32)


def contract_cols(left_rows, right_rows):
    return jnp.einsum("hqk,khd->qhd", left_rows, right_rows, preferred_element_type=jnp.float32)


SEQ_PARTS = ("c", "x", "zh", "y")


GATHER_ORDER = ("zh", "c", "x", "y")


def gather_seq(x):
    for axis in GATHER_ORDER:
        x = lax.all_gather(x, axis, axis=0, tiled=False)
    order = [GATHER_ORDER[::-1].index(axis) for axis in SEQ_AXES]
    x = jnp.transpose(x, (*order, *range(4, x.ndim)))
    return x.reshape(-1, *x.shape[5:])


def merged_seq(row_max, row_sum):
    for axis in SEQ_PARTS:
        both = lax.all_gather(jnp.stack([row_max, row_sum]), axis)
        top = jnp.max(both[:, 0], axis=0)
        row_sum = jnp.sum(both[:, 1] * jnp.exp(both[:, 0] - top), axis=0)
        row_max = top
    return row_max, row_sum


def shards(
    cross_q,
    cross_out,
    cross_grad,
    prefix_k,
    prefix_v,
    pad_counts,
    self_q,
    self_k,
    self_v,
    self_grad,
):
    score_scale = HEAD_DIM ** (-0.5)
    own_rows, feature_width = cross_q.shape
    local_heads = feature_width // HEAD_DIM
    tokens = prefix_k.shape[0]
    grad_own = cross_grad.reshape(own_rows, local_heads, HEAD_DIM).astype(jnp.float32)
    out_own = cross_out.reshape(own_rows, local_heads, HEAD_DIM).astype(jnp.float32)
    row_dot = jnp.sum(grad_own * out_own, axis=2).astype(jnp.bfloat16)
    head_groups = lax.axis_size("zl")
    stacked = jnp.stack([self_q, self_k, self_v, self_grad]).reshape(4, head_groups, feature_width)
    regrouped = lax.all_to_all(
        jnp.transpose(stacked, (1, 0, 2)), "zl", split_axis=0, concat_axis=0, tiled=True
    )
    block_rows = regrouped.shape[0]
    self_cols = regrouped.reshape(block_rows, -1)
    pieces = (cross_q, cross_grad, row_dot, self_cols)
    ends, at = [], 0
    for piece in pieces[:-1]:
        at += piece.shape[1]
        ends.append(at)
    gathered = gather_seq(jnp.concatenate(pieces, axis=1))
    query_all, grad_all, dots_all, self_all = jnp.split(gathered, ends, axis=1)
    latents = query_all.shape[0]
    query_heads = query_all.reshape(latents, local_heads, HEAD_DIM)
    grad_heads = grad_all.reshape(latents, local_heads, HEAD_DIM)
    key_heads = prefix_k.reshape(tokens, local_heads, HEAD_DIM)
    value_heads = prefix_v.reshape(tokens, local_heads, HEAD_DIM)
    valid_keys = jnp.arange(tokens) < tokens - pad_counts[0]
    scores = head_scores(query_heads, key_heads, score_scale)
    scores = jnp.where(valid_keys[None, None, :], scores, -jnp.inf)
    row_max = jnp.max(scores, axis=2)
    row_sum = jnp.sum(jnp.exp(scores - row_max[:, :, None]), axis=2)
    row_maxes, row_sums = merged_seq(row_max, row_sum)
    log_total = row_maxes + jnp.log(row_sums)
    row_dots = dots_all.astype(jnp.float32)
    weights = jnp.exp(scores - log_total[:, :, None])
    prefix_dv = (
        contract_rows(weights.astype(jnp.bfloat16), grad_heads)
        .reshape(tokens, feature_width)
        .astype(jnp.bfloat16)
    )
    grad_scores = scores_grad(weights, grad_heads, value_heads, row_dots, score_scale)
    prefix_dk = (
        contract_rows(grad_scores, query_heads).reshape(tokens, feature_width).astype(jnp.bfloat16)
    )
    partial_value = contract_cols(grad_scores, key_heads).reshape(latents, feature_width)
    cross_dq = sum_at_owner(partial_value, SEQ_AXES, 0).astype(jnp.bfloat16)
    everything = jnp.transpose(self_all.reshape(latents, 4, feature_width), (1, 0, 2))
    row_start = lax.axis_index(SEQ_AXES) * block_rows
    all_rows = everything.shape[1]
    query_every = everything[0].reshape(all_rows, local_heads, HEAD_DIM)
    key_every = everything[1].reshape(all_rows, local_heads, HEAD_DIM)
    value_every = everything[2].reshape(all_rows, local_heads, HEAD_DIM)
    grad_every = everything[3].reshape(all_rows, local_heads, HEAD_DIM)
    row_ids = jnp.arange(all_rows)
    causal_full = row_ids[:, None] >= row_ids[None, :]
    full_scores = head_scores(query_every, key_every, score_scale)
    full_scores = jnp.where(causal_full[None, :, :], full_scores, -jnp.inf)
    full_lse = jax.nn.logsumexp(full_scores, axis=2)
    full_weights = jnp.exp(full_scores - full_lse[:, :, None])
    full_half = full_weights.astype(jnp.bfloat16)
    full_out = contract_cols(full_half, value_every)
    full_dot = jnp.sum(grad_every.astype(jnp.float32) * full_out, axis=2)
    full_gs = scores_grad(full_weights, grad_every, value_every, full_dot, score_scale)
    query_part = lax.dynamic_slice_in_dim(full_gs, row_start, block_rows, 1)
    self_dq = (
        contract_cols(query_part, key_every).reshape(block_rows, feature_width).astype(jnp.bfloat16)
    )
    key_part = lax.dynamic_slice_in_dim(full_gs, row_start, block_rows, 2)
    half_part = lax.dynamic_slice_in_dim(full_half, row_start, block_rows, 2)
    self_dk = (
        contract_rows(key_part, query_every).reshape(block_rows, feature_width).astype(jnp.bfloat16)
    )
    self_dv = (
        contract_rows(half_part, grad_every).reshape(block_rows, feature_width).astype(jnp.bfloat16)
    )
    return (cross_dq, prefix_dk, prefix_dv, self_dq, self_dk, self_dv)


SEQ_AXES = ("y", "zh", "x", "c")


def solution(mesh):
    sizes = dict(mesh.shape)
    split = mesh.devices.reshape(4, 2, 4, 2, sizes["head"])
    mesh = jax.sharding.Mesh(split, (*SEQ_AXES, "zl"))
    in_specs = (
        P(SEQ_AXES, "zl"),
        P(SEQ_AXES, "zl"),
        P(SEQ_AXES, "zl"),
        P(SEQ_AXES, "zl"),
        P(SEQ_AXES, "zl"),
        P(SEQ_AXES),
        P((*SEQ_AXES, "zl"), None),
        P((*SEQ_AXES, "zl"), None),
        P((*SEQ_AXES, "zl"), None),
        P((*SEQ_AXES, "zl"), None),
    )
    out_specs = (
        P(SEQ_AXES, "zl"),
        P(SEQ_AXES, "zl"),
        P(SEQ_AXES, "zl"),
        P(SEQ_AXES, "zl"),
        P(SEQ_AXES, "zl"),
        P(SEQ_AXES, "zl"),
    )
    return jax.shard_map(shards, mesh=mesh, in_specs=in_specs, out_specs=out_specs, check_vma=False)
```

```python
import jax
import jax.numpy as jnp
from jax import lax
from jax.sharding import PartitionSpec as P

HEAD_DIM = 128


def in_one_piece(arrays, axis, dim, along):
    ends, at = ([], 0)
    for a in arrays[:-1]:
        at += a.shape[along]
        ends.append(at)
    both = jnp.concatenate(arrays, axis=along)
    return tuple(jnp.split(lax.all_gather(both, axis, axis=dim, tiled=True), ends, axis=along))


def from_everyone(x, axis):
    copies = jnp.broadcast_to(x, (lax.axis_size(axis), *x.shape))
    return lax.all_to_all(copies, axis, split_axis=0, concat_axis=0, tiled=True)


def all_in_one(x, axis):
    leaves = jax.tree.leaves(x)
    order = sorted(range(len(leaves)), key=lambda k: -leaves[k].size)
    width = (1, *leaves[order[0]].shape)[-1]
    lines = [
        jnp.pad(leaves[k].reshape(-1), (0, -leaves[k].size % width)).reshape(-1, width)
        for k in order
    ]
    both, at, found = (from_everyone(jnp.concatenate(lines), axis), 0, {})
    for k, line in zip(order, lines):
        section = both[:, at : at + len(line)].reshape(len(both), -1)
        found[k] = section[:, : leaves[k].size].reshape(-1, *leaves[k].shape)
        at += len(line)
    numbers = iter(range(len(leaves)))
    return jax.tree.map(lambda _: found[next(numbers)], x)


def joined_by_halves(pieces, combine):
    while len(jax.tree.leaves(pieces)[0]) > 1:
        pieces = jax.vmap(combine)(
            *(jax.tree.map(lambda part: part[side::2], pieces) for side in (0, 1))
        )
    return jax.tree.map(lambda part: part[0], pieces)


def merged(x, axis, combine):
    pieces = all_in_one(x, axis)
    return joined_by_halves(pieces, combine)


def split_up(x, dim, size):
    before, after = (x.shape[:dim], x.shape[dim + 1 :])
    return jnp.moveaxis(x.reshape(*before, size, -1, *after), dim, 0)


def sum_at_owner(x, axis, dim):
    size = lax.axis_size(axis)
    parts = lax.all_to_all(split_up(x, dim, size), axis, 0, 0, tiled=True)
    return jnp.sum(parts, axis=0)


def joined_along(parts, dim):
    lengths = list(parts.shape[1:])
    lengths[dim] *= parts.shape[0]
    return jnp.moveaxis(parts, 0, dim).reshape(lengths)


def gathered_copies(x, axis, dim):
    return joined_along(from_everyone(x, axis), dim)


def merge_stats(left_stats, right_stats):
    row_max = jnp.maximum(left_stats[0], right_stats[0])
    row_sum = left_stats[1] * jnp.exp(left_stats[0] - row_max) + right_stats[1] * jnp.exp(
        right_stats[0] - row_max
    )
    return (row_max, row_sum)


def head_scores(queries, key_rows, score_scale):
    return (
        jnp.einsum("qhd,khd->hqk", queries, key_rows, preferred_element_type=jnp.float32)
        * score_scale
    )


def scores_grad(weights, grad_rows, value_rows, row_dot, score_scale):
    grad_probs = jnp.einsum(
        "qhd,khd->hqk", grad_rows, value_rows, preferred_element_type=jnp.float32
    )
    return (weights * (grad_probs - jnp.transpose(row_dot)[:, :, None]) * score_scale).astype(
        jnp.bfloat16
    )


def contract_rows(left_rows, right_rows):
    return jnp.einsum("hqk,qhd->khd", left_rows, right_rows, preferred_element_type=jnp.float32)


def contract_cols(left_rows, right_rows):
    return jnp.einsum("hqk,khd->qhd", left_rows, right_rows, preferred_element_type=jnp.float32)


SEQ_PARTS = ("c", "x", "zh", "y")


GATHER_ORDER = ("zh", "c", "x", "y")


def gather_seq(x, axes):
    for axis in axes:
        x = lax.all_gather(x, axis, axis=0, tiled=False)
    order = [GATHER_ORDER[::-1].index(axis) for axis in SEQ_AXES]
    x = jnp.transpose(x, (*order, *range(4, x.ndim)))
    return x.reshape(-1, *x.shape[5:])


def merged_seq(row_max, row_sum):
    for axis in SEQ_PARTS:
        both = lax.all_gather(jnp.stack([row_max, row_sum]), axis)
        top = jnp.max(both[:, 0], axis=0)
        row_sum = jnp.sum(both[:, 1] * jnp.exp(both[:, 0] - top), axis=0)
        row_max = top
    return row_max, row_sum


def shards(
    cross_q,
    cross_out,
    cross_grad,
    prefix_k,
    prefix_v,
    pad_counts,
    self_q,
    self_k,
    self_v,
    self_grad,
):
    score_scale = HEAD_DIM ** (-0.5)
    own_rows, feature_width = cross_q.shape
    local_heads = feature_width // HEAD_DIM
    tokens = prefix_k.shape[0]
    grad_own = cross_grad.reshape(own_rows, local_heads, HEAD_DIM).astype(jnp.float32)
    out_own = cross_out.reshape(own_rows, local_heads, HEAD_DIM).astype(jnp.float32)
    row_dot = jnp.sum(grad_own * out_own, axis=2).astype(jnp.bfloat16)
    head_groups = lax.axis_size("zl")
    stacked = jnp.stack([self_q, self_k, self_v, self_grad]).reshape(4, head_groups, feature_width)
    regrouped = lax.all_to_all(
        jnp.transpose(stacked, (1, 0, 2)), "zl", split_axis=0, concat_axis=0, tiled=True
    )
    block_rows = regrouped.shape[0]
    self_cols = regrouped.reshape(block_rows, -1)
    cross_cols = jnp.concatenate((cross_q, cross_grad, row_dot), axis=1)
    cross_width = cross_cols.shape[1]
    first = jnp.concatenate((cross_cols, self_cols), axis=1)
    for axis in GATHER_ORDER[:2]:
        first = lax.all_gather(first, axis, axis=0)
    core = lax.axis_index("c")
    self_heads = first[..., cross_width:].reshape(*first.shape[:-1], 4, local_heads, HEAD_DIM)
    self_mine = lax.dynamic_index_in_dim(self_heads, core, axis=4, keepdims=False)
    rest = jnp.concatenate(
        (first[..., :cross_width], self_mine.reshape(*first.shape[:-1], -1)), axis=-1
    )
    gathered = gather_seq(rest, GATHER_ORDER[2:])
    query_all = gathered[:, : cross_q.shape[1]]
    grad_all = gathered[:, cross_q.shape[1] : 2 * cross_q.shape[1]]
    dots_all = gathered[:, 2 * cross_q.shape[1] : cross_width]
    self_all = gathered[:, cross_width:]
    latents = query_all.shape[0]
    query_heads = query_all.reshape(latents, local_heads, HEAD_DIM)
    grad_heads = grad_all.reshape(latents, local_heads, HEAD_DIM)
    key_heads = prefix_k.reshape(tokens, local_heads, HEAD_DIM)
    value_heads = prefix_v.reshape(tokens, local_heads, HEAD_DIM)
    valid_keys = jnp.arange(tokens) < tokens - pad_counts[0]
    scores = head_scores(query_heads, key_heads, score_scale)
    scores = jnp.where(valid_keys[None, None, :], scores, -jnp.inf)
    row_max = jnp.max(scores, axis=2)
    row_sum = jnp.sum(jnp.exp(scores - row_max[:, :, None]), axis=2)
    row_maxes, row_sums = merged_seq(row_max, row_sum)
    log_total = row_maxes + jnp.log(row_sums)
    row_dots = dots_all.astype(jnp.float32)
    weights = jnp.exp(scores - log_total[:, :, None])
    prefix_dv = (
        contract_rows(weights.astype(jnp.bfloat16), grad_heads)
        .reshape(tokens, feature_width)
        .astype(jnp.bfloat16)
    )
    grad_scores = scores_grad(weights, grad_heads, value_heads, row_dots, score_scale)
    prefix_dk = (
        contract_rows(grad_scores, query_heads).reshape(tokens, feature_width).astype(jnp.bfloat16)
    )
    partial_value = contract_cols(grad_scores, key_heads).reshape(latents, feature_width)
    cross_dq = sum_at_owner(partial_value, SEQ_AXES, 0).astype(jnp.bfloat16)
    everything = jnp.transpose(self_all.reshape(latents, 4, HEAD_DIM), (1, 0, 2))
    all_rows = everything.shape[1]
    query_every = everything[0].reshape(all_rows, 1, HEAD_DIM)
    key_every = everything[1].reshape(all_rows, 1, HEAD_DIM)
    value_every = everything[2].reshape(all_rows, 1, HEAD_DIM)
    grad_every = everything[3].reshape(all_rows, 1, HEAD_DIM)
    row_ids = jnp.arange(all_rows)
    causal_full = row_ids[:, None] >= row_ids[None, :]
    full_scores = head_scores(query_every, key_every, score_scale)
    full_scores = jnp.where(causal_full[None, :, :], full_scores, -jnp.inf)
    full_lse = jax.nn.logsumexp(full_scores, axis=2)
    full_weights = jnp.exp(full_scores - full_lse[:, :, None])
    full_half = full_weights.astype(jnp.bfloat16)
    full_out = contract_cols(full_half, value_every)
    full_dot = jnp.sum(grad_every.astype(jnp.float32) * full_out, axis=2)
    full_gs = scores_grad(full_weights, grad_every, value_every, full_dot, score_scale)
    cores = lax.axis_size("c")
    chip_rows = block_rows * cores
    chip_start = (lax.axis_index(SEQ_AXES) - core) * block_rows
    query_part = lax.dynamic_slice_in_dim(full_gs, chip_start, chip_rows, 1)
    key_part = lax.dynamic_slice_in_dim(full_gs, chip_start, chip_rows, 2)
    half_part = lax.dynamic_slice_in_dim(full_half, chip_start, chip_rows, 2)
    head_results = jnp.stack(
        [
            contract_cols(query_part, key_every),
            contract_rows(key_part, query_every),
            contract_rows(half_part, grad_every),
        ]
    ).astype(jnp.bfloat16)
    both = lax.all_gather(head_results.reshape(3, chip_rows, HEAD_DIM), "c", axis=0)
    mine = lax.dynamic_slice_in_dim(both, core * block_rows, block_rows, 2)
    mine = jnp.transpose(mine, (1, 2, 0, 3)).reshape(3, block_rows, feature_width)
    self_dq, self_dk, self_dv = mine[0], mine[1], mine[2]
    return (cross_dq, prefix_dk, prefix_dv, self_dq, self_dk, self_dv)


SEQ_AXES = ("y", "zh", "x", "c")


def solution(mesh):
    sizes = dict(mesh.shape)
    split = mesh.devices.reshape(4, 2, 4, 2, sizes["head"])
    mesh = jax.sharding.Mesh(split, (*SEQ_AXES, "zl"))
    in_specs = (
        P(SEQ_AXES, "zl"),
        P(SEQ_AXES, "zl"),
        P(SEQ_AXES, "zl"),
        P(SEQ_AXES, "zl"),
        P(SEQ_AXES, "zl"),
        P(SEQ_AXES),
        P((*SEQ_AXES, "zl"), None),
        P((*SEQ_AXES, "zl"), None),
        P((*SEQ_AXES, "zl"), None),
        P((*SEQ_AXES, "zl"), None),
    )
    out_specs = (
        P(SEQ_AXES, "zl"),
        P(SEQ_AXES, "zl"),
        P(SEQ_AXES, "zl"),
        P(SEQ_AXES, "zl"),
        P(SEQ_AXES, "zl"),
        P(SEQ_AXES, "zl"),
    )
    return jax.shard_map(shards, mesh=mesh, in_specs=in_specs, out_specs=out_specs, check_vma=False)
```

```python
import jax
import jax.numpy as jnp
from jax import lax
from jax.sharding import PartitionSpec as P

HEAD_DIM = 128


def in_one_piece(arrays, axis, dim, along):
    ends, at = ([], 0)
    for a in arrays[:-1]:
        at += a.shape[along]
        ends.append(at)
    both = jnp.concatenate(arrays, axis=along)
    return tuple(jnp.split(lax.all_gather(both, axis, axis=dim, tiled=True), ends, axis=along))


def from_everyone(x, axis):
    copies = jnp.broadcast_to(x, (lax.axis_size(axis), *x.shape))
    return lax.all_to_all(copies, axis, split_axis=0, concat_axis=0, tiled=True)


def all_in_one(x, axis):
    leaves = jax.tree.leaves(x)
    order = sorted(range(len(leaves)), key=lambda k: -leaves[k].size)
    width = (1, *leaves[order[0]].shape)[-1]
    lines = [
        jnp.pad(leaves[k].reshape(-1), (0, -leaves[k].size % width)).reshape(-1, width)
        for k in order
    ]
    both, at, found = (from_everyone(jnp.concatenate(lines), axis), 0, {})
    for k, line in zip(order, lines):
        section = both[:, at : at + len(line)].reshape(len(both), -1)
        found[k] = section[:, : leaves[k].size].reshape(-1, *leaves[k].shape)
        at += len(line)
    numbers = iter(range(len(leaves)))
    return jax.tree.map(lambda _: found[next(numbers)], x)


def joined_by_halves(pieces, combine):
    while len(jax.tree.leaves(pieces)[0]) > 1:
        pieces = jax.vmap(combine)(
            *(jax.tree.map(lambda part: part[side::2], pieces) for side in (0, 1))
        )
    return jax.tree.map(lambda part: part[0], pieces)


def merged(x, axis, combine):
    pieces = all_in_one(x, axis)
    return joined_by_halves(pieces, combine)


def split_up(x, dim, size):
    before, after = (x.shape[:dim], x.shape[dim + 1 :])
    return jnp.moveaxis(x.reshape(*before, size, -1, *after), dim, 0)


def sum_at_owner(x, axis, dim):
    size = lax.axis_size(axis)
    parts = lax.all_to_all(split_up(x, dim, size), axis, 0, 0, tiled=True)
    return jnp.sum(parts, axis=0)


def joined_along(parts, dim):
    lengths = list(parts.shape[1:])
    lengths[dim] *= parts.shape[0]
    return jnp.moveaxis(parts, 0, dim).reshape(lengths)


def gathered_copies(x, axis, dim):
    return joined_along(from_everyone(x, axis), dim)


def merge_stats(left_stats, right_stats):
    row_max = jnp.maximum(left_stats[0], right_stats[0])
    row_sum = left_stats[1] * jnp.exp(left_stats[0] - row_max) + right_stats[1] * jnp.exp(
        right_stats[0] - row_max
    )
    return (row_max, row_sum)


def head_scores(queries, key_rows, score_scale):
    return (
        jnp.einsum("qhd,khd->hqk", queries, key_rows, preferred_element_type=jnp.float32)
        * score_scale
    )


def scores_grad(weights, grad_rows, value_rows, row_dot, score_scale):
    grad_probs = jnp.einsum(
        "qhd,khd->hqk", grad_rows, value_rows, preferred_element_type=jnp.float32
    )
    return (weights * (grad_probs - jnp.transpose(row_dot)[:, :, None]) * score_scale).astype(
        jnp.bfloat16
    )


def contract_rows(left_rows, right_rows):
    return jnp.einsum("hqk,qhd->khd", left_rows, right_rows, preferred_element_type=jnp.float32)


def contract_cols(left_rows, right_rows):
    return jnp.einsum("hqk,khd->qhd", left_rows, right_rows, preferred_element_type=jnp.float32)


SEQ_PARTS = ("c", "x", "zh", "y")


GATHER_ORDER = ("zh", "c", "x", "y")


def gather_seq(x, axes):
    for axis in axes:
        x = lax.all_gather(x, axis, axis=0, tiled=False)
    order = [GATHER_ORDER[::-1].index(axis) for axis in SEQ_AXES]
    x = jnp.transpose(x, (*order, *range(4, x.ndim)))
    return x.reshape(-1, *x.shape[5:])


def merged_with_dq(row_max, row_sum, partial_dq):
    rows = partial_dq.shape[0]
    width = partial_dq[0].size
    start = 0
    for axis in SEQ_AXES:
        size = lax.axis_size(axis)
        rows //= size
        stats = jnp.stack([row_max, row_sum]).reshape(1, -1)
        send = jnp.concatenate(
            [partial_dq.reshape(size, -1), jnp.broadcast_to(stats, (size, stats.shape[1]))], axis=1
        )
        got = lax.all_to_all(send, axis, 0, 0, tiled=True)
        got_dq = got[:, : rows * width].reshape(size, rows, *partial_dq.shape[1:])
        got_stats = got[:, rows * width :].reshape(size, 2, *row_max.shape)
        top = jnp.max(got_stats[:, 0], axis=0)
        rescale = jnp.exp(got_stats[:, 0] - top)
        row_sum = jnp.sum(got_stats[:, 1] * rescale, axis=0)
        row_max = top
        start = start + lax.axis_index(axis) * rows
        dq_rescale = jnp.transpose(lax.dynamic_slice_in_dim(rescale, start, rows, 2), (0, 2, 1))
        partial_dq = jnp.sum(dq_rescale[..., None] * got_dq, axis=0)
    own_sum = jnp.transpose(lax.dynamic_slice_in_dim(row_sum, start, rows, 1))
    return row_max, row_sum, partial_dq / own_sum[..., None]


def shards(
    cross_q,
    cross_out,
    cross_grad,
    prefix_k,
    prefix_v,
    pad_counts,
    self_q,
    self_k,
    self_v,
    self_grad,
):
    score_scale = HEAD_DIM ** (-0.5)
    own_rows, feature_width = cross_q.shape
    local_heads = feature_width // HEAD_DIM
    tokens = prefix_k.shape[0]
    grad_own = cross_grad.reshape(own_rows, local_heads, HEAD_DIM).astype(jnp.float32)
    out_own = cross_out.reshape(own_rows, local_heads, HEAD_DIM).astype(jnp.float32)
    row_dot = jnp.sum(grad_own * out_own, axis=2).astype(jnp.bfloat16)
    head_groups = lax.axis_size("zl")
    stacked = jnp.stack([self_q, self_k, self_v, self_grad]).reshape(4, head_groups, feature_width)
    regrouped = lax.all_to_all(
        jnp.transpose(stacked, (1, 0, 2)), "zl", split_axis=0, concat_axis=0, tiled=True
    )
    block_rows = regrouped.shape[0]
    self_cols = regrouped.reshape(block_rows, -1)
    cross_cols = jnp.concatenate((cross_q, cross_grad, row_dot), axis=1)
    cross_width = cross_cols.shape[1]
    first = jnp.concatenate((cross_cols, self_cols), axis=1)
    for axis in GATHER_ORDER[:2]:
        first = lax.all_gather(first, axis, axis=0)
    core = lax.axis_index("c")
    self_heads = first[..., cross_width:].reshape(*first.shape[:-1], 4, local_heads, HEAD_DIM)
    self_mine = lax.dynamic_index_in_dim(self_heads, core, axis=4, keepdims=False)
    rest = jnp.concatenate(
        (first[..., :cross_width], self_mine.reshape(*first.shape[:-1], -1)), axis=-1
    )
    gathered = gather_seq(rest, GATHER_ORDER[2:])
    query_all = gathered[:, : cross_q.shape[1]]
    grad_all = gathered[:, cross_q.shape[1] : 2 * cross_q.shape[1]]
    dots_all = gathered[:, 2 * cross_q.shape[1] : cross_width]
    self_all = gathered[:, cross_width:]
    latents = query_all.shape[0]
    query_heads = query_all.reshape(latents, local_heads, HEAD_DIM)
    grad_heads = grad_all.reshape(latents, local_heads, HEAD_DIM)
    key_heads = prefix_k.reshape(tokens, local_heads, HEAD_DIM)
    value_heads = prefix_v.reshape(tokens, local_heads, HEAD_DIM)
    valid_keys = jnp.arange(tokens) < tokens - pad_counts[0]
    scores = head_scores(query_heads, key_heads, score_scale)
    scores = jnp.where(valid_keys[None, None, :], scores, -jnp.inf)
    row_max = jnp.max(scores, axis=2)
    shifted = jnp.exp(scores - row_max[:, :, None])
    row_sum = jnp.sum(shifted, axis=2)
    row_dots = dots_all.astype(jnp.float32)
    grad_probs = jnp.einsum(
        "qhd,khd->hqk", grad_heads, value_heads, preferred_element_type=jnp.float32
    )
    local_gs = shifted * (grad_probs - jnp.transpose(row_dots)[:, :, None]) * score_scale
    local_dq = jnp.einsum(
        "hqk,khd->qhd",
        local_gs,
        key_heads.astype(jnp.float32),
        precision=lax.Precision.HIGHEST,
        preferred_element_type=jnp.float32,
    )
    row_maxes, row_sums, own_dq = merged_with_dq(row_max, row_sum, local_dq)
    log_total = row_maxes + jnp.log(row_sums)
    weights = jnp.exp(scores - log_total[:, :, None])
    prefix_dv = (
        contract_rows(weights.astype(jnp.bfloat16), grad_heads)
        .reshape(tokens, feature_width)
        .astype(jnp.bfloat16)
    )
    grad_scores = scores_grad(weights, grad_heads, value_heads, row_dots, score_scale)
    prefix_dk = (
        contract_rows(grad_scores, query_heads).reshape(tokens, feature_width).astype(jnp.bfloat16)
    )
    cross_dq = own_dq.reshape(own_rows, feature_width).astype(jnp.bfloat16)
    everything = jnp.transpose(self_all.reshape(latents, 4, HEAD_DIM), (1, 0, 2))
    all_rows = everything.shape[1]
    query_every = everything[0].reshape(all_rows, 1, HEAD_DIM)
    key_every = everything[1].reshape(all_rows, 1, HEAD_DIM)
    value_every = everything[2].reshape(all_rows, 1, HEAD_DIM)
    grad_every = everything[3].reshape(all_rows, 1, HEAD_DIM)
    row_ids = jnp.arange(all_rows)
    causal_full = row_ids[:, None] >= row_ids[None, :]
    full_scores = head_scores(query_every, key_every, score_scale)
    full_scores = jnp.where(causal_full[None, :, :], full_scores, -jnp.inf)
    full_lse = jax.nn.logsumexp(full_scores, axis=2)
    full_weights = jnp.exp(full_scores - full_lse[:, :, None])
    full_half = full_weights.astype(jnp.bfloat16)
    full_out = contract_cols(full_half, value_every)
    full_dot = jnp.sum(grad_every.astype(jnp.float32) * full_out, axis=2)
    full_gs = scores_grad(full_weights, grad_every, value_every, full_dot, score_scale)
    cores = lax.axis_size("c")
    chip_rows = block_rows * cores
    chip_start = (lax.axis_index(SEQ_AXES) - core) * block_rows
    query_part = lax.dynamic_slice_in_dim(full_gs, chip_start, chip_rows, 1)
    key_part = lax.dynamic_slice_in_dim(full_gs, chip_start, chip_rows, 2)
    half_part = lax.dynamic_slice_in_dim(full_half, chip_start, chip_rows, 2)
    head_results = jnp.stack(
        [
            contract_cols(query_part, key_every),
            contract_rows(key_part, query_every),
            contract_rows(half_part, grad_every),
        ]
    ).astype(jnp.bfloat16)
    both = lax.all_gather(head_results.reshape(3, chip_rows, HEAD_DIM), "c", axis=0)
    mine = lax.dynamic_slice_in_dim(both, core * block_rows, block_rows, 2)
    mine = jnp.transpose(mine, (1, 2, 0, 3)).reshape(3, block_rows, feature_width)
    self_dq, self_dk, self_dv = mine[0], mine[1], mine[2]
    return (cross_dq, prefix_dk, prefix_dv, self_dq, self_dk, self_dv)


SEQ_AXES = ("y", "zh", "x", "c")


def solution(mesh):
    sizes = dict(mesh.shape)
    split = mesh.devices.reshape(4, 2, 4, 2, sizes["head"])
    mesh = jax.sharding.Mesh(split, (*SEQ_AXES, "zl"))
    in_specs = (
        P(SEQ_AXES, "zl"),
        P(SEQ_AXES, "zl"),
        P(SEQ_AXES, "zl"),
        P(SEQ_AXES, "zl"),
        P(SEQ_AXES, "zl"),
        P(SEQ_AXES),
        P((*SEQ_AXES, "zl"), None),
        P((*SEQ_AXES, "zl"), None),
        P((*SEQ_AXES, "zl"), None),
        P((*SEQ_AXES, "zl"), None),
    )
    out_specs = (
        P(SEQ_AXES, "zl"),
        P(SEQ_AXES, "zl"),
        P(SEQ_AXES, "zl"),
        P(SEQ_AXES, "zl"),
        P(SEQ_AXES, "zl"),
        P(SEQ_AXES, "zl"),
    )
    return jax.shard_map(shards, mesh=mesh, in_specs=in_specs, out_specs=out_specs, check_vma=False)
```

```python
import jax
import jax.numpy as jnp
from jax import lax
from jax.sharding import PartitionSpec as P

HEAD_DIM = 128


def in_one_piece(arrays, axis, dim, along):
    ends, at = ([], 0)
    for a in arrays[:-1]:
        at += a.shape[along]
        ends.append(at)
    both = jnp.concatenate(arrays, axis=along)
    return tuple(jnp.split(lax.all_gather(both, axis, axis=dim, tiled=True), ends, axis=along))


def from_everyone(x, axis):
    copies = jnp.broadcast_to(x, (lax.axis_size(axis), *x.shape))
    return lax.all_to_all(copies, axis, split_axis=0, concat_axis=0, tiled=True)


def all_in_one(x, axis):
    leaves = jax.tree.leaves(x)
    order = sorted(range(len(leaves)), key=lambda k: -leaves[k].size)
    width = (1, *leaves[order[0]].shape)[-1]
    lines = [
        jnp.pad(leaves[k].reshape(-1), (0, -leaves[k].size % width)).reshape(-1, width)
        for k in order
    ]
    both, at, found = (from_everyone(jnp.concatenate(lines), axis), 0, {})
    for k, line in zip(order, lines):
        section = both[:, at : at + len(line)].reshape(len(both), -1)
        found[k] = section[:, : leaves[k].size].reshape(-1, *leaves[k].shape)
        at += len(line)
    numbers = iter(range(len(leaves)))
    return jax.tree.map(lambda _: found[next(numbers)], x)


def joined_by_halves(pieces, combine):
    while len(jax.tree.leaves(pieces)[0]) > 1:
        pieces = jax.vmap(combine)(
            *(jax.tree.map(lambda part: part[side::2], pieces) for side in (0, 1))
        )
    return jax.tree.map(lambda part: part[0], pieces)


def merged(x, axis, combine):
    pieces = all_in_one(x, axis)
    return joined_by_halves(pieces, combine)


def split_up(x, dim, size):
    before, after = (x.shape[:dim], x.shape[dim + 1 :])
    return jnp.moveaxis(x.reshape(*before, size, -1, *after), dim, 0)


def sum_at_owner(x, axis, dim):
    size = lax.axis_size(axis)
    parts = lax.all_to_all(split_up(x, dim, size), axis, 0, 0, tiled=True)
    return jnp.sum(parts, axis=0)


def joined_along(parts, dim):
    lengths = list(parts.shape[1:])
    lengths[dim] *= parts.shape[0]
    return jnp.moveaxis(parts, 0, dim).reshape(lengths)


def gathered_copies(x, axis, dim):
    return joined_along(from_everyone(x, axis), dim)


def merge_stats(left_stats, right_stats):
    row_max = jnp.maximum(left_stats[0], right_stats[0])
    row_sum = left_stats[1] * jnp.exp(left_stats[0] - row_max) + right_stats[1] * jnp.exp(
        right_stats[0] - row_max
    )
    return (row_max, row_sum)


def head_scores(queries, key_rows, score_scale):
    return (
        jnp.einsum("qhd,khd->hqk", queries, key_rows, preferred_element_type=jnp.float32)
        * score_scale
    )


def scores_grad(weights, grad_rows, value_rows, row_dot, score_scale):
    grad_probs = jnp.einsum(
        "qhd,khd->hqk", grad_rows, value_rows, preferred_element_type=jnp.float32
    )
    return (weights * (grad_probs - jnp.transpose(row_dot)[:, :, None]) * score_scale).astype(
        jnp.bfloat16
    )


def contract_rows(left_rows, right_rows):
    return jnp.einsum("hqk,qhd->khd", left_rows, right_rows, preferred_element_type=jnp.float32)


def contract_cols(left_rows, right_rows):
    return jnp.einsum("hqk,khd->qhd", left_rows, right_rows, preferred_element_type=jnp.float32)


SEQ_PARTS = ("c", "x", "zh", "y")


GATHER_ORDER = ("zh", "c", "x", "y")


def gather_seq(x, axes):
    for axis in axes:
        x = from_everyone(x, axis)
    order = [GATHER_ORDER[::-1].index(axis) for axis in SEQ_AXES]
    x = jnp.transpose(x, (*order, *range(4, x.ndim)))
    return x.reshape(-1, *x.shape[5:])


def merged_with_dq(row_max, row_sum, partial_dq):
    rows = partial_dq.shape[0]
    width = partial_dq[0].size
    start = 0
    for axis in SEQ_AXES:
        size = lax.axis_size(axis)
        rows //= size
        stats = jnp.stack([row_max, row_sum]).reshape(1, -1)
        send = jnp.concatenate(
            [partial_dq.reshape(size, -1), jnp.broadcast_to(stats, (size, stats.shape[1]))], axis=1
        )
        got = lax.all_to_all(send, axis, 0, 0, tiled=True)
        got_dq = got[:, : rows * width].reshape(size, rows, *partial_dq.shape[1:])
        got_stats = got[:, rows * width :].reshape(size, 2, *row_max.shape)
        top = jnp.max(got_stats[:, 0], axis=0)
        rescale = jnp.exp(got_stats[:, 0] - top)
        row_sum = jnp.sum(got_stats[:, 1] * rescale, axis=0)
        row_max = top
        start = start + lax.axis_index(axis) * rows
        dq_rescale = jnp.transpose(lax.dynamic_slice_in_dim(rescale, start, rows, 2), (0, 2, 1))
        partial_dq = jnp.sum(dq_rescale[..., None] * got_dq, axis=0)
    own_sum = jnp.transpose(lax.dynamic_slice_in_dim(row_sum, start, rows, 1))
    return row_max, row_sum, partial_dq / own_sum[..., None]


def shards(
    cross_q,
    cross_out,
    cross_grad,
    prefix_k,
    prefix_v,
    pad_counts,
    self_q,
    self_k,
    self_v,
    self_grad,
):
    score_scale = HEAD_DIM ** (-0.5)
    own_rows, feature_width = cross_q.shape
    local_heads = feature_width // HEAD_DIM
    tokens = prefix_k.shape[0]
    grad_own = cross_grad.reshape(own_rows, local_heads, HEAD_DIM).astype(jnp.float32)
    out_own = cross_out.reshape(own_rows, local_heads, HEAD_DIM).astype(jnp.float32)
    row_dot = jnp.sum(grad_own * out_own, axis=2).astype(jnp.bfloat16)
    head_groups = lax.axis_size("zl")
    stacked = jnp.stack([self_q, self_k, self_v, self_grad]).reshape(4, head_groups, feature_width)
    regrouped = lax.all_to_all(
        jnp.transpose(stacked, (1, 0, 2)), "zl", split_axis=0, concat_axis=0, tiled=True
    )
    block_rows = regrouped.shape[0]
    self_cols = regrouped.reshape(block_rows, -1)
    cross_cols = jnp.concatenate((cross_q, cross_grad, row_dot), axis=1)
    cross_width = cross_cols.shape[1]
    first = jnp.concatenate((cross_cols, self_cols), axis=1)
    for axis in GATHER_ORDER[:2]:
        first = from_everyone(first, axis)
    core = lax.axis_index("c")
    self_heads = first[..., cross_width:].reshape(*first.shape[:-1], 4, local_heads, HEAD_DIM)
    self_mine = lax.dynamic_index_in_dim(self_heads, core, axis=4, keepdims=False)
    rest = jnp.concatenate(
        (first[..., :cross_width], self_mine.reshape(*first.shape[:-1], -1)), axis=-1
    )
    gathered = gather_seq(rest, GATHER_ORDER[2:])
    query_all = gathered[:, : cross_q.shape[1]]
    grad_all = gathered[:, cross_q.shape[1] : 2 * cross_q.shape[1]]
    dots_all = gathered[:, 2 * cross_q.shape[1] : cross_width]
    self_all = gathered[:, cross_width:]
    latents = query_all.shape[0]
    query_heads = query_all.reshape(latents, local_heads, HEAD_DIM)
    grad_heads = grad_all.reshape(latents, local_heads, HEAD_DIM)
    key_heads = prefix_k.reshape(tokens, local_heads, HEAD_DIM)
    value_heads = prefix_v.reshape(tokens, local_heads, HEAD_DIM)
    valid_keys = jnp.arange(tokens) < tokens - pad_counts[0]
    scores = head_scores(query_heads, key_heads, score_scale)
    scores = jnp.where(valid_keys[None, None, :], scores, -jnp.inf)
    row_max = jnp.max(scores, axis=2)
    shifted = jnp.exp(scores - row_max[:, :, None])
    row_sum = jnp.sum(shifted, axis=2)
    row_dots = dots_all.astype(jnp.float32)
    grad_probs = jnp.einsum(
        "qhd,khd->hqk", grad_heads, value_heads, preferred_element_type=jnp.float32
    )
    local_gs = shifted * (grad_probs - jnp.transpose(row_dots)[:, :, None]) * score_scale
    local_dq = jnp.einsum(
        "hqk,khd->qhd",
        local_gs,
        key_heads.astype(jnp.float32),
        precision=lax.Precision.HIGHEST,
        preferred_element_type=jnp.float32,
    )
    row_maxes, row_sums, own_dq = merged_with_dq(row_max, row_sum, local_dq)
    log_total = row_maxes + jnp.log(row_sums)
    weights = jnp.exp(scores - log_total[:, :, None])
    prefix_dv = (
        contract_rows(weights.astype(jnp.bfloat16), grad_heads)
        .reshape(tokens, feature_width)
        .astype(jnp.bfloat16)
    )
    grad_scores = scores_grad(weights, grad_heads, value_heads, row_dots, score_scale)
    prefix_dk = (
        contract_rows(grad_scores, query_heads).reshape(tokens, feature_width).astype(jnp.bfloat16)
    )
    cross_dq = own_dq.reshape(own_rows, feature_width).astype(jnp.bfloat16)
    everything = jnp.transpose(self_all.reshape(latents, 4, HEAD_DIM), (1, 0, 2))
    all_rows = everything.shape[1]
    query_every = everything[0].reshape(all_rows, 1, HEAD_DIM)
    key_every = everything[1].reshape(all_rows, 1, HEAD_DIM)
    value_every = everything[2].reshape(all_rows, 1, HEAD_DIM)
    grad_every = everything[3].reshape(all_rows, 1, HEAD_DIM)
    row_ids = jnp.arange(all_rows)
    causal_full = row_ids[:, None] >= row_ids[None, :]
    full_scores = head_scores(query_every, key_every, score_scale)
    full_scores = jnp.where(causal_full[None, :, :], full_scores, -jnp.inf)
    full_lse = jax.nn.logsumexp(full_scores, axis=2)
    full_weights = jnp.exp(full_scores - full_lse[:, :, None])
    full_half = full_weights.astype(jnp.bfloat16)
    full_out = contract_cols(full_half, value_every)
    full_dot = jnp.sum(grad_every.astype(jnp.float32) * full_out, axis=2)
    full_gs = scores_grad(full_weights, grad_every, value_every, full_dot, score_scale)
    cores = lax.axis_size("c")
    chip_rows = block_rows * cores
    chip_start = (lax.axis_index(SEQ_AXES) - core) * block_rows
    query_part = lax.dynamic_slice_in_dim(full_gs, chip_start, chip_rows, 1)
    key_part = lax.dynamic_slice_in_dim(full_gs, chip_start, chip_rows, 2)
    half_part = lax.dynamic_slice_in_dim(full_half, chip_start, chip_rows, 2)
    head_results = jnp.stack(
        [
            contract_cols(query_part, key_every),
            contract_rows(key_part, query_every),
            contract_rows(half_part, grad_every),
        ]
    ).astype(jnp.bfloat16)
    both = lax.all_gather(head_results.reshape(3, chip_rows, HEAD_DIM), "c", axis=0)
    mine = lax.dynamic_slice_in_dim(both, core * block_rows, block_rows, 2)
    mine = jnp.transpose(mine, (1, 2, 0, 3)).reshape(3, block_rows, feature_width)
    self_dq, self_dk, self_dv = mine[0], mine[1], mine[2]
    return (cross_dq, prefix_dk, prefix_dv, self_dq, self_dk, self_dv)


SEQ_AXES = ("y", "zh", "x", "c")


def solution(mesh):
    sizes = dict(mesh.shape)
    split = mesh.devices.reshape(4, 2, 4, 2, sizes["head"])
    mesh = jax.sharding.Mesh(split, (*SEQ_AXES, "zl"))
    in_specs = (
        P(SEQ_AXES, "zl"),
        P(SEQ_AXES, "zl"),
        P(SEQ_AXES, "zl"),
        P(SEQ_AXES, "zl"),
        P(SEQ_AXES, "zl"),
        P(SEQ_AXES),
        P((*SEQ_AXES, "zl"), None),
        P((*SEQ_AXES, "zl"), None),
        P((*SEQ_AXES, "zl"), None),
        P((*SEQ_AXES, "zl"), None),
    )
    out_specs = (
        P(SEQ_AXES, "zl"),
        P(SEQ_AXES, "zl"),
        P(SEQ_AXES, "zl"),
        P(SEQ_AXES, "zl"),
        P(SEQ_AXES, "zl"),
        P(SEQ_AXES, "zl"),
    )
    return jax.shard_map(shards, mesh=mesh, in_specs=in_specs, out_specs=out_specs, check_vma=False)
```

```python
import jax
import jax.numpy as jnp
from jax import lax
from jax.sharding import PartitionSpec as P

HEAD_DIM = 128


def in_one_piece(arrays, axis, dim, along):
    ends, at = ([], 0)
    for a in arrays[:-1]:
        at += a.shape[along]
        ends.append(at)
    both = jnp.concatenate(arrays, axis=along)
    return tuple(jnp.split(lax.all_gather(both, axis, axis=dim, tiled=True), ends, axis=along))


def from_everyone(x, axis):
    copies = jnp.broadcast_to(x, (lax.axis_size(axis), *x.shape))
    return lax.all_to_all(copies, axis, split_axis=0, concat_axis=0, tiled=True)


def all_in_one(x, axis):
    leaves = jax.tree.leaves(x)
    order = sorted(range(len(leaves)), key=lambda k: -leaves[k].size)
    width = (1, *leaves[order[0]].shape)[-1]
    lines = [
        jnp.pad(leaves[k].reshape(-1), (0, -leaves[k].size % width)).reshape(-1, width)
        for k in order
    ]
    both, at, found = (from_everyone(jnp.concatenate(lines), axis), 0, {})
    for k, line in zip(order, lines):
        section = both[:, at : at + len(line)].reshape(len(both), -1)
        found[k] = section[:, : leaves[k].size].reshape(-1, *leaves[k].shape)
        at += len(line)
    numbers = iter(range(len(leaves)))
    return jax.tree.map(lambda _: found[next(numbers)], x)


def joined_by_halves(pieces, combine):
    while len(jax.tree.leaves(pieces)[0]) > 1:
        pieces = jax.vmap(combine)(
            *(jax.tree.map(lambda part: part[side::2], pieces) for side in (0, 1))
        )
    return jax.tree.map(lambda part: part[0], pieces)


def merged(x, axis, combine):
    pieces = all_in_one(x, axis)
    return joined_by_halves(pieces, combine)


def split_up(x, dim, size):
    before, after = (x.shape[:dim], x.shape[dim + 1 :])
    return jnp.moveaxis(x.reshape(*before, size, -1, *after), dim, 0)


def sum_at_owner(x, axis, dim):
    size = lax.axis_size(axis)
    parts = lax.all_to_all(split_up(x, dim, size), axis, 0, 0, tiled=True)
    return jnp.sum(parts, axis=0)


def joined_along(parts, dim):
    lengths = list(parts.shape[1:])
    lengths[dim] *= parts.shape[0]
    return jnp.moveaxis(parts, 0, dim).reshape(lengths)


def gathered_copies(x, axis, dim):
    return joined_along(from_everyone(x, axis), dim)


def merge_stats(left_stats, right_stats):
    row_max = jnp.maximum(left_stats[0], right_stats[0])
    row_sum = left_stats[1] * jnp.exp(left_stats[0] - row_max) + right_stats[1] * jnp.exp(
        right_stats[0] - row_max
    )
    return (row_max, row_sum)


def head_scores(queries, key_rows, score_scale):
    return (
        jnp.einsum("qhd,khd->hqk", queries, key_rows, preferred_element_type=jnp.float32)
        * score_scale
    )


def scores_grad(weights, grad_rows, value_rows, row_dot, score_scale):
    grad_probs = jnp.einsum(
        "qhd,khd->hqk", grad_rows, value_rows, preferred_element_type=jnp.float32
    )
    return (weights * (grad_probs - jnp.transpose(row_dot)[:, :, None]) * score_scale).astype(
        jnp.bfloat16
    )


def contract_rows(left_rows, right_rows):
    return jnp.einsum("hqk,qhd->khd", left_rows, right_rows, preferred_element_type=jnp.float32)


def contract_cols(left_rows, right_rows):
    return jnp.einsum("hqk,khd->qhd", left_rows, right_rows, preferred_element_type=jnp.float32)


SEQ_PARTS = ("c", "x", "zh", "y")


GATHER_ORDER = ("zh", "c", "x", "y")


def gather_seq(x, axes):
    for axis in axes:
        x = from_everyone(x, axis)
    order = [GATHER_ORDER[::-1].index(axis) for axis in SEQ_AXES]
    x = jnp.transpose(x, (*order, *range(4, x.ndim)))
    return x.reshape(-1, *x.shape[5:])


def merged_with_dq(row_max, row_sum, partial_dq):
    rows = partial_dq.shape[0]
    width = partial_dq[0].size
    start = 0
    for axis in SEQ_AXES:
        size = lax.axis_size(axis)
        rows //= size
        stats = jnp.stack([row_max, row_sum]).reshape(1, -1)
        send = jnp.concatenate(
            [partial_dq.reshape(size, -1), jnp.broadcast_to(stats, (size, stats.shape[1]))], axis=1
        )
        got = lax.all_to_all(send, axis, 0, 0, tiled=True)
        got_dq = got[:, : rows * width].reshape(size, rows, *partial_dq.shape[1:])
        got_stats = got[:, rows * width :].reshape(size, 2, *row_max.shape)
        top = jnp.max(got_stats[:, 0], axis=0)
        rescale = jnp.exp(got_stats[:, 0] - top)
        row_sum = jnp.sum(got_stats[:, 1] * rescale, axis=0)
        row_max = top
        start = start + lax.axis_index(axis) * rows
        dq_rescale = jnp.transpose(lax.dynamic_slice_in_dim(rescale, start, rows, 2), (0, 2, 1))
        partial_dq = jnp.sum(dq_rescale[..., None] * got_dq, axis=0)
    own_sum = jnp.transpose(lax.dynamic_slice_in_dim(row_sum, start, rows, 1))
    return row_max, row_sum, partial_dq / own_sum[..., None]


def shards(
    cross_q,
    cross_out,
    cross_grad,
    prefix_k,
    prefix_v,
    pad_counts,
    self_q,
    self_k,
    self_v,
    self_grad,
):
    score_scale = HEAD_DIM ** (-0.5)
    own_rows, feature_width = cross_q.shape
    local_heads = feature_width // HEAD_DIM
    tokens = prefix_k.shape[0]
    grad_own = cross_grad.reshape(own_rows, local_heads, HEAD_DIM).astype(jnp.float32)
    out_own = cross_out.reshape(own_rows, local_heads, HEAD_DIM).astype(jnp.float32)
    row_dot = jnp.sum(grad_own * out_own, axis=2).astype(jnp.bfloat16)
    head_groups = lax.axis_size("zl")
    far_pairs = lax.axis_size("zh")
    stacked = jnp.stack([self_q, self_k, self_v, self_grad]).reshape(4, head_groups, feature_width)
    self_chunks = jnp.transpose(stacked, (1, 0, 2)).reshape(head_groups, -1)
    cross_cols = jnp.concatenate((cross_q, cross_grad, row_dot), axis=1)
    cross_width = cross_cols.shape[1]
    self_width = self_chunks.shape[1]
    outgoing = jnp.concatenate(
        (
            self_chunks,
            jnp.broadcast_to(cross_cols.reshape(1, -1), (head_groups, cross_cols.size)),
        ),
        axis=1,
    )
    outgoing = jnp.broadcast_to(outgoing[None], (far_pairs, *outgoing.shape))
    incoming = lax.all_to_all(
        outgoing.reshape(far_pairs * head_groups, -1), ("zh", "zl"), 0, 0, tiled=True
    ).reshape(far_pairs, head_groups, -1)
    block_rows = head_groups
    self_cols = incoming[:, :, :self_width]
    far_cross = lax.dynamic_index_in_dim(incoming, lax.axis_index("zl"), 1, keepdims=False)
    far_cross = far_cross[:, self_width:].reshape(far_pairs, own_rows, cross_width)
    first = jnp.concatenate((far_cross, self_cols), axis=2)
    first = from_everyone(first, "c")
    core = lax.axis_index("c")
    self_heads = first[..., cross_width:].reshape(*first.shape[:-1], 4, local_heads, HEAD_DIM)
    self_mine = lax.dynamic_index_in_dim(self_heads, core, axis=4, keepdims=False)
    rest = jnp.concatenate(
        (first[..., :cross_width], self_mine.reshape(*first.shape[:-1], -1)), axis=-1
    )
    gathered = gather_seq(rest, GATHER_ORDER[2:])
    query_all = gathered[:, : cross_q.shape[1]]
    grad_all = gathered[:, cross_q.shape[1] : 2 * cross_q.shape[1]]
    dots_all = gathered[:, 2 * cross_q.shape[1] : cross_width]
    self_all = gathered[:, cross_width:]
    latents = query_all.shape[0]
    query_heads = query_all.reshape(latents, local_heads, HEAD_DIM)
    grad_heads = grad_all.reshape(latents, local_heads, HEAD_DIM)
    key_heads = prefix_k.reshape(tokens, local_heads, HEAD_DIM)
    value_heads = prefix_v.reshape(tokens, local_heads, HEAD_DIM)
    valid_keys = jnp.arange(tokens) < tokens - pad_counts[0]
    scores = head_scores(query_heads, key_heads, score_scale)
    scores = jnp.where(valid_keys[None, None, :], scores, -jnp.inf)
    row_max = jnp.max(scores, axis=2)
    shifted = jnp.exp(scores - row_max[:, :, None])
    row_sum = jnp.sum(shifted, axis=2)
    row_dots = dots_all.astype(jnp.float32)
    grad_probs = jnp.einsum(
        "qhd,khd->hqk", grad_heads, value_heads, preferred_element_type=jnp.float32
    )
    local_gs = shifted * (grad_probs - jnp.transpose(row_dots)[:, :, None]) * score_scale
    local_dq = jnp.einsum(
        "hqk,khd->qhd",
        local_gs,
        key_heads.astype(jnp.float32),
        precision=lax.Precision.HIGHEST,
        preferred_element_type=jnp.float32,
    )
    row_maxes, row_sums, own_dq = merged_with_dq(row_max, row_sum, local_dq)
    log_total = row_maxes + jnp.log(row_sums)
    weights = jnp.exp(scores - log_total[:, :, None])
    prefix_dv = (
        contract_rows(weights.astype(jnp.bfloat16), grad_heads)
        .reshape(tokens, feature_width)
        .astype(jnp.bfloat16)
    )
    grad_scores = scores_grad(weights, grad_heads, value_heads, row_dots, score_scale)
    prefix_dk = (
        contract_rows(grad_scores, query_heads).reshape(tokens, feature_width).astype(jnp.bfloat16)
    )
    cross_dq = own_dq.reshape(own_rows, feature_width).astype(jnp.bfloat16)
    everything = jnp.transpose(self_all.reshape(latents, 4, HEAD_DIM), (1, 0, 2))
    all_rows = everything.shape[1]
    query_every = everything[0].reshape(all_rows, 1, HEAD_DIM)
    key_every = everything[1].reshape(all_rows, 1, HEAD_DIM)
    value_every = everything[2].reshape(all_rows, 1, HEAD_DIM)
    grad_every = everything[3].reshape(all_rows, 1, HEAD_DIM)
    row_ids = jnp.arange(all_rows)
    causal_full = row_ids[:, None] >= row_ids[None, :]
    full_scores = head_scores(query_every, key_every, score_scale)
    full_scores = jnp.where(causal_full[None, :, :], full_scores, -jnp.inf)
    full_lse = jax.nn.logsumexp(full_scores, axis=2)
    full_weights = jnp.exp(full_scores - full_lse[:, :, None])
    full_half = full_weights.astype(jnp.bfloat16)
    full_out = contract_cols(full_half, value_every)
    full_dot = jnp.sum(grad_every.astype(jnp.float32) * full_out, axis=2)
    full_gs = scores_grad(full_weights, grad_every, value_every, full_dot, score_scale)
    cores = lax.axis_size("c")
    chip_rows = block_rows * cores
    chip_start = (lax.axis_index(SEQ_AXES) - core) * block_rows
    query_part = lax.dynamic_slice_in_dim(full_gs, chip_start, chip_rows, 1)
    key_part = lax.dynamic_slice_in_dim(full_gs, chip_start, chip_rows, 2)
    half_part = lax.dynamic_slice_in_dim(full_half, chip_start, chip_rows, 2)
    head_results = jnp.stack(
        [
            contract_cols(query_part, key_every),
            contract_rows(key_part, query_every),
            contract_rows(half_part, grad_every),
        ]
    ).astype(jnp.bfloat16)
    both = lax.all_gather(head_results.reshape(3, chip_rows, HEAD_DIM), "c", axis=0)
    mine = lax.dynamic_slice_in_dim(both, core * block_rows, block_rows, 2)
    mine = jnp.transpose(mine, (1, 2, 0, 3)).reshape(3, block_rows, feature_width)
    self_dq, self_dk, self_dv = mine[0], mine[1], mine[2]
    return (cross_dq, prefix_dk, prefix_dv, self_dq, self_dk, self_dv)


SEQ_AXES = ("y", "zh", "x", "c")


def solution(mesh):
    sizes = dict(mesh.shape)
    split = mesh.devices.reshape(4, 2, 4, 2, sizes["head"])
    mesh = jax.sharding.Mesh(split, (*SEQ_AXES, "zl"))
    in_specs = (
        P(SEQ_AXES, "zl"),
        P(SEQ_AXES, "zl"),
        P(SEQ_AXES, "zl"),
        P(SEQ_AXES, "zl"),
        P(SEQ_AXES, "zl"),
        P(SEQ_AXES),
        P((*SEQ_AXES, "zl"), None),
        P((*SEQ_AXES, "zl"), None),
        P((*SEQ_AXES, "zl"), None),
        P((*SEQ_AXES, "zl"), None),
    )
    out_specs = (
        P(SEQ_AXES, "zl"),
        P(SEQ_AXES, "zl"),
        P(SEQ_AXES, "zl"),
        P(SEQ_AXES, "zl"),
        P(SEQ_AXES, "zl"),
        P(SEQ_AXES, "zl"),
    )
    return jax.shard_map(shards, mesh=mesh, in_specs=in_specs, out_specs=out_specs, check_vma=False)
```

```python
import jax
import jax.numpy as jnp
from jax import lax
from jax.sharding import PartitionSpec as P

HEAD_DIM = 128


def in_one_piece(arrays, axis, dim, along):
    ends, at = ([], 0)
    for a in arrays[:-1]:
        at += a.shape[along]
        ends.append(at)
    both = jnp.concatenate(arrays, axis=along)
    return tuple(jnp.split(lax.all_gather(both, axis, axis=dim, tiled=True), ends, axis=along))


def from_everyone(x, axis):
    copies = jnp.broadcast_to(x, (lax.axis_size(axis), *x.shape))
    return lax.all_to_all(copies, axis, split_axis=0, concat_axis=0, tiled=True)


def all_in_one(x, axis):
    leaves = jax.tree.leaves(x)
    order = sorted(range(len(leaves)), key=lambda k: -leaves[k].size)
    width = (1, *leaves[order[0]].shape)[-1]
    lines = [
        jnp.pad(leaves[k].reshape(-1), (0, -leaves[k].size % width)).reshape(-1, width)
        for k in order
    ]
    both, at, found = (from_everyone(jnp.concatenate(lines), axis), 0, {})
    for k, line in zip(order, lines):
        section = both[:, at : at + len(line)].reshape(len(both), -1)
        found[k] = section[:, : leaves[k].size].reshape(-1, *leaves[k].shape)
        at += len(line)
    numbers = iter(range(len(leaves)))
    return jax.tree.map(lambda _: found[next(numbers)], x)


def joined_by_halves(pieces, combine):
    while len(jax.tree.leaves(pieces)[0]) > 1:
        pieces = jax.vmap(combine)(
            *(jax.tree.map(lambda part: part[side::2], pieces) for side in (0, 1))
        )
    return jax.tree.map(lambda part: part[0], pieces)


def merged(x, axis, combine):
    pieces = all_in_one(x, axis)
    return joined_by_halves(pieces, combine)


def split_up(x, dim, size):
    before, after = (x.shape[:dim], x.shape[dim + 1 :])
    return jnp.moveaxis(x.reshape(*before, size, -1, *after), dim, 0)


def sum_at_owner(x, axis, dim):
    size = lax.axis_size(axis)
    parts = lax.all_to_all(split_up(x, dim, size), axis, 0, 0, tiled=True)
    return jnp.sum(parts, axis=0)


def joined_along(parts, dim):
    lengths = list(parts.shape[1:])
    lengths[dim] *= parts.shape[0]
    return jnp.moveaxis(parts, 0, dim).reshape(lengths)


def gathered_copies(x, axis, dim):
    return joined_along(from_everyone(x, axis), dim)


def merge_stats(left_stats, right_stats):
    row_max = jnp.maximum(left_stats[0], right_stats[0])
    row_sum = left_stats[1] * jnp.exp(left_stats[0] - row_max) + right_stats[1] * jnp.exp(
        right_stats[0] - row_max
    )
    return (row_max, row_sum)


def head_scores(queries, key_rows, score_scale):
    return (
        jnp.einsum("qhd,khd->hqk", queries, key_rows, preferred_element_type=jnp.float32)
        * score_scale
    )


def scores_grad(weights, grad_rows, value_rows, row_dot, score_scale):
    grad_probs = jnp.einsum(
        "qhd,khd->hqk", grad_rows, value_rows, preferred_element_type=jnp.float32
    )
    return (weights * (grad_probs - jnp.transpose(row_dot)[:, :, None]) * score_scale).astype(
        jnp.bfloat16
    )


def contract_rows(left_rows, right_rows):
    return jnp.einsum("hqk,qhd->khd", left_rows, right_rows, preferred_element_type=jnp.float32)


def contract_cols(left_rows, right_rows):
    return jnp.einsum("hqk,khd->qhd", left_rows, right_rows, preferred_element_type=jnp.float32)


SEQ_PARTS = ("c", "x", "zh", "y")


GATHER_ORDER = ("zh", "c", "x", "y")


def gather_seq(x, axes):
    for axis in axes:
        x = from_everyone(x, axis)
    order = [GATHER_ORDER[::-1].index(axis) for axis in SEQ_AXES]
    x = jnp.transpose(x, (*order, *range(4, x.ndim)))
    return x.reshape(-1, *x.shape[5:])


MERGE_ORDER = ("c", "y", "x", "zh")


def pick_own(values, digits, at):
    for axis in digits:
        values = lax.dynamic_index_in_dim(
            values, lax.axis_index(axis), at + SEQ_AXES.index(axis) - digits.index(axis), False
        )
    return values


def merged_with_dq(row_max, row_sum, partial_dq):
    sizes = [lax.axis_size(axis) for axis in SEQ_AXES]
    heads = row_max.shape[0]
    by_digit = (heads, *sizes, -1)
    partial_dq = partial_dq.reshape(*sizes, -1, *partial_dq.shape[1:])
    left = list(SEQ_AXES)
    done = []
    for axis in MERGE_ORDER:
        size = lax.axis_size(axis)
        moved = jnp.moveaxis(partial_dq, left.index(axis), 0)
        left.remove(axis)
        done.append(axis)
        stats = jnp.stack([row_max, row_sum]).reshape(1, -1)
        send = jnp.concatenate(
            [moved.reshape(size, -1), jnp.broadcast_to(stats, (size, stats.shape[1]))], axis=1
        )
        got = lax.all_to_all(send, axis, 0, 0, tiled=True)
        got_dq = got[:, : moved[0].size].reshape(moved.shape)
        got_stats = got[:, moved[0].size :].reshape(size, 2, *row_max.shape)
        top = jnp.max(got_stats[:, 0], axis=0)
        rescale = jnp.exp(got_stats[:, 0] - top)
        row_sum = jnp.sum(got_stats[:, 1] * rescale, axis=0)
        row_max = top
        own_done = [d for d in SEQ_AXES if d in done]
        dq_rescale = pick_own(rescale.reshape(size, *by_digit), own_done, 2)
        dq_rescale = jnp.moveaxis(dq_rescale, 1, -1)
        partial_dq = jnp.sum(dq_rescale[..., None] * got_dq, axis=0)
    own_sum = jnp.transpose(pick_own(row_sum.reshape(by_digit), list(SEQ_AXES), 1))
    return row_max, row_sum, partial_dq / own_sum[..., None]


def shards(
    cross_q,
    cross_out,
    cross_grad,
    prefix_k,
    prefix_v,
    pad_counts,
    self_q,
    self_k,
    self_v,
    self_grad,
):
    score_scale = HEAD_DIM ** (-0.5)
    own_rows, feature_width = cross_q.shape
    local_heads = feature_width // HEAD_DIM
    tokens = prefix_k.shape[0]
    grad_own = cross_grad.reshape(own_rows, local_heads, HEAD_DIM).astype(jnp.float32)
    out_own = cross_out.reshape(own_rows, local_heads, HEAD_DIM).astype(jnp.float32)
    row_dot = jnp.sum(grad_own * out_own, axis=2).astype(jnp.bfloat16)
    head_groups = lax.axis_size("zl")
    far_pairs = lax.axis_size("zh")
    stacked = jnp.stack([self_q, self_k, self_v, self_grad]).reshape(4, head_groups, feature_width)
    self_chunks = jnp.transpose(stacked, (1, 0, 2)).reshape(head_groups, -1)
    cross_cols = jnp.concatenate((cross_q, cross_grad, row_dot), axis=1)
    cross_width = cross_cols.shape[1]
    self_width = self_chunks.shape[1]
    outgoing = jnp.concatenate(
        (
            self_chunks,
            jnp.broadcast_to(cross_cols.reshape(1, -1), (head_groups, cross_cols.size)),
        ),
        axis=1,
    )
    outgoing = jnp.broadcast_to(outgoing[None], (far_pairs, *outgoing.shape))
    incoming = lax.all_to_all(
        outgoing.reshape(far_pairs * head_groups, -1), ("zh", "zl"), 0, 0, tiled=True
    ).reshape(far_pairs, head_groups, -1)
    block_rows = head_groups
    self_cols = incoming[:, :, :self_width]
    far_cross = lax.dynamic_index_in_dim(incoming, lax.axis_index("zl"), 1, keepdims=False)
    far_cross = far_cross[:, self_width:].reshape(far_pairs, own_rows, cross_width)
    first = jnp.concatenate((far_cross, self_cols), axis=2)
    first = from_everyone(first, "c")
    core = lax.axis_index("c")
    self_heads = first[..., cross_width:].reshape(*first.shape[:-1], 4, local_heads, HEAD_DIM)
    self_mine = lax.dynamic_index_in_dim(self_heads, core, axis=4, keepdims=False)
    rest = jnp.concatenate(
        (first[..., :cross_width], self_mine.reshape(*first.shape[:-1], -1)), axis=-1
    )
    gathered = gather_seq(rest, GATHER_ORDER[2:])
    query_all = gathered[:, : cross_q.shape[1]]
    grad_all = gathered[:, cross_q.shape[1] : 2 * cross_q.shape[1]]
    dots_all = gathered[:, 2 * cross_q.shape[1] : cross_width]
    self_all = gathered[:, cross_width:]
    latents = query_all.shape[0]
    query_heads = query_all.reshape(latents, local_heads, HEAD_DIM)
    grad_heads = grad_all.reshape(latents, local_heads, HEAD_DIM)
    key_heads = prefix_k.reshape(tokens, local_heads, HEAD_DIM)
    value_heads = prefix_v.reshape(tokens, local_heads, HEAD_DIM)
    valid_keys = jnp.arange(tokens) < tokens - pad_counts[0]
    scores = head_scores(query_heads, key_heads, score_scale)
    scores = jnp.where(valid_keys[None, None, :], scores, -jnp.inf)
    row_max = jnp.max(scores, axis=2)
    shifted = jnp.exp(scores - row_max[:, :, None])
    row_sum = jnp.sum(shifted, axis=2)
    row_dots = dots_all.astype(jnp.float32)
    grad_probs = jnp.einsum(
        "qhd,khd->hqk", grad_heads, value_heads, preferred_element_type=jnp.float32
    )
    local_gs = shifted * (grad_probs - jnp.transpose(row_dots)[:, :, None]) * score_scale
    local_dq = jnp.einsum(
        "hqk,khd->qhd",
        local_gs,
        key_heads.astype(jnp.float32),
        precision=lax.Precision.HIGHEST,
        preferred_element_type=jnp.float32,
    )
    row_maxes, row_sums, own_dq = merged_with_dq(row_max, row_sum, local_dq)
    log_total = row_maxes + jnp.log(row_sums)
    weights = jnp.exp(scores - log_total[:, :, None])
    prefix_dv = (
        contract_rows(weights.astype(jnp.bfloat16), grad_heads)
        .reshape(tokens, feature_width)
        .astype(jnp.bfloat16)
    )
    grad_scores = scores_grad(weights, grad_heads, value_heads, row_dots, score_scale)
    prefix_dk = (
        contract_rows(grad_scores, query_heads).reshape(tokens, feature_width).astype(jnp.bfloat16)
    )
    cross_dq = own_dq.reshape(own_rows, feature_width).astype(jnp.bfloat16)
    everything = jnp.transpose(self_all.reshape(latents, 4, HEAD_DIM), (1, 0, 2))
    all_rows = everything.shape[1]
    query_every = everything[0].reshape(all_rows, 1, HEAD_DIM)
    key_every = everything[1].reshape(all_rows, 1, HEAD_DIM)
    value_every = everything[2].reshape(all_rows, 1, HEAD_DIM)
    grad_every = everything[3].reshape(all_rows, 1, HEAD_DIM)
    row_ids = jnp.arange(all_rows)
    causal_full = row_ids[:, None] >= row_ids[None, :]
    full_scores = head_scores(query_every, key_every, score_scale)
    full_scores = jnp.where(causal_full[None, :, :], full_scores, -jnp.inf)
    full_lse = jax.nn.logsumexp(full_scores, axis=2)
    full_weights = jnp.exp(full_scores - full_lse[:, :, None])
    full_half = full_weights.astype(jnp.bfloat16)
    full_out = contract_cols(full_half, value_every)
    full_dot = jnp.sum(grad_every.astype(jnp.float32) * full_out, axis=2)
    full_gs = scores_grad(full_weights, grad_every, value_every, full_dot, score_scale)
    cores = lax.axis_size("c")
    chip_rows = block_rows * cores
    chip_start = (lax.axis_index(SEQ_AXES) - core) * block_rows
    query_part = lax.dynamic_slice_in_dim(full_gs, chip_start, chip_rows, 1)
    key_part = lax.dynamic_slice_in_dim(full_gs, chip_start, chip_rows, 2)
    half_part = lax.dynamic_slice_in_dim(full_half, chip_start, chip_rows, 2)
    head_results = jnp.stack(
        [
            contract_cols(query_part, key_every),
            contract_rows(key_part, query_every),
            contract_rows(half_part, grad_every),
        ]
    ).astype(jnp.bfloat16)
    both = lax.all_gather(head_results.reshape(3, chip_rows, HEAD_DIM), "c", axis=0)
    mine = lax.dynamic_slice_in_dim(both, core * block_rows, block_rows, 2)
    mine = jnp.transpose(mine, (1, 2, 0, 3)).reshape(3, block_rows, feature_width)
    self_dq, self_dk, self_dv = mine[0], mine[1], mine[2]
    return (cross_dq, prefix_dk, prefix_dv, self_dq, self_dk, self_dv)


SEQ_AXES = ("y", "zh", "x", "c")


def solution(mesh):
    sizes = dict(mesh.shape)
    split = mesh.devices.reshape(4, 2, 4, 2, sizes["head"])
    mesh = jax.sharding.Mesh(split, (*SEQ_AXES, "zl"))
    in_specs = (
        P(SEQ_AXES, "zl"),
        P(SEQ_AXES, "zl"),
        P(SEQ_AXES, "zl"),
        P(SEQ_AXES, "zl"),
        P(SEQ_AXES, "zl"),
        P(SEQ_AXES),
        P((*SEQ_AXES, "zl"), None),
        P((*SEQ_AXES, "zl"), None),
        P((*SEQ_AXES, "zl"), None),
        P((*SEQ_AXES, "zl"), None),
    )
    out_specs = (
        P(SEQ_AXES, "zl"),
        P(SEQ_AXES, "zl"),
        P(SEQ_AXES, "zl"),
        P(SEQ_AXES, "zl"),
        P(SEQ_AXES, "zl"),
        P(SEQ_AXES, "zl"),
    )
    return jax.shard_map(shards, mesh=mesh, in_specs=in_specs, out_specs=out_specs, check_vma=False)
```

```python
import jax
import jax.numpy as jnp
from jax import lax
from jax.sharding import PartitionSpec as P

HEAD_DIM = 128


def in_one_piece(arrays, axis, dim, along):
    ends, at = ([], 0)
    for a in arrays[:-1]:
        at += a.shape[along]
        ends.append(at)
    both = jnp.concatenate(arrays, axis=along)
    return tuple(jnp.split(lax.all_gather(both, axis, axis=dim, tiled=True), ends, axis=along))


def from_everyone(x, axis):
    copies = jnp.broadcast_to(x, (lax.axis_size(axis), *x.shape))
    return lax.all_to_all(copies, axis, split_axis=0, concat_axis=0, tiled=True)


def all_in_one(x, axis):
    leaves = jax.tree.leaves(x)
    order = sorted(range(len(leaves)), key=lambda k: -leaves[k].size)
    width = (1, *leaves[order[0]].shape)[-1]
    lines = [
        jnp.pad(leaves[k].reshape(-1), (0, -leaves[k].size % width)).reshape(-1, width)
        for k in order
    ]
    both, at, found = (from_everyone(jnp.concatenate(lines), axis), 0, {})
    for k, line in zip(order, lines):
        section = both[:, at : at + len(line)].reshape(len(both), -1)
        found[k] = section[:, : leaves[k].size].reshape(-1, *leaves[k].shape)
        at += len(line)
    numbers = iter(range(len(leaves)))
    return jax.tree.map(lambda _: found[next(numbers)], x)


def joined_by_halves(pieces, combine):
    while len(jax.tree.leaves(pieces)[0]) > 1:
        pieces = jax.vmap(combine)(
            *(jax.tree.map(lambda part: part[side::2], pieces) for side in (0, 1))
        )
    return jax.tree.map(lambda part: part[0], pieces)


def merged(x, axis, combine):
    pieces = all_in_one(x, axis)
    return joined_by_halves(pieces, combine)


def split_up(x, dim, size):
    before, after = (x.shape[:dim], x.shape[dim + 1 :])
    return jnp.moveaxis(x.reshape(*before, size, -1, *after), dim, 0)


def sum_at_owner(x, axis, dim):
    size = lax.axis_size(axis)
    parts = lax.all_to_all(split_up(x, dim, size), axis, 0, 0, tiled=True)
    return jnp.sum(parts, axis=0)


def joined_along(parts, dim):
    lengths = list(parts.shape[1:])
    lengths[dim] *= parts.shape[0]
    return jnp.moveaxis(parts, 0, dim).reshape(lengths)


def gathered_copies(x, axis, dim):
    return joined_along(from_everyone(x, axis), dim)


def merge_stats(left_stats, right_stats):
    row_max = jnp.maximum(left_stats[0], right_stats[0])
    row_sum = left_stats[1] * jnp.exp(left_stats[0] - row_max) + right_stats[1] * jnp.exp(
        right_stats[0] - row_max
    )
    return (row_max, row_sum)


def head_scores(queries, key_rows, score_scale):
    return (
        jnp.einsum("qhd,khd->hqk", queries, key_rows, preferred_element_type=jnp.float32)
        * score_scale
    )


def scores_grad(weights, grad_rows, value_rows, row_dot, score_scale):
    grad_probs = jnp.einsum(
        "qhd,khd->hqk", grad_rows, value_rows, preferred_element_type=jnp.float32
    )
    return (weights * (grad_probs - jnp.transpose(row_dot)[:, :, None]) * score_scale).astype(
        jnp.bfloat16
    )


def contract_rows(left_rows, right_rows):
    return jnp.einsum("hqk,qhd->khd", left_rows, right_rows, preferred_element_type=jnp.float32)


def contract_cols(left_rows, right_rows):
    return jnp.einsum("hqk,khd->qhd", left_rows, right_rows, preferred_element_type=jnp.float32)


SEQ_PARTS = ("c", "x", "zh", "y")


GATHER_ORDER = ("zh", "c", "x", "y")


def gather_seq(x, axes):
    x = from_everyone(x, axes)
    x = x.reshape(*[lax.axis_size(axis) for axis in axes], *x.shape[1:])
    stacked = (*axes, *GATHER_ORDER[: 4 - len(axes)][::-1])
    order = [stacked.index(axis) for axis in SEQ_AXES]
    x = jnp.transpose(x, (*order, *range(4, x.ndim)))
    return x.reshape(-1, *x.shape[5:])


MERGE_GROUPS = ("y", ("zh", "x"), "c")


def merged_with_dq(row_max, row_sum, partial_dq):
    rows = partial_dq.shape[0]
    width = partial_dq[0].size
    start = 0
    for axis in MERGE_GROUPS:
        size = lax.axis_size(axis)
        rows //= size
        stats = jnp.stack([row_max, row_sum]).reshape(1, -1)
        send = jnp.concatenate(
            [partial_dq.reshape(size, -1), jnp.broadcast_to(stats, (size, stats.shape[1]))], axis=1
        )
        got = lax.all_to_all(send, axis, 0, 0, tiled=True)
        got_dq = got[:, : rows * width].reshape(size, rows, *partial_dq.shape[1:])
        got_stats = got[:, rows * width :].reshape(size, 2, *row_max.shape)
        top = jnp.max(got_stats[:, 0], axis=0)
        rescale = jnp.exp(got_stats[:, 0] - top)
        row_sum = jnp.sum(got_stats[:, 1] * rescale, axis=0)
        row_max = top
        start = start + lax.axis_index(axis) * rows
        dq_rescale = jnp.transpose(lax.dynamic_slice_in_dim(rescale, start, rows, 2), (0, 2, 1))
        partial_dq = jnp.sum(dq_rescale[..., None] * got_dq, axis=0)
    own_sum = jnp.transpose(lax.dynamic_slice_in_dim(row_sum, start, rows, 1))
    return row_max, row_sum, partial_dq / own_sum[..., None]


def shards(
    cross_q,
    cross_out,
    cross_grad,
    prefix_k,
    prefix_v,
    pad_counts,
    self_q,
    self_k,
    self_v,
    self_grad,
):
    score_scale = HEAD_DIM ** (-0.5)
    own_rows, feature_width = cross_q.shape
    local_heads = feature_width // HEAD_DIM
    tokens = prefix_k.shape[0]
    grad_own = cross_grad.reshape(own_rows, local_heads, HEAD_DIM).astype(jnp.float32)
    out_own = cross_out.reshape(own_rows, local_heads, HEAD_DIM).astype(jnp.float32)
    row_dot = jnp.sum(grad_own * out_own, axis=2).astype(jnp.bfloat16)
    head_groups = lax.axis_size("zl")
    far_pairs = lax.axis_size("zh")
    stacked = jnp.stack([self_q, self_k, self_v, self_grad]).reshape(4, head_groups, feature_width)
    self_chunks = jnp.transpose(stacked, (1, 0, 2)).reshape(head_groups, -1)
    cross_cols = jnp.concatenate((cross_q, cross_grad, row_dot), axis=1)
    cross_width = cross_cols.shape[1]
    self_width = self_chunks.shape[1]
    outgoing = jnp.concatenate(
        (
            self_chunks,
            jnp.broadcast_to(cross_cols.reshape(1, -1), (head_groups, cross_cols.size)),
        ),
        axis=1,
    )
    outgoing = jnp.broadcast_to(outgoing[None], (far_pairs, *outgoing.shape))
    incoming = lax.all_to_all(
        outgoing.reshape(far_pairs * head_groups, -1), ("zh", "zl"), 0, 0, tiled=True
    ).reshape(far_pairs, head_groups, -1)
    block_rows = head_groups
    self_cols = incoming[:, :, :self_width]
    far_cross = lax.dynamic_index_in_dim(incoming, lax.axis_index("zl"), 1, keepdims=False)
    far_cross = far_cross[:, self_width:].reshape(far_pairs, own_rows, cross_width)
    first = jnp.concatenate((far_cross, self_cols), axis=2)
    first = from_everyone(first, "c")
    core = lax.axis_index("c")
    self_heads = first[..., cross_width:].reshape(*first.shape[:-1], 4, local_heads, HEAD_DIM)
    self_mine = lax.dynamic_index_in_dim(self_heads, core, axis=4, keepdims=False)
    rest = jnp.concatenate(
        (first[..., :cross_width], self_mine.reshape(*first.shape[:-1], -1)), axis=-1
    )
    gathered = gather_seq(rest, GATHER_ORDER[2:][::-1])
    query_all = gathered[:, : cross_q.shape[1]]
    grad_all = gathered[:, cross_q.shape[1] : 2 * cross_q.shape[1]]
    dots_all = gathered[:, 2 * cross_q.shape[1] : cross_width]
    self_all = gathered[:, cross_width:]
    latents = query_all.shape[0]
    query_heads = query_all.reshape(latents, local_heads, HEAD_DIM)
    grad_heads = grad_all.reshape(latents, local_heads, HEAD_DIM)
    key_heads = prefix_k.reshape(tokens, local_heads, HEAD_DIM)
    value_heads = prefix_v.reshape(tokens, local_heads, HEAD_DIM)
    valid_keys = jnp.arange(tokens) < tokens - pad_counts[0]
    scores = head_scores(query_heads, key_heads, score_scale)
    scores = jnp.where(valid_keys[None, None, :], scores, -jnp.inf)
    row_max = jnp.max(scores, axis=2)
    shifted = jnp.exp(scores - row_max[:, :, None])
    row_sum = jnp.sum(shifted, axis=2)
    row_dots = dots_all.astype(jnp.float32)
    grad_probs = jnp.einsum(
        "qhd,khd->hqk", grad_heads, value_heads, preferred_element_type=jnp.float32
    )
    local_gs = shifted * (grad_probs - jnp.transpose(row_dots)[:, :, None]) * score_scale
    local_dq = jnp.einsum(
        "hqk,khd->qhd",
        local_gs,
        key_heads.astype(jnp.float32),
        precision=lax.Precision.HIGHEST,
        preferred_element_type=jnp.float32,
    )
    row_maxes, row_sums, own_dq = merged_with_dq(row_max, row_sum, local_dq)
    log_total = row_maxes + jnp.log(row_sums)
    weights = jnp.exp(scores - log_total[:, :, None])
    prefix_dv = (
        contract_rows(weights.astype(jnp.bfloat16), grad_heads)
        .reshape(tokens, feature_width)
        .astype(jnp.bfloat16)
    )
    grad_scores = scores_grad(weights, grad_heads, value_heads, row_dots, score_scale)
    prefix_dk = (
        contract_rows(grad_scores, query_heads).reshape(tokens, feature_width).astype(jnp.bfloat16)
    )
    cross_dq = own_dq.reshape(own_rows, feature_width).astype(jnp.bfloat16)
    everything = jnp.transpose(self_all.reshape(latents, 4, HEAD_DIM), (1, 0, 2))
    all_rows = everything.shape[1]
    query_every = everything[0].reshape(all_rows, 1, HEAD_DIM)
    key_every = everything[1].reshape(all_rows, 1, HEAD_DIM)
    value_every = everything[2].reshape(all_rows, 1, HEAD_DIM)
    grad_every = everything[3].reshape(all_rows, 1, HEAD_DIM)
    row_ids = jnp.arange(all_rows)
    causal_full = row_ids[:, None] >= row_ids[None, :]
    full_scores = head_scores(query_every, key_every, score_scale)
    full_scores = jnp.where(causal_full[None, :, :], full_scores, -jnp.inf)
    full_lse = jax.nn.logsumexp(full_scores, axis=2)
    full_weights = jnp.exp(full_scores - full_lse[:, :, None])
    full_half = full_weights.astype(jnp.bfloat16)
    full_out = contract_cols(full_half, value_every)
    full_dot = jnp.sum(grad_every.astype(jnp.float32) * full_out, axis=2)
    full_gs = scores_grad(full_weights, grad_every, value_every, full_dot, score_scale)
    cores = lax.axis_size("c")
    chip_rows = block_rows * cores
    chip_start = (lax.axis_index(SEQ_AXES) - core) * block_rows
    query_part = lax.dynamic_slice_in_dim(full_gs, chip_start, chip_rows, 1)
    key_part = lax.dynamic_slice_in_dim(full_gs, chip_start, chip_rows, 2)
    half_part = lax.dynamic_slice_in_dim(full_half, chip_start, chip_rows, 2)
    head_results = jnp.stack(
        [
            contract_cols(query_part, key_every),
            contract_rows(key_part, query_every),
            contract_rows(half_part, grad_every),
        ]
    ).astype(jnp.bfloat16)
    both = lax.all_gather(head_results.reshape(3, chip_rows, HEAD_DIM), "c", axis=0)
    mine = lax.dynamic_slice_in_dim(both, core * block_rows, block_rows, 2)
    mine = jnp.transpose(mine, (1, 2, 0, 3)).reshape(3, block_rows, feature_width)
    self_dq, self_dk, self_dv = mine[0], mine[1], mine[2]
    return (cross_dq, prefix_dk, prefix_dv, self_dq, self_dk, self_dv)


SEQ_AXES = ("y", "zh", "x", "c")


def solution(mesh):
    sizes = dict(mesh.shape)
    split = mesh.devices.reshape(4, 2, 4, 2, sizes["head"])
    mesh = jax.sharding.Mesh(split, (*SEQ_AXES, "zl"))
    in_specs = (
        P(SEQ_AXES, "zl"),
        P(SEQ_AXES, "zl"),
        P(SEQ_AXES, "zl"),
        P(SEQ_AXES, "zl"),
        P(SEQ_AXES, "zl"),
        P(SEQ_AXES),
        P((*SEQ_AXES, "zl"), None),
        P((*SEQ_AXES, "zl"), None),
        P((*SEQ_AXES, "zl"), None),
        P((*SEQ_AXES, "zl"), None),
    )
    out_specs = (
        P(SEQ_AXES, "zl"),
        P(SEQ_AXES, "zl"),
        P(SEQ_AXES, "zl"),
        P(SEQ_AXES, "zl"),
        P(SEQ_AXES, "zl"),
        P(SEQ_AXES, "zl"),
    )
    return jax.shard_map(shards, mesh=mesh, in_specs=in_specs, out_specs=out_specs, check_vma=False)
```

```python
import jax
import jax.numpy as jnp
from jax import lax
from jax.sharding import PartitionSpec as P

HEAD_DIM = 128


def in_one_piece(arrays, axis, dim, along):
    ends, at = ([], 0)
    for a in arrays[:-1]:
        at += a.shape[along]
        ends.append(at)
    both = jnp.concatenate(arrays, axis=along)
    return tuple(jnp.split(lax.all_gather(both, axis, axis=dim, tiled=True), ends, axis=along))


def from_everyone(x, axis):
    copies = jnp.broadcast_to(x, (lax.axis_size(axis), *x.shape))
    return lax.all_to_all(copies, axis, split_axis=0, concat_axis=0, tiled=True)


def all_in_one(x, axis):
    leaves = jax.tree.leaves(x)
    order = sorted(range(len(leaves)), key=lambda k: -leaves[k].size)
    width = (1, *leaves[order[0]].shape)[-1]
    lines = [
        jnp.pad(leaves[k].reshape(-1), (0, -leaves[k].size % width)).reshape(-1, width)
        for k in order
    ]
    both, at, found = (from_everyone(jnp.concatenate(lines), axis), 0, {})
    for k, line in zip(order, lines):
        section = both[:, at : at + len(line)].reshape(len(both), -1)
        found[k] = section[:, : leaves[k].size].reshape(-1, *leaves[k].shape)
        at += len(line)
    numbers = iter(range(len(leaves)))
    return jax.tree.map(lambda _: found[next(numbers)], x)


def joined_by_halves(pieces, combine):
    while len(jax.tree.leaves(pieces)[0]) > 1:
        pieces = jax.vmap(combine)(
            *(jax.tree.map(lambda part: part[side::2], pieces) for side in (0, 1))
        )
    return jax.tree.map(lambda part: part[0], pieces)


def merged(x, axis, combine):
    pieces = all_in_one(x, axis)
    return joined_by_halves(pieces, combine)


def split_up(x, dim, size):
    before, after = (x.shape[:dim], x.shape[dim + 1 :])
    return jnp.moveaxis(x.reshape(*before, size, -1, *after), dim, 0)


def sum_at_owner(x, axis, dim):
    size = lax.axis_size(axis)
    parts = lax.all_to_all(split_up(x, dim, size), axis, 0, 0, tiled=True)
    return jnp.sum(parts, axis=0)


def joined_along(parts, dim):
    lengths = list(parts.shape[1:])
    lengths[dim] *= parts.shape[0]
    return jnp.moveaxis(parts, 0, dim).reshape(lengths)


def gathered_copies(x, axis, dim):
    return joined_along(from_everyone(x, axis), dim)


def merge_stats(left_stats, right_stats):
    row_max = jnp.maximum(left_stats[0], right_stats[0])
    row_sum = left_stats[1] * jnp.exp(left_stats[0] - row_max) + right_stats[1] * jnp.exp(
        right_stats[0] - row_max
    )
    return (row_max, row_sum)


def head_scores(queries, key_rows, score_scale):
    return (
        jnp.einsum("qhd,khd->hqk", queries, key_rows, preferred_element_type=jnp.float32)
        * score_scale
    )


def scores_grad(weights, grad_rows, value_rows, row_dot, score_scale):
    grad_probs = jnp.einsum(
        "qhd,khd->hqk", grad_rows, value_rows, preferred_element_type=jnp.float32
    )
    return (weights * (grad_probs - jnp.transpose(row_dot)[:, :, None]) * score_scale).astype(
        jnp.bfloat16
    )


def contract_rows(left_rows, right_rows):
    return jnp.einsum("hqk,qhd->khd", left_rows, right_rows, preferred_element_type=jnp.float32)


def contract_cols(left_rows, right_rows):
    return jnp.einsum("hqk,khd->qhd", left_rows, right_rows, preferred_element_type=jnp.float32)


SEQ_PARTS = ("c", "x", "zh", "y")


GATHER_ORDER = ("zh", "c", "x", "y")


def gather_seq(x, axes):
    x = from_everyone(x, axes)
    x = x.reshape(*[lax.axis_size(axis) for axis in axes], *x.shape[1:])
    stacked = (*axes, *GATHER_ORDER[: 4 - len(axes)][::-1])
    order = [stacked.index(axis) for axis in SEQ_AXES]
    x = jnp.transpose(x, (*order, *range(4, x.ndim)))
    return x.reshape(-1, *x.shape[5:])


MERGE_GROUPS = ("y", ("zh", "x", "c"))


def merged_with_dq(row_max, row_sum, partial_dq):
    rows = partial_dq.shape[0]
    width = partial_dq[0].size
    start = 0
    for axis in MERGE_GROUPS:
        size = lax.axis_size(axis)
        rows //= size
        stats = jnp.stack([row_max, row_sum]).reshape(1, -1)
        send = jnp.concatenate(
            [partial_dq.reshape(size, -1), jnp.broadcast_to(stats, (size, stats.shape[1]))], axis=1
        )
        got = lax.all_to_all(send, axis, 0, 0, tiled=True)
        got_dq = got[:, : rows * width].reshape(size, rows, *partial_dq.shape[1:])
        got_stats = got[:, rows * width :].reshape(size, 2, *row_max.shape)
        top = jnp.max(got_stats[:, 0], axis=0)
        rescale = jnp.exp(got_stats[:, 0] - top)
        row_sum = jnp.sum(got_stats[:, 1] * rescale, axis=0)
        row_max = top
        start = start + lax.axis_index(axis) * rows
        dq_rescale = jnp.transpose(lax.dynamic_slice_in_dim(rescale, start, rows, 2), (0, 2, 1))
        partial_dq = jnp.sum(dq_rescale[..., None] * got_dq, axis=0)
    own_sum = jnp.transpose(lax.dynamic_slice_in_dim(row_sum, start, rows, 1))
    return row_max, row_sum, partial_dq / own_sum[..., None]


def shards(
    cross_q,
    cross_out,
    cross_grad,
    prefix_k,
    prefix_v,
    pad_counts,
    self_q,
    self_k,
    self_v,
    self_grad,
):
    score_scale = HEAD_DIM ** (-0.5)
    own_rows, feature_width = cross_q.shape
    local_heads = feature_width // HEAD_DIM
    tokens = prefix_k.shape[0]
    grad_own = cross_grad.reshape(own_rows, local_heads, HEAD_DIM).astype(jnp.float32)
    out_own = cross_out.reshape(own_rows, local_heads, HEAD_DIM).astype(jnp.float32)
    row_dot = jnp.sum(grad_own * out_own, axis=2).astype(jnp.bfloat16)
    head_groups = lax.axis_size("zl")
    far_pairs = lax.axis_size("zh")
    stacked = jnp.stack([self_q, self_k, self_v, self_grad]).reshape(4, head_groups, feature_width)
    self_chunks = jnp.transpose(stacked, (1, 0, 2)).reshape(head_groups, -1)
    cross_cols = jnp.concatenate((cross_q, cross_grad, row_dot), axis=1)
    cross_width = cross_cols.shape[1]
    self_width = self_chunks.shape[1]
    outgoing = jnp.concatenate(
        (
            self_chunks,
            jnp.broadcast_to(cross_cols.reshape(1, -1), (head_groups, cross_cols.size)),
        ),
        axis=1,
    )
    outgoing = jnp.broadcast_to(outgoing[None], (far_pairs, *outgoing.shape))
    incoming = lax.all_to_all(
        outgoing.reshape(far_pairs * head_groups, -1), ("zh", "zl"), 0, 0, tiled=True
    ).reshape(far_pairs, head_groups, -1)
    block_rows = head_groups
    self_cols = incoming[:, :, :self_width]
    far_cross = lax.dynamic_index_in_dim(incoming, lax.axis_index("zl"), 1, keepdims=False)
    far_cross = far_cross[:, self_width:].reshape(far_pairs, own_rows, cross_width)
    first = jnp.concatenate((far_cross, self_cols), axis=2)
    first = from_everyone(first, "c")
    core = lax.axis_index("c")
    self_heads = first[..., cross_width:].reshape(*first.shape[:-1], 4, local_heads, HEAD_DIM)
    self_mine = lax.dynamic_index_in_dim(self_heads, core, axis=4, keepdims=False)
    rest = jnp.concatenate(
        (first[..., :cross_width], self_mine.reshape(*first.shape[:-1], -1)), axis=-1
    )
    gathered = gather_seq(rest, GATHER_ORDER[2:][::-1])
    query_all = gathered[:, : cross_q.shape[1]]
    grad_all = gathered[:, cross_q.shape[1] : 2 * cross_q.shape[1]]
    dots_all = gathered[:, 2 * cross_q.shape[1] : cross_width]
    self_all = gathered[:, cross_width:]
    latents = query_all.shape[0]
    query_heads = query_all.reshape(latents, local_heads, HEAD_DIM)
    grad_heads = grad_all.reshape(latents, local_heads, HEAD_DIM)
    key_heads = prefix_k.reshape(tokens, local_heads, HEAD_DIM)
    value_heads = prefix_v.reshape(tokens, local_heads, HEAD_DIM)
    valid_keys = jnp.arange(tokens) < tokens - pad_counts[0]
    scores = head_scores(query_heads, key_heads, score_scale)
    scores = jnp.where(valid_keys[None, None, :], scores, -jnp.inf)
    row_max = jnp.max(scores, axis=2)
    shifted = jnp.exp(scores - row_max[:, :, None])
    row_sum = jnp.sum(shifted, axis=2)
    row_dots = dots_all.astype(jnp.float32)
    grad_probs = jnp.einsum(
        "qhd,khd->hqk", grad_heads, value_heads, preferred_element_type=jnp.float32
    )
    local_gs = shifted * (grad_probs - jnp.transpose(row_dots)[:, :, None]) * score_scale
    local_dq = jnp.einsum(
        "hqk,khd->qhd",
        local_gs,
        key_heads.astype(jnp.float32),
        precision=lax.Precision.HIGHEST,
        preferred_element_type=jnp.float32,
    )
    row_maxes, row_sums, own_dq = merged_with_dq(row_max, row_sum, local_dq)
    log_total = row_maxes + jnp.log(row_sums)
    weights = jnp.exp(scores - log_total[:, :, None])
    prefix_dv = (
        contract_rows(weights.astype(jnp.bfloat16), grad_heads)
        .reshape(tokens, feature_width)
        .astype(jnp.bfloat16)
    )
    grad_scores = scores_grad(weights, grad_heads, value_heads, row_dots, score_scale)
    prefix_dk = (
        contract_rows(grad_scores, query_heads).reshape(tokens, feature_width).astype(jnp.bfloat16)
    )
    cross_dq = own_dq.reshape(own_rows, feature_width).astype(jnp.bfloat16)
    everything = jnp.transpose(self_all.reshape(latents, 4, HEAD_DIM), (1, 0, 2))
    all_rows = everything.shape[1]
    query_every = everything[0].reshape(all_rows, 1, HEAD_DIM)
    key_every = everything[1].reshape(all_rows, 1, HEAD_DIM)
    value_every = everything[2].reshape(all_rows, 1, HEAD_DIM)
    grad_every = everything[3].reshape(all_rows, 1, HEAD_DIM)
    row_ids = jnp.arange(all_rows)
    causal_full = row_ids[:, None] >= row_ids[None, :]
    full_scores = head_scores(query_every, key_every, score_scale)
    full_scores = jnp.where(causal_full[None, :, :], full_scores, -jnp.inf)
    full_lse = jax.nn.logsumexp(full_scores, axis=2)
    full_weights = jnp.exp(full_scores - full_lse[:, :, None])
    full_half = full_weights.astype(jnp.bfloat16)
    full_out = contract_cols(full_half, value_every)
    full_dot = jnp.sum(grad_every.astype(jnp.float32) * full_out, axis=2)
    full_gs = scores_grad(full_weights, grad_every, value_every, full_dot, score_scale)
    cores = lax.axis_size("c")
    chip_rows = block_rows * cores
    chip_start = (lax.axis_index(SEQ_AXES) - core) * block_rows
    query_part = lax.dynamic_slice_in_dim(full_gs, chip_start, chip_rows, 1)
    key_part = lax.dynamic_slice_in_dim(full_gs, chip_start, chip_rows, 2)
    half_part = lax.dynamic_slice_in_dim(full_half, chip_start, chip_rows, 2)
    head_results = jnp.stack(
        [
            contract_cols(query_part, key_every),
            contract_rows(key_part, query_every),
            contract_rows(half_part, grad_every),
        ]
    ).astype(jnp.bfloat16)
    both = lax.all_gather(head_results.reshape(3, chip_rows, HEAD_DIM), "c", axis=0)
    mine = lax.dynamic_slice_in_dim(both, core * block_rows, block_rows, 2)
    mine = jnp.transpose(mine, (1, 2, 0, 3)).reshape(3, block_rows, feature_width)
    self_dq, self_dk, self_dv = mine[0], mine[1], mine[2]
    return (cross_dq, prefix_dk, prefix_dv, self_dq, self_dk, self_dv)


SEQ_AXES = ("y", "zh", "x", "c")


def solution(mesh):
    sizes = dict(mesh.shape)
    split = mesh.devices.reshape(4, 2, 4, 2, sizes["head"])
    mesh = jax.sharding.Mesh(split, (*SEQ_AXES, "zl"))
    in_specs = (
        P(SEQ_AXES, "zl"),
        P(SEQ_AXES, "zl"),
        P(SEQ_AXES, "zl"),
        P(SEQ_AXES, "zl"),
        P(SEQ_AXES, "zl"),
        P(SEQ_AXES),
        P((*SEQ_AXES, "zl"), None),
        P((*SEQ_AXES, "zl"), None),
        P((*SEQ_AXES, "zl"), None),
        P((*SEQ_AXES, "zl"), None),
    )
    out_specs = (
        P(SEQ_AXES, "zl"),
        P(SEQ_AXES, "zl"),
        P(SEQ_AXES, "zl"),
        P(SEQ_AXES, "zl"),
        P(SEQ_AXES, "zl"),
        P(SEQ_AXES, "zl"),
    )
    return jax.shard_map(shards, mesh=mesh, in_specs=in_specs, out_specs=out_specs, check_vma=False)
```

```python
import jax
import jax.numpy as jnp
from jax import lax
from jax.sharding import PartitionSpec as P

HEAD_DIM = 128


def in_one_piece(arrays, axis, dim, along):
    ends, at = ([], 0)
    for a in arrays[:-1]:
        at += a.shape[along]
        ends.append(at)
    both = jnp.concatenate(arrays, axis=along)
    return tuple(jnp.split(lax.all_gather(both, axis, axis=dim, tiled=True), ends, axis=along))


def from_everyone(x, axis):
    copies = jnp.broadcast_to(x, (lax.axis_size(axis), *x.shape))
    return lax.all_to_all(copies, axis, split_axis=0, concat_axis=0, tiled=True)


def all_in_one(x, axis):
    leaves = jax.tree.leaves(x)
    order = sorted(range(len(leaves)), key=lambda k: -leaves[k].size)
    width = (1, *leaves[order[0]].shape)[-1]
    lines = [
        jnp.pad(leaves[k].reshape(-1), (0, -leaves[k].size % width)).reshape(-1, width)
        for k in order
    ]
    both, at, found = (from_everyone(jnp.concatenate(lines), axis), 0, {})
    for k, line in zip(order, lines):
        section = both[:, at : at + len(line)].reshape(len(both), -1)
        found[k] = section[:, : leaves[k].size].reshape(-1, *leaves[k].shape)
        at += len(line)
    numbers = iter(range(len(leaves)))
    return jax.tree.map(lambda _: found[next(numbers)], x)


def joined_by_halves(pieces, combine):
    while len(jax.tree.leaves(pieces)[0]) > 1:
        pieces = jax.vmap(combine)(
            *(jax.tree.map(lambda part: part[side::2], pieces) for side in (0, 1))
        )
    return jax.tree.map(lambda part: part[0], pieces)


def merged(x, axis, combine):
    pieces = all_in_one(x, axis)
    return joined_by_halves(pieces, combine)


def split_up(x, dim, size):
    before, after = (x.shape[:dim], x.shape[dim + 1 :])
    return jnp.moveaxis(x.reshape(*before, size, -1, *after), dim, 0)


def sum_at_owner(x, axis, dim):
    size = lax.axis_size(axis)
    parts = lax.all_to_all(split_up(x, dim, size), axis, 0, 0, tiled=True)
    return jnp.sum(parts, axis=0)


def joined_along(parts, dim):
    lengths = list(parts.shape[1:])
    lengths[dim] *= parts.shape[0]
    return jnp.moveaxis(parts, 0, dim).reshape(lengths)


def gathered_copies(x, axis, dim):
    return joined_along(from_everyone(x, axis), dim)


def merge_stats(left_stats, right_stats):
    row_max = jnp.maximum(left_stats[0], right_stats[0])
    row_sum = left_stats[1] * jnp.exp(left_stats[0] - row_max) + right_stats[1] * jnp.exp(
        right_stats[0] - row_max
    )
    return (row_max, row_sum)


def head_scores(queries, key_rows, score_scale):
    return (
        jnp.einsum("qhd,khd->hqk", queries, key_rows, preferred_element_type=jnp.float32)
        * score_scale
    )


def scores_grad(weights, grad_rows, value_rows, row_dot, score_scale):
    grad_probs = jnp.einsum(
        "qhd,khd->hqk", grad_rows, value_rows, preferred_element_type=jnp.float32
    )
    return (weights * (grad_probs - jnp.transpose(row_dot)[:, :, None]) * score_scale).astype(
        jnp.bfloat16
    )


def contract_rows(left_rows, right_rows):
    return jnp.einsum("hqk,qhd->khd", left_rows, right_rows, preferred_element_type=jnp.float32)


def contract_cols(left_rows, right_rows):
    return jnp.einsum("hqk,khd->qhd", left_rows, right_rows, preferred_element_type=jnp.float32)


SEQ_PARTS = ("c", "x", "zh", "y")


GATHER_ORDER = ("zh", "c", "x", "y")


def gather_seq(x, axes):
    x = from_everyone(x, axes)
    x = x.reshape(*[lax.axis_size(axis) for axis in axes], *x.shape[1:])
    stacked = (*axes, *GATHER_ORDER[: 4 - len(axes)][::-1])
    order = [stacked.index(axis) for axis in SEQ_AXES]
    x = jnp.transpose(x, (*order, *range(4, x.ndim)))
    return x.reshape(-1, *x.shape[5:])


MERGE_GROUPS = ("y", ("zh", "x"), "c")


def merged_with_dq(row_max, row_sum, partial_dq, extra):
    rows = partial_dq.shape[0]
    width = partial_dq[0].size
    start = 0
    for axis in MERGE_GROUPS:
        size = lax.axis_size(axis)
        rows //= size
        stats = jnp.stack([row_max, row_sum]).reshape(1, -1)
        if axis == MERGE_GROUPS[-1]:
            stats = jnp.concatenate([stats, extra.reshape(1, -1)], axis=1)
        send = jnp.concatenate(
            [partial_dq.reshape(size, -1), jnp.broadcast_to(stats, (size, stats.shape[1]))], axis=1
        )
        got = lax.all_to_all(send, axis, 0, 0, tiled=True)
        if axis == MERGE_GROUPS[-1]:
            got_extra = got[:, send.shape[1] - extra.size :]
            got = got[:, : send.shape[1] - extra.size]
        got_dq = got[:, : rows * width].reshape(size, rows, *partial_dq.shape[1:])
        got_stats = got[:, rows * width :].reshape(size, 2, *row_max.shape)
        top = jnp.max(got_stats[:, 0], axis=0)
        rescale = jnp.exp(got_stats[:, 0] - top)
        row_sum = jnp.sum(got_stats[:, 1] * rescale, axis=0)
        row_max = top
        start = start + lax.axis_index(axis) * rows
        dq_rescale = jnp.transpose(lax.dynamic_slice_in_dim(rescale, start, rows, 2), (0, 2, 1))
        partial_dq = jnp.sum(dq_rescale[..., None] * got_dq, axis=0)
    own_sum = jnp.transpose(lax.dynamic_slice_in_dim(row_sum, start, rows, 1))
    return row_max, row_sum, partial_dq / own_sum[..., None], got_extra


def shards(
    cross_q,
    cross_out,
    cross_grad,
    prefix_k,
    prefix_v,
    pad_counts,
    self_q,
    self_k,
    self_v,
    self_grad,
):
    score_scale = HEAD_DIM ** (-0.5)
    own_rows, feature_width = cross_q.shape
    local_heads = feature_width // HEAD_DIM
    tokens = prefix_k.shape[0]
    grad_own = cross_grad.reshape(own_rows, local_heads, HEAD_DIM).astype(jnp.float32)
    out_own = cross_out.reshape(own_rows, local_heads, HEAD_DIM).astype(jnp.float32)
    row_dot = jnp.sum(grad_own * out_own, axis=2).astype(jnp.bfloat16)
    head_groups = lax.axis_size("zl")
    far_pairs = lax.axis_size("zh")
    stacked = jnp.stack([self_q, self_k, self_v, self_grad]).reshape(4, head_groups, feature_width)
    self_chunks = jnp.transpose(stacked, (1, 0, 2)).reshape(head_groups, -1)
    cross_cols = jnp.concatenate((cross_q, cross_grad, row_dot), axis=1)
    cross_width = cross_cols.shape[1]
    self_width = self_chunks.shape[1]
    outgoing = jnp.concatenate(
        (
            self_chunks,
            jnp.broadcast_to(cross_cols.reshape(1, -1), (head_groups, cross_cols.size)),
        ),
        axis=1,
    )
    outgoing = jnp.broadcast_to(outgoing[None], (far_pairs, *outgoing.shape))
    incoming = lax.all_to_all(
        outgoing.reshape(far_pairs * head_groups, -1), ("zh", "zl"), 0, 0, tiled=True
    ).reshape(far_pairs, head_groups, -1)
    block_rows = head_groups
    self_cols = incoming[:, :, :self_width]
    far_cross = lax.dynamic_index_in_dim(incoming, lax.axis_index("zl"), 1, keepdims=False)
    far_cross = far_cross[:, self_width:].reshape(far_pairs, own_rows, cross_width)
    first = jnp.concatenate((far_cross, self_cols), axis=2)
    first = from_everyone(first, "c")
    core = lax.axis_index("c")
    self_heads = first[..., cross_width:].reshape(*first.shape[:-1], 4, local_heads, HEAD_DIM)
    self_mine = lax.dynamic_index_in_dim(self_heads, core, axis=4, keepdims=False)
    rest = jnp.concatenate(
        (first[..., :cross_width], self_mine.reshape(*first.shape[:-1], -1)), axis=-1
    )
    gathered = gather_seq(rest, GATHER_ORDER[2:][::-1])
    query_all = gathered[:, : cross_q.shape[1]]
    grad_all = gathered[:, cross_q.shape[1] : 2 * cross_q.shape[1]]
    dots_all = gathered[:, 2 * cross_q.shape[1] : cross_width]
    self_all = gathered[:, cross_width:]
    latents = query_all.shape[0]
    query_heads = query_all.reshape(latents, local_heads, HEAD_DIM)
    grad_heads = grad_all.reshape(latents, local_heads, HEAD_DIM)
    key_heads = prefix_k.reshape(tokens, local_heads, HEAD_DIM)
    value_heads = prefix_v.reshape(tokens, local_heads, HEAD_DIM)
    valid_keys = jnp.arange(tokens) < tokens - pad_counts[0]
    scores = head_scores(query_heads, key_heads, score_scale)
    scores = jnp.where(valid_keys[None, None, :], scores, -jnp.inf)
    row_max = jnp.max(scores, axis=2)
    shifted = jnp.exp(scores - row_max[:, :, None])
    row_sum = jnp.sum(shifted, axis=2)
    row_dots = dots_all.astype(jnp.float32)
    grad_probs = jnp.einsum(
        "qhd,khd->hqk", grad_heads, value_heads, preferred_element_type=jnp.float32
    )
    local_gs = shifted * (grad_probs - jnp.transpose(row_dots)[:, :, None]) * score_scale
    local_dq = jnp.einsum(
        "hqk,khd->qhd",
        local_gs,
        key_heads.astype(jnp.float32),
        precision=lax.Precision.HIGHEST,
        preferred_element_type=jnp.float32,
    )
    everything = jnp.transpose(self_all.reshape(latents, 4, HEAD_DIM), (1, 0, 2))
    all_rows = everything.shape[1]
    query_every = everything[0].reshape(all_rows, 1, HEAD_DIM)
    key_every = everything[1].reshape(all_rows, 1, HEAD_DIM)
    value_every = everything[2].reshape(all_rows, 1, HEAD_DIM)
    grad_every = everything[3].reshape(all_rows, 1, HEAD_DIM)
    row_ids = jnp.arange(all_rows)
    causal_full = row_ids[:, None] >= row_ids[None, :]
    full_scores = head_scores(query_every, key_every, score_scale)
    full_scores = jnp.where(causal_full[None, :, :], full_scores, -jnp.inf)
    full_lse = jax.nn.logsumexp(full_scores, axis=2)
    full_weights = jnp.exp(full_scores - full_lse[:, :, None])
    full_half = full_weights.astype(jnp.bfloat16)
    full_out = contract_cols(full_half, value_every)
    full_dot = jnp.sum(grad_every.astype(jnp.float32) * full_out, axis=2)
    full_gs = scores_grad(full_weights, grad_every, value_every, full_dot, score_scale)
    cores = lax.axis_size("c")
    chip_rows = block_rows * cores
    chip_start = (lax.axis_index(SEQ_AXES) - core) * block_rows
    query_part = lax.dynamic_slice_in_dim(full_gs, chip_start, chip_rows, 1)
    key_part = lax.dynamic_slice_in_dim(full_gs, chip_start, chip_rows, 2)
    half_part = lax.dynamic_slice_in_dim(full_half, chip_start, chip_rows, 2)
    head_results = jnp.stack(
        [
            contract_cols(query_part, key_every),
            contract_rows(key_part, query_every),
            contract_rows(half_part, grad_every),
        ]
    ).astype(jnp.bfloat16)
    self_extra = head_results.astype(jnp.float32).reshape(-1)
    row_maxes, row_sums, own_dq, got_extra = merged_with_dq(row_max, row_sum, local_dq, self_extra)
    both = got_extra.astype(jnp.bfloat16).reshape(cores, 3, chip_rows, HEAD_DIM)
    mine = lax.dynamic_slice_in_dim(both, core * block_rows, block_rows, 2)
    mine = jnp.transpose(mine, (1, 2, 0, 3)).reshape(3, block_rows, feature_width)
    self_dq, self_dk, self_dv = mine[0], mine[1], mine[2]
    log_total = row_maxes + jnp.log(row_sums)
    weights = jnp.exp(scores - log_total[:, :, None])
    prefix_dv = (
        contract_rows(weights.astype(jnp.bfloat16), grad_heads)
        .reshape(tokens, feature_width)
        .astype(jnp.bfloat16)
    )
    grad_scores = scores_grad(weights, grad_heads, value_heads, row_dots, score_scale)
    prefix_dk = (
        contract_rows(grad_scores, query_heads).reshape(tokens, feature_width).astype(jnp.bfloat16)
    )
    cross_dq = own_dq.reshape(own_rows, feature_width).astype(jnp.bfloat16)
    return (cross_dq, prefix_dk, prefix_dv, self_dq, self_dk, self_dv)


SEQ_AXES = ("y", "zh", "x", "c")


def solution(mesh):
    sizes = dict(mesh.shape)
    split = mesh.devices.reshape(4, 2, 4, 2, sizes["head"])
    mesh = jax.sharding.Mesh(split, (*SEQ_AXES, "zl"))
    in_specs = (
        P(SEQ_AXES, "zl"),
        P(SEQ_AXES, "zl"),
        P(SEQ_AXES, "zl"),
        P(SEQ_AXES, "zl"),
        P(SEQ_AXES, "zl"),
        P(SEQ_AXES),
        P((*SEQ_AXES, "zl"), None),
        P((*SEQ_AXES, "zl"), None),
        P((*SEQ_AXES, "zl"), None),
        P((*SEQ_AXES, "zl"), None),
    )
    out_specs = (
        P(SEQ_AXES, "zl"),
        P(SEQ_AXES, "zl"),
        P(SEQ_AXES, "zl"),
        P(SEQ_AXES, "zl"),
        P(SEQ_AXES, "zl"),
        P(SEQ_AXES, "zl"),
    )
    return jax.shard_map(shards, mesh=mesh, in_specs=in_specs, out_specs=out_specs, check_vma=False)
```

```python
import jax
import jax.numpy as jnp
from jax import lax
from jax.sharding import PartitionSpec as P

HEAD_DIM = 128


def in_one_piece(arrays, axis, dim, along):
    ends, at = ([], 0)
    for a in arrays[:-1]:
        at += a.shape[along]
        ends.append(at)
    both = jnp.concatenate(arrays, axis=along)
    return tuple(jnp.split(lax.all_gather(both, axis, axis=dim, tiled=True), ends, axis=along))


def from_everyone(x, axis):
    copies = jnp.broadcast_to(x, (lax.axis_size(axis), *x.shape))
    return lax.all_to_all(copies, axis, split_axis=0, concat_axis=0, tiled=True)


def all_in_one(x, axis):
    leaves = jax.tree.leaves(x)
    order = sorted(range(len(leaves)), key=lambda k: -leaves[k].size)
    width = (1, *leaves[order[0]].shape)[-1]
    lines = [
        jnp.pad(leaves[k].reshape(-1), (0, -leaves[k].size % width)).reshape(-1, width)
        for k in order
    ]
    both, at, found = (from_everyone(jnp.concatenate(lines), axis), 0, {})
    for k, line in zip(order, lines):
        section = both[:, at : at + len(line)].reshape(len(both), -1)
        found[k] = section[:, : leaves[k].size].reshape(-1, *leaves[k].shape)
        at += len(line)
    numbers = iter(range(len(leaves)))
    return jax.tree.map(lambda _: found[next(numbers)], x)


def joined_by_halves(pieces, combine):
    while len(jax.tree.leaves(pieces)[0]) > 1:
        pieces = jax.vmap(combine)(
            *(jax.tree.map(lambda part: part[side::2], pieces) for side in (0, 1))
        )
    return jax.tree.map(lambda part: part[0], pieces)


def merged(x, axis, combine):
    pieces = all_in_one(x, axis)
    return joined_by_halves(pieces, combine)


def split_up(x, dim, size):
    before, after = (x.shape[:dim], x.shape[dim + 1 :])
    return jnp.moveaxis(x.reshape(*before, size, -1, *after), dim, 0)


def sum_at_owner(x, axis, dim):
    size = lax.axis_size(axis)
    parts = lax.all_to_all(split_up(x, dim, size), axis, 0, 0, tiled=True)
    return jnp.sum(parts, axis=0)


def joined_along(parts, dim):
    lengths = list(parts.shape[1:])
    lengths[dim] *= parts.shape[0]
    return jnp.moveaxis(parts, 0, dim).reshape(lengths)


def gathered_copies(x, axis, dim):
    return joined_along(from_everyone(x, axis), dim)


def merge_stats(left_stats, right_stats):
    row_max = jnp.maximum(left_stats[0], right_stats[0])
    row_sum = left_stats[1] * jnp.exp(left_stats[0] - row_max) + right_stats[1] * jnp.exp(
        right_stats[0] - row_max
    )
    return (row_max, row_sum)


def head_scores(queries, key_rows, score_scale):
    return (
        jnp.einsum("qhd,khd->hqk", queries, key_rows, preferred_element_type=jnp.float32)
        * score_scale
    )


def scores_grad(weights, grad_rows, value_rows, row_dot, score_scale):
    grad_probs = jnp.einsum(
        "qhd,khd->hqk", grad_rows, value_rows, preferred_element_type=jnp.float32
    )
    return (weights * (grad_probs - jnp.transpose(row_dot)[:, :, None]) * score_scale).astype(
        jnp.bfloat16
    )


def contract_rows(left_rows, right_rows):
    return jnp.einsum("hqk,qhd->khd", left_rows, right_rows, preferred_element_type=jnp.float32)


def contract_cols(left_rows, right_rows):
    return jnp.einsum("hqk,khd->qhd", left_rows, right_rows, preferred_element_type=jnp.float32)


SEQ_PARTS = ("c", "x", "zh", "y")


GATHER_ORDER = ("zh", "c", "x", "y")


def gather_seq(x, axes):
    x = from_everyone(x, axes)
    x = x.reshape(*[lax.axis_size(axis) for axis in axes], *x.shape[1:])
    stacked = (*axes, *GATHER_ORDER[: 4 - len(axes)][::-1])
    order = [stacked.index(axis) for axis in SEQ_AXES]
    x = jnp.transpose(x, (*order, *range(4, x.ndim)))
    return x.reshape(-1, *x.shape[5:])


MERGE_GROUPS = (("y", "zh"), "x", "c")


def merged_with_dq(row_max, row_sum, partial_dq):
    rows = partial_dq.shape[0]
    width = partial_dq[0].size
    start = 0
    for axis in MERGE_GROUPS:
        size = lax.axis_size(axis)
        rows //= size
        stats = jnp.stack([row_max, row_sum]).reshape(1, -1)
        send = jnp.concatenate(
            [partial_dq.reshape(size, -1), jnp.broadcast_to(stats, (size, stats.shape[1]))], axis=1
        )
        got = lax.all_to_all(send, axis, 0, 0, tiled=True)
        got_dq = got[:, : rows * width].reshape(size, rows, *partial_dq.shape[1:])
        got_stats = got[:, rows * width :].reshape(size, 2, *row_max.shape)
        top = jnp.max(got_stats[:, 0], axis=0)
        rescale = jnp.exp(got_stats[:, 0] - top)
        row_sum = jnp.sum(got_stats[:, 1] * rescale, axis=0)
        row_max = top
        start = start + lax.axis_index(axis) * rows
        dq_rescale = jnp.transpose(lax.dynamic_slice_in_dim(rescale, start, rows, 2), (0, 2, 1))
        partial_dq = jnp.sum(dq_rescale[..., None] * got_dq, axis=0)
    own_sum = jnp.transpose(lax.dynamic_slice_in_dim(row_sum, start, rows, 1))
    return row_max, row_sum, partial_dq / own_sum[..., None]


def shards(
    cross_q,
    cross_out,
    cross_grad,
    prefix_k,
    prefix_v,
    pad_counts,
    self_q,
    self_k,
    self_v,
    self_grad,
):
    score_scale = HEAD_DIM ** (-0.5)
    own_rows, feature_width = cross_q.shape
    local_heads = feature_width // HEAD_DIM
    tokens = prefix_k.shape[0]
    grad_own = cross_grad.reshape(own_rows, local_heads, HEAD_DIM).astype(jnp.float32)
    out_own = cross_out.reshape(own_rows, local_heads, HEAD_DIM).astype(jnp.float32)
    row_dot = jnp.sum(grad_own * out_own, axis=2).astype(jnp.bfloat16)
    head_groups = lax.axis_size("zl")
    far_pairs = lax.axis_size("zh")
    stacked = jnp.stack([self_q, self_k, self_v, self_grad]).reshape(4, head_groups, feature_width)
    self_chunks = jnp.transpose(stacked, (1, 0, 2)).reshape(head_groups, -1)
    cross_cols = jnp.concatenate((cross_q, cross_grad, row_dot), axis=1)
    cross_width = cross_cols.shape[1]
    self_width = self_chunks.shape[1]
    outgoing = jnp.concatenate(
        (
            self_chunks,
            jnp.broadcast_to(cross_cols.reshape(1, -1), (head_groups, cross_cols.size)),
        ),
        axis=1,
    )
    outgoing = jnp.broadcast_to(outgoing[None], (far_pairs, *outgoing.shape))
    incoming = lax.all_to_all(
        outgoing.reshape(far_pairs * head_groups, -1), ("zh", "zl"), 0, 0, tiled=True
    ).reshape(far_pairs, head_groups, -1)
    block_rows = head_groups
    self_cols = incoming[:, :, :self_width]
    far_cross = lax.dynamic_index_in_dim(incoming, lax.axis_index("zl"), 1, keepdims=False)
    far_cross = far_cross[:, self_width:].reshape(far_pairs, own_rows, cross_width)
    first = jnp.concatenate((far_cross, self_cols), axis=2)
    first = from_everyone(first, "c")
    core = lax.axis_index("c")
    self_heads = first[..., cross_width:].reshape(*first.shape[:-1], 4, local_heads, HEAD_DIM)
    self_mine = lax.dynamic_index_in_dim(self_heads, core, axis=4, keepdims=False)
    rest = jnp.concatenate(
        (first[..., :cross_width], self_mine.reshape(*first.shape[:-1], -1)), axis=-1
    )
    gathered = gather_seq(rest, GATHER_ORDER[2:][::-1])
    query_all = gathered[:, : cross_q.shape[1]]
    grad_all = gathered[:, cross_q.shape[1] : 2 * cross_q.shape[1]]
    dots_all = gathered[:, 2 * cross_q.shape[1] : cross_width]
    self_all = gathered[:, cross_width:]
    latents = query_all.shape[0]
    query_heads = query_all.reshape(latents, local_heads, HEAD_DIM)
    grad_heads = grad_all.reshape(latents, local_heads, HEAD_DIM)
    key_heads = prefix_k.reshape(tokens, local_heads, HEAD_DIM)
    value_heads = prefix_v.reshape(tokens, local_heads, HEAD_DIM)
    valid_keys = jnp.arange(tokens) < tokens - pad_counts[0]
    scores = head_scores(query_heads, key_heads, score_scale)
    scores = jnp.where(valid_keys[None, None, :], scores, -jnp.inf)
    row_max = jnp.max(scores, axis=2)
    shifted = jnp.exp(scores - row_max[:, :, None])
    row_sum = jnp.sum(shifted, axis=2)
    row_dots = dots_all.astype(jnp.float32)
    grad_probs = jnp.einsum(
        "qhd,khd->hqk", grad_heads, value_heads, preferred_element_type=jnp.float32
    )
    local_gs = shifted * (grad_probs - jnp.transpose(row_dots)[:, :, None]) * score_scale
    local_dq = jnp.einsum(
        "hqk,khd->qhd",
        local_gs,
        key_heads.astype(jnp.float32),
        precision=lax.Precision.HIGHEST,
        preferred_element_type=jnp.float32,
    )
    row_maxes, row_sums, own_dq = merged_with_dq(row_max, row_sum, local_dq)
    log_total = row_maxes + jnp.log(row_sums)
    weights = jnp.exp(scores - log_total[:, :, None])
    prefix_dv = (
        contract_rows(weights.astype(jnp.bfloat16), grad_heads)
        .reshape(tokens, feature_width)
        .astype(jnp.bfloat16)
    )
    grad_scores = scores_grad(weights, grad_heads, value_heads, row_dots, score_scale)
    prefix_dk = (
        contract_rows(grad_scores, query_heads).reshape(tokens, feature_width).astype(jnp.bfloat16)
    )
    cross_dq = own_dq.reshape(own_rows, feature_width).astype(jnp.bfloat16)
    everything = jnp.transpose(self_all.reshape(latents, 4, HEAD_DIM), (1, 0, 2))
    all_rows = everything.shape[1]
    query_every = everything[0].reshape(all_rows, 1, HEAD_DIM)
    key_every = everything[1].reshape(all_rows, 1, HEAD_DIM)
    value_every = everything[2].reshape(all_rows, 1, HEAD_DIM)
    grad_every = everything[3].reshape(all_rows, 1, HEAD_DIM)
    row_ids = jnp.arange(all_rows)
    causal_full = row_ids[:, None] >= row_ids[None, :]
    full_scores = head_scores(query_every, key_every, score_scale)
    full_scores = jnp.where(causal_full[None, :, :], full_scores, -jnp.inf)
    full_lse = jax.nn.logsumexp(full_scores, axis=2)
    full_weights = jnp.exp(full_scores - full_lse[:, :, None])
    full_half = full_weights.astype(jnp.bfloat16)
    full_out = contract_cols(full_half, value_every)
    full_dot = jnp.sum(grad_every.astype(jnp.float32) * full_out, axis=2)
    full_gs = scores_grad(full_weights, grad_every, value_every, full_dot, score_scale)
    cores = lax.axis_size("c")
    chip_rows = block_rows * cores
    chip_start = (lax.axis_index(SEQ_AXES) - core) * block_rows
    query_part = lax.dynamic_slice_in_dim(full_gs, chip_start, chip_rows, 1)
    key_part = lax.dynamic_slice_in_dim(full_gs, chip_start, chip_rows, 2)
    half_part = lax.dynamic_slice_in_dim(full_half, chip_start, chip_rows, 2)
    head_results = jnp.stack(
        [
            contract_cols(query_part, key_every),
            contract_rows(key_part, query_every),
            contract_rows(half_part, grad_every),
        ]
    ).astype(jnp.bfloat16)
    both = lax.all_gather(head_results.reshape(3, chip_rows, HEAD_DIM), "c", axis=0)
    mine = lax.dynamic_slice_in_dim(both, core * block_rows, block_rows, 2)
    mine = jnp.transpose(mine, (1, 2, 0, 3)).reshape(3, block_rows, feature_width)
    self_dq, self_dk, self_dv = mine[0], mine[1], mine[2]
    return (cross_dq, prefix_dk, prefix_dv, self_dq, self_dk, self_dv)


SEQ_AXES = ("y", "zh", "x", "c")


def solution(mesh):
    sizes = dict(mesh.shape)
    split = mesh.devices.reshape(4, 2, 4, 2, sizes["head"])
    mesh = jax.sharding.Mesh(split, (*SEQ_AXES, "zl"))
    in_specs = (
        P(SEQ_AXES, "zl"),
        P(SEQ_AXES, "zl"),
        P(SEQ_AXES, "zl"),
        P(SEQ_AXES, "zl"),
        P(SEQ_AXES, "zl"),
        P(SEQ_AXES),
        P((*SEQ_AXES, "zl"), None),
        P((*SEQ_AXES, "zl"), None),
        P((*SEQ_AXES, "zl"), None),
        P((*SEQ_AXES, "zl"), None),
    )
    out_specs = (
        P(SEQ_AXES, "zl"),
        P(SEQ_AXES, "zl"),
        P(SEQ_AXES, "zl"),
        P(SEQ_AXES, "zl"),
        P(SEQ_AXES, "zl"),
        P(SEQ_AXES, "zl"),
    )
    return jax.shard_map(shards, mesh=mesh, in_specs=in_specs, out_specs=out_specs, check_vma=False)
```

```python
import jax
import jax.numpy as jnp
from jax import lax
from jax.sharding import PartitionSpec as P

HEAD_DIM = 128


def in_one_piece(arrays, axis, dim, along):
    ends, at = ([], 0)
    for a in arrays[:-1]:
        at += a.shape[along]
        ends.append(at)
    both = jnp.concatenate(arrays, axis=along)
    return tuple(jnp.split(lax.all_gather(both, axis, axis=dim, tiled=True), ends, axis=along))


def from_everyone(x, axis):
    copies = jnp.broadcast_to(x, (lax.axis_size(axis), *x.shape))
    return lax.all_to_all(copies, axis, split_axis=0, concat_axis=0, tiled=True)


def all_in_one(x, axis):
    leaves = jax.tree.leaves(x)
    order = sorted(range(len(leaves)), key=lambda k: -leaves[k].size)
    width = (1, *leaves[order[0]].shape)[-1]
    lines = [
        jnp.pad(leaves[k].reshape(-1), (0, -leaves[k].size % width)).reshape(-1, width)
        for k in order
    ]
    both, at, found = (from_everyone(jnp.concatenate(lines), axis), 0, {})
    for k, line in zip(order, lines):
        section = both[:, at : at + len(line)].reshape(len(both), -1)
        found[k] = section[:, : leaves[k].size].reshape(-1, *leaves[k].shape)
        at += len(line)
    numbers = iter(range(len(leaves)))
    return jax.tree.map(lambda _: found[next(numbers)], x)


def joined_by_halves(pieces, combine):
    while len(jax.tree.leaves(pieces)[0]) > 1:
        pieces = jax.vmap(combine)(
            *(jax.tree.map(lambda part: part[side::2], pieces) for side in (0, 1))
        )
    return jax.tree.map(lambda part: part[0], pieces)


def merged(x, axis, combine):
    pieces = all_in_one(x, axis)
    return joined_by_halves(pieces, combine)


def split_up(x, dim, size):
    before, after = (x.shape[:dim], x.shape[dim + 1 :])
    return jnp.moveaxis(x.reshape(*before, size, -1, *after), dim, 0)


def sum_at_owner(x, axis, dim):
    size = lax.axis_size(axis)
    parts = lax.all_to_all(split_up(x, dim, size), axis, 0, 0, tiled=True)
    return jnp.sum(parts, axis=0)


def joined_along(parts, dim):
    lengths = list(parts.shape[1:])
    lengths[dim] *= parts.shape[0]
    return jnp.moveaxis(parts, 0, dim).reshape(lengths)


def gathered_copies(x, axis, dim):
    return joined_along(from_everyone(x, axis), dim)


def merge_stats(left_stats, right_stats):
    row_max = jnp.maximum(left_stats[0], right_stats[0])
    row_sum = left_stats[1] * jnp.exp(left_stats[0] - row_max) + right_stats[1] * jnp.exp(
        right_stats[0] - row_max
    )
    return (row_max, row_sum)


def head_scores(queries, key_rows, score_scale):
    return (
        jnp.einsum("qhd,khd->hqk", queries, key_rows, preferred_element_type=jnp.float32)
        * score_scale
    )


def scores_grad(weights, grad_rows, value_rows, row_dot, score_scale):
    grad_probs = jnp.einsum(
        "qhd,khd->hqk", grad_rows, value_rows, preferred_element_type=jnp.float32
    )
    return (weights * (grad_probs - jnp.transpose(row_dot)[:, :, None]) * score_scale).astype(
        jnp.bfloat16
    )


def contract_rows(left_rows, right_rows):
    return jnp.einsum("hqk,qhd->khd", left_rows, right_rows, preferred_element_type=jnp.float32)


def contract_cols(left_rows, right_rows):
    return jnp.einsum("hqk,khd->qhd", left_rows, right_rows, preferred_element_type=jnp.float32)


SEQ_PARTS = ("c", "x", "zh", "y")


GATHER_ORDER = ("zh", "c", "x", "y")


def gather_seq(x, axes):
    x = from_everyone(x, axes)
    x = x.reshape(*[lax.axis_size(axis) for axis in axes], *x.shape[1:])
    stacked = (*axes, *GATHER_ORDER[: 4 - len(axes)][::-1])
    order = [stacked.index(axis) for axis in SEQ_AXES]
    x = jnp.transpose(x, (*order, *range(4, x.ndim)))
    return x.reshape(-1, *x.shape[5:])


MERGE_GROUPS = ("y", ("zh", "x"), "c")


def merged_with_dq(row_max, row_sum, partial_dq):
    rows = partial_dq.shape[0]
    width = partial_dq[0].size
    start = 0
    for axis in MERGE_GROUPS:
        size = lax.axis_size(axis)
        rows //= size
        stats = jnp.stack([row_max, row_sum]).reshape(1, -1)
        send = jnp.concatenate(
            [partial_dq.reshape(size, -1), jnp.broadcast_to(stats, (size, stats.shape[1]))], axis=1
        )
        got = lax.all_to_all(send, axis, 0, 0, tiled=True)
        got_dq = got[:, : rows * width].reshape(size, rows, *partial_dq.shape[1:])
        got_stats = got[:, rows * width :].reshape(size, 2, *row_max.shape)
        top = jnp.max(got_stats[:, 0], axis=0)
        rescale = jnp.exp(got_stats[:, 0] - top)
        row_sum = jnp.sum(got_stats[:, 1] * rescale, axis=0)
        row_max = top
        start = start + lax.axis_index(axis) * rows
        dq_rescale = jnp.transpose(lax.dynamic_slice_in_dim(rescale, start, rows, 2), (0, 2, 1))
        partial_dq = jnp.sum(dq_rescale[..., None] * got_dq, axis=0)
    own_sum = jnp.transpose(lax.dynamic_slice_in_dim(row_sum, start, rows, 1))
    return row_max, row_sum, partial_dq / own_sum[..., None]


def shards(
    cross_q,
    cross_out,
    cross_grad,
    prefix_k,
    prefix_v,
    pad_counts,
    self_q,
    self_k,
    self_v,
    self_grad,
):
    score_scale = HEAD_DIM ** (-0.5)
    own_rows, feature_width = cross_q.shape
    local_heads = feature_width // HEAD_DIM
    tokens = prefix_k.shape[0]
    grad_own = cross_grad.reshape(own_rows, local_heads, HEAD_DIM).astype(jnp.float32)
    out_own = cross_out.reshape(own_rows, local_heads, HEAD_DIM).astype(jnp.float32)
    row_dot = jnp.sum(grad_own * out_own, axis=2).astype(jnp.bfloat16)
    head_groups = lax.axis_size("zl")
    far_pairs = lax.axis_size("zh")
    stacked = jnp.stack([self_q, self_k, self_v, self_grad]).reshape(4, head_groups, feature_width)
    self_chunks = jnp.transpose(stacked, (1, 0, 2)).reshape(head_groups, -1)
    cross_cols = jnp.concatenate((cross_q, cross_grad, row_dot), axis=1)
    cross_width = cross_cols.shape[1]
    self_width = self_chunks.shape[1]
    outgoing = jnp.concatenate(
        (
            self_chunks,
            jnp.broadcast_to(cross_cols.reshape(1, -1), (head_groups, cross_cols.size)),
        ),
        axis=1,
    )
    outgoing = jnp.broadcast_to(outgoing[None], (far_pairs, *outgoing.shape))
    incoming = lax.all_to_all(
        outgoing.reshape(far_pairs * head_groups, -1), ("zh", "zl"), 0, 0, tiled=True
    ).reshape(far_pairs, head_groups, -1)
    block_rows = head_groups
    self_cols = incoming[:, :, :self_width]
    far_cross = lax.dynamic_index_in_dim(incoming, lax.axis_index("zl"), 1, keepdims=False)
    far_cross = far_cross[:, self_width:].reshape(far_pairs, own_rows, cross_width)
    core = lax.axis_index("c")
    cores = lax.axis_size("c")
    self_heads = self_cols.reshape(far_pairs, head_groups, 4, local_heads, HEAD_DIM)
    per_core = jnp.moveaxis(self_heads, 3, 0).reshape(cores, far_pairs, head_groups, -1)
    chunks = jnp.concatenate(
        (jnp.broadcast_to(far_cross[None], (cores, *far_cross.shape)), per_core), axis=-1
    )
    plane = lax.axis_size("y") * lax.axis_size("x")
    sent = jnp.broadcast_to(chunks[None], (plane, *chunks.shape)).reshape(plane * cores, *chunks.shape[1:])
    got = lax.all_to_all(sent, ("y", "x", "c"), 0, 0, tiled=True)
    got = got.reshape(lax.axis_size("y"), lax.axis_size("x"), cores, *chunks.shape[1:])
    gathered = jnp.transpose(got, (0, 3, 1, 2, 4, 5)).reshape(-1, got.shape[-1])
    query_all = gathered[:, : cross_q.shape[1]]
    grad_all = gathered[:, cross_q.shape[1] : 2 * cross_q.shape[1]]
    dots_all = gathered[:, 2 * cross_q.shape[1] : cross_width]
    self_all = gathered[:, cross_width:]
    latents = query_all.shape[0]
    query_heads = query_all.reshape(latents, local_heads, HEAD_DIM)
    grad_heads = grad_all.reshape(latents, local_heads, HEAD_DIM)
    key_heads = prefix_k.reshape(tokens, local_heads, HEAD_DIM)
    value_heads = prefix_v.reshape(tokens, local_heads, HEAD_DIM)
    valid_keys = jnp.arange(tokens) < tokens - pad_counts[0]
    scores = head_scores(query_heads, key_heads, score_scale)
    scores = jnp.where(valid_keys[None, None, :], scores, -jnp.inf)
    row_max = jnp.max(scores, axis=2)
    shifted = jnp.exp(scores - row_max[:, :, None])
    row_sum = jnp.sum(shifted, axis=2)
    row_dots = dots_all.astype(jnp.float32)
    grad_probs = jnp.einsum(
        "qhd,khd->hqk", grad_heads, value_heads, preferred_element_type=jnp.float32
    )
    local_gs = shifted * (grad_probs - jnp.transpose(row_dots)[:, :, None]) * score_scale
    local_dq = jnp.einsum(
        "hqk,khd->qhd",
        local_gs,
        key_heads.astype(jnp.float32),
        precision=lax.Precision.HIGHEST,
        preferred_element_type=jnp.float32,
    )
    row_maxes, row_sums, own_dq = merged_with_dq(row_max, row_sum, local_dq)
    log_total = row_maxes + jnp.log(row_sums)
    weights = jnp.exp(scores - log_total[:, :, None])
    prefix_dv = (
        contract_rows(weights.astype(jnp.bfloat16), grad_heads)
        .reshape(tokens, feature_width)
        .astype(jnp.bfloat16)
    )
    grad_scores = scores_grad(weights, grad_heads, value_heads, row_dots, score_scale)
    prefix_dk = (
        contract_rows(grad_scores, query_heads).reshape(tokens, feature_width).astype(jnp.bfloat16)
    )
    cross_dq = own_dq.reshape(own_rows, feature_width).astype(jnp.bfloat16)
    everything = jnp.transpose(self_all.reshape(latents, 4, HEAD_DIM), (1, 0, 2))
    all_rows = everything.shape[1]
    query_every = everything[0].reshape(all_rows, 1, HEAD_DIM)
    key_every = everything[1].reshape(all_rows, 1, HEAD_DIM)
    value_every = everything[2].reshape(all_rows, 1, HEAD_DIM)
    grad_every = everything[3].reshape(all_rows, 1, HEAD_DIM)
    row_ids = jnp.arange(all_rows)
    causal_full = row_ids[:, None] >= row_ids[None, :]
    full_scores = head_scores(query_every, key_every, score_scale)
    full_scores = jnp.where(causal_full[None, :, :], full_scores, -jnp.inf)
    full_lse = jax.nn.logsumexp(full_scores, axis=2)
    full_weights = jnp.exp(full_scores - full_lse[:, :, None])
    full_half = full_weights.astype(jnp.bfloat16)
    full_out = contract_cols(full_half, value_every)
    full_dot = jnp.sum(grad_every.astype(jnp.float32) * full_out, axis=2)
    full_gs = scores_grad(full_weights, grad_every, value_every, full_dot, score_scale)
    cores = lax.axis_size("c")
    chip_rows = block_rows * cores
    chip_start = (lax.axis_index(SEQ_AXES) - core) * block_rows
    query_part = lax.dynamic_slice_in_dim(full_gs, chip_start, chip_rows, 1)
    key_part = lax.dynamic_slice_in_dim(full_gs, chip_start, chip_rows, 2)
    half_part = lax.dynamic_slice_in_dim(full_half, chip_start, chip_rows, 2)
    head_results = jnp.stack(
        [
            contract_cols(query_part, key_every),
            contract_rows(key_part, query_every),
            contract_rows(half_part, grad_every),
        ]
    ).astype(jnp.bfloat16)
    both = lax.all_gather(head_results.reshape(3, chip_rows, HEAD_DIM), "c", axis=0)
    mine = lax.dynamic_slice_in_dim(both, core * block_rows, block_rows, 2)
    mine = jnp.transpose(mine, (1, 2, 0, 3)).reshape(3, block_rows, feature_width)
    self_dq, self_dk, self_dv = mine[0], mine[1], mine[2]
    return (cross_dq, prefix_dk, prefix_dv, self_dq, self_dk, self_dv)


SEQ_AXES = ("y", "zh", "x", "c")


def solution(mesh):
    sizes = dict(mesh.shape)
    split = mesh.devices.reshape(4, 2, 4, 2, sizes["head"])
    mesh = jax.sharding.Mesh(split, (*SEQ_AXES, "zl"))
    in_specs = (
        P(SEQ_AXES, "zl"),
        P(SEQ_AXES, "zl"),
        P(SEQ_AXES, "zl"),
        P(SEQ_AXES, "zl"),
        P(SEQ_AXES, "zl"),
        P(SEQ_AXES),
        P((*SEQ_AXES, "zl"), None),
        P((*SEQ_AXES, "zl"), None),
        P((*SEQ_AXES, "zl"), None),
        P((*SEQ_AXES, "zl"), None),
    )
    out_specs = (
        P(SEQ_AXES, "zl"),
        P(SEQ_AXES, "zl"),
        P(SEQ_AXES, "zl"),
        P(SEQ_AXES, "zl"),
        P(SEQ_AXES, "zl"),
        P(SEQ_AXES, "zl"),
    )
    return jax.shard_map(shards, mesh=mesh, in_specs=in_specs, out_specs=out_specs, check_vma=False)
```

```python
import jax
import jax.numpy as jnp
from jax import lax
from jax.sharding import PartitionSpec as P

HEAD_DIM = 128


def in_one_piece(arrays, axis, dim, along):
    ends, at = ([], 0)
    for a in arrays[:-1]:
        at += a.shape[along]
        ends.append(at)
    both = jnp.concatenate(arrays, axis=along)
    return tuple(jnp.split(lax.all_gather(both, axis, axis=dim, tiled=True), ends, axis=along))


def from_everyone(x, axis):
    copies = jnp.broadcast_to(x, (lax.axis_size(axis), *x.shape))
    return lax.all_to_all(copies, axis, split_axis=0, concat_axis=0, tiled=True)


def all_in_one(x, axis):
    leaves = jax.tree.leaves(x)
    order = sorted(range(len(leaves)), key=lambda k: -leaves[k].size)
    width = (1, *leaves[order[0]].shape)[-1]
    lines = [
        jnp.pad(leaves[k].reshape(-1), (0, -leaves[k].size % width)).reshape(-1, width)
        for k in order
    ]
    both, at, found = (from_everyone(jnp.concatenate(lines), axis), 0, {})
    for k, line in zip(order, lines):
        section = both[:, at : at + len(line)].reshape(len(both), -1)
        found[k] = section[:, : leaves[k].size].reshape(-1, *leaves[k].shape)
        at += len(line)
    numbers = iter(range(len(leaves)))
    return jax.tree.map(lambda _: found[next(numbers)], x)


def joined_by_halves(pieces, combine):
    while len(jax.tree.leaves(pieces)[0]) > 1:
        pieces = jax.vmap(combine)(
            *(jax.tree.map(lambda part: part[side::2], pieces) for side in (0, 1))
        )
    return jax.tree.map(lambda part: part[0], pieces)


def merged(x, axis, combine):
    pieces = all_in_one(x, axis)
    return joined_by_halves(pieces, combine)


def split_up(x, dim, size):
    before, after = (x.shape[:dim], x.shape[dim + 1 :])
    return jnp.moveaxis(x.reshape(*before, size, -1, *after), dim, 0)


def sum_at_owner(x, axis, dim):
    size = lax.axis_size(axis)
    parts = lax.all_to_all(split_up(x, dim, size), axis, 0, 0, tiled=True)
    return jnp.sum(parts, axis=0)


def joined_along(parts, dim):
    lengths = list(parts.shape[1:])
    lengths[dim] *= parts.shape[0]
    return jnp.moveaxis(parts, 0, dim).reshape(lengths)


def gathered_copies(x, axis, dim):
    return joined_along(from_everyone(x, axis), dim)


def merge_stats(left_stats, right_stats):
    row_max = jnp.maximum(left_stats[0], right_stats[0])
    row_sum = left_stats[1] * jnp.exp(left_stats[0] - row_max) + right_stats[1] * jnp.exp(
        right_stats[0] - row_max
    )
    return (row_max, row_sum)


def head_scores(queries, key_rows, score_scale):
    return (
        jnp.einsum("qhd,khd->hqk", queries, key_rows, preferred_element_type=jnp.float32)
        * score_scale
    )


def scores_grad(weights, grad_rows, value_rows, row_dot, score_scale):
    grad_probs = jnp.einsum(
        "qhd,khd->hqk", grad_rows, value_rows, preferred_element_type=jnp.float32
    )
    return (weights * (grad_probs - jnp.transpose(row_dot)[:, :, None]) * score_scale).astype(
        jnp.bfloat16
    )


def contract_rows(left_rows, right_rows):
    return jnp.einsum("hqk,qhd->khd", left_rows, right_rows, preferred_element_type=jnp.float32)


def contract_cols(left_rows, right_rows):
    return jnp.einsum("hqk,khd->qhd", left_rows, right_rows, preferred_element_type=jnp.float32)


SEQ_PARTS = ("c", "x", "zh", "y")


GATHER_ORDER = ("zh", "c", "x", "y")


def gather_seq(x, axes):
    x = from_everyone(x, axes)
    x = x.reshape(*[lax.axis_size(axis) for axis in axes], *x.shape[1:])
    stacked = (*axes, *GATHER_ORDER[: 4 - len(axes)][::-1])
    order = [stacked.index(axis) for axis in SEQ_AXES]
    x = jnp.transpose(x, (*order, *range(4, x.ndim)))
    return x.reshape(-1, *x.shape[5:])


MERGE_GROUPS = (("y", "zh"), ("x", "c"))


def merged_with_dq(row_max, row_sum, partial_dq):
    rows = partial_dq.shape[0]
    width = partial_dq[0].size
    start = 0
    for axis in MERGE_GROUPS:
        size = lax.axis_size(axis)
        rows //= size
        stats = jnp.stack([row_max, row_sum]).reshape(1, -1)
        send = jnp.concatenate(
            [partial_dq.reshape(size, -1), jnp.broadcast_to(stats, (size, stats.shape[1]))], axis=1
        )
        got = lax.all_to_all(send, axis, 0, 0, tiled=True)
        got_dq = got[:, : rows * width].reshape(size, rows, *partial_dq.shape[1:])
        got_stats = got[:, rows * width :].reshape(size, 2, *row_max.shape)
        top = jnp.max(got_stats[:, 0], axis=0)
        rescale = jnp.exp(got_stats[:, 0] - top)
        row_sum = jnp.sum(got_stats[:, 1] * rescale, axis=0)
        row_max = top
        start = start + lax.axis_index(axis) * rows
        dq_rescale = jnp.transpose(lax.dynamic_slice_in_dim(rescale, start, rows, 2), (0, 2, 1))
        partial_dq = jnp.sum(dq_rescale[..., None] * got_dq, axis=0)
    own_sum = jnp.transpose(lax.dynamic_slice_in_dim(row_sum, start, rows, 1))
    return row_max, row_sum, partial_dq / own_sum[..., None]


def shards(
    cross_q,
    cross_out,
    cross_grad,
    prefix_k,
    prefix_v,
    pad_counts,
    self_q,
    self_k,
    self_v,
    self_grad,
):
    score_scale = HEAD_DIM ** (-0.5)
    own_rows, feature_width = cross_q.shape
    local_heads = feature_width // HEAD_DIM
    tokens = prefix_k.shape[0]
    grad_own = cross_grad.reshape(own_rows, local_heads, HEAD_DIM).astype(jnp.float32)
    out_own = cross_out.reshape(own_rows, local_heads, HEAD_DIM).astype(jnp.float32)
    row_dot = jnp.sum(grad_own * out_own, axis=2).astype(jnp.bfloat16)
    head_groups = lax.axis_size("zl")
    far_pairs = lax.axis_size("zh")
    stacked = jnp.stack([self_q, self_k, self_v, self_grad]).reshape(4, head_groups, feature_width)
    self_chunks = jnp.transpose(stacked, (1, 0, 2)).reshape(head_groups, -1)
    cross_cols = jnp.concatenate((cross_q, cross_grad, row_dot), axis=1)
    cross_width = cross_cols.shape[1]
    self_width = self_chunks.shape[1]
    outgoing = jnp.concatenate(
        (
            self_chunks,
            jnp.broadcast_to(cross_cols.reshape(1, -1), (head_groups, cross_cols.size)),
        ),
        axis=1,
    )
    outgoing = jnp.broadcast_to(outgoing[None], (far_pairs, *outgoing.shape))
    incoming = lax.all_to_all(
        outgoing.reshape(far_pairs * head_groups, -1), ("zh", "zl"), 0, 0, tiled=True
    ).reshape(far_pairs, head_groups, -1)
    block_rows = head_groups
    self_cols = incoming[:, :, :self_width]
    far_cross = lax.dynamic_index_in_dim(incoming, lax.axis_index("zl"), 1, keepdims=False)
    far_cross = far_cross[:, self_width:].reshape(far_pairs, own_rows, cross_width)
    core = lax.axis_index("c")
    cores = lax.axis_size("c")
    self_heads = self_cols.reshape(far_pairs, head_groups, 4, local_heads, HEAD_DIM)
    per_core = jnp.moveaxis(self_heads, 3, 0).reshape(cores, far_pairs, head_groups, -1)
    chunks = jnp.concatenate(
        (jnp.broadcast_to(far_cross[None], (cores, *far_cross.shape)), per_core), axis=-1
    )
    plane = lax.axis_size("y") * lax.axis_size("x")
    sent = jnp.broadcast_to(chunks[None], (plane, *chunks.shape)).reshape(plane * cores, *chunks.shape[1:])
    got = lax.all_to_all(sent, ("y", "x", "c"), 0, 0, tiled=True)
    got = got.reshape(lax.axis_size("y"), lax.axis_size("x"), cores, *chunks.shape[1:])
    gathered = jnp.transpose(got, (0, 3, 1, 2, 4, 5)).reshape(-1, got.shape[-1])
    query_all = gathered[:, : cross_q.shape[1]]
    grad_all = gathered[:, cross_q.shape[1] : 2 * cross_q.shape[1]]
    dots_all = gathered[:, 2 * cross_q.shape[1] : cross_width]
    self_all = gathered[:, cross_width:]
    latents = query_all.shape[0]
    query_heads = query_all.reshape(latents, local_heads, HEAD_DIM)
    grad_heads = grad_all.reshape(latents, local_heads, HEAD_DIM)
    key_heads = prefix_k.reshape(tokens, local_heads, HEAD_DIM)
    value_heads = prefix_v.reshape(tokens, local_heads, HEAD_DIM)
    valid_keys = jnp.arange(tokens) < tokens - pad_counts[0]
    scores = head_scores(query_heads, key_heads, score_scale)
    scores = jnp.where(valid_keys[None, None, :], scores, -jnp.inf)
    row_max = jnp.max(scores, axis=2)
    shifted = jnp.exp(scores - row_max[:, :, None])
    row_sum = jnp.sum(shifted, axis=2)
    row_dots = dots_all.astype(jnp.float32)
    grad_probs = jnp.einsum(
        "qhd,khd->hqk", grad_heads, value_heads, preferred_element_type=jnp.float32
    )
    local_gs = shifted * (grad_probs - jnp.transpose(row_dots)[:, :, None]) * score_scale
    local_dq = jnp.einsum(
        "hqk,khd->qhd",
        local_gs,
        key_heads.astype(jnp.float32),
        precision=lax.Precision.HIGHEST,
        preferred_element_type=jnp.float32,
    )
    row_maxes, row_sums, own_dq = merged_with_dq(row_max, row_sum, local_dq)
    log_total = row_maxes + jnp.log(row_sums)
    weights = jnp.exp(scores - log_total[:, :, None])
    prefix_dv = (
        contract_rows(weights.astype(jnp.bfloat16), grad_heads)
        .reshape(tokens, feature_width)
        .astype(jnp.bfloat16)
    )
    grad_scores = scores_grad(weights, grad_heads, value_heads, row_dots, score_scale)
    prefix_dk = (
        contract_rows(grad_scores, query_heads).reshape(tokens, feature_width).astype(jnp.bfloat16)
    )
    cross_dq = own_dq.reshape(own_rows, feature_width).astype(jnp.bfloat16)
    everything = jnp.transpose(self_all.reshape(latents, 4, HEAD_DIM), (1, 0, 2))
    all_rows = everything.shape[1]
    query_every = everything[0].reshape(all_rows, 1, HEAD_DIM)
    key_every = everything[1].reshape(all_rows, 1, HEAD_DIM)
    value_every = everything[2].reshape(all_rows, 1, HEAD_DIM)
    grad_every = everything[3].reshape(all_rows, 1, HEAD_DIM)
    row_ids = jnp.arange(all_rows)
    causal_full = row_ids[:, None] >= row_ids[None, :]
    full_scores = head_scores(query_every, key_every, score_scale)
    full_scores = jnp.where(causal_full[None, :, :], full_scores, -jnp.inf)
    full_lse = jax.nn.logsumexp(full_scores, axis=2)
    full_weights = jnp.exp(full_scores - full_lse[:, :, None])
    full_half = full_weights.astype(jnp.bfloat16)
    full_out = contract_cols(full_half, value_every)
    full_dot = jnp.sum(grad_every.astype(jnp.float32) * full_out, axis=2)
    full_gs = scores_grad(full_weights, grad_every, value_every, full_dot, score_scale)
    cores = lax.axis_size("c")
    chip_rows = block_rows * cores
    chip_start = (lax.axis_index(SEQ_AXES) - core) * block_rows
    query_part = lax.dynamic_slice_in_dim(full_gs, chip_start, chip_rows, 1)
    key_part = lax.dynamic_slice_in_dim(full_gs, chip_start, chip_rows, 2)
    half_part = lax.dynamic_slice_in_dim(full_half, chip_start, chip_rows, 2)
    head_results = jnp.stack(
        [
            contract_cols(query_part, key_every),
            contract_rows(key_part, query_every),
            contract_rows(half_part, grad_every),
        ]
    ).astype(jnp.bfloat16)
    both = lax.all_gather(head_results.reshape(3, chip_rows, HEAD_DIM), "c", axis=0)
    mine = lax.dynamic_slice_in_dim(both, core * block_rows, block_rows, 2)
    mine = jnp.transpose(mine, (1, 2, 0, 3)).reshape(3, block_rows, feature_width)
    self_dq, self_dk, self_dv = mine[0], mine[1], mine[2]
    return (cross_dq, prefix_dk, prefix_dv, self_dq, self_dk, self_dv)


SEQ_AXES = ("y", "zh", "x", "c")


def solution(mesh):
    sizes = dict(mesh.shape)
    split = mesh.devices.reshape(4, 2, 4, 2, sizes["head"])
    mesh = jax.sharding.Mesh(split, (*SEQ_AXES, "zl"))
    in_specs = (
        P(SEQ_AXES, "zl"),
        P(SEQ_AXES, "zl"),
        P(SEQ_AXES, "zl"),
        P(SEQ_AXES, "zl"),
        P(SEQ_AXES, "zl"),
        P(SEQ_AXES),
        P((*SEQ_AXES, "zl"), None),
        P((*SEQ_AXES, "zl"), None),
        P((*SEQ_AXES, "zl"), None),
        P((*SEQ_AXES, "zl"), None),
    )
    out_specs = (
        P(SEQ_AXES, "zl"),
        P(SEQ_AXES, "zl"),
        P(SEQ_AXES, "zl"),
        P(SEQ_AXES, "zl"),
        P(SEQ_AXES, "zl"),
        P(SEQ_AXES, "zl"),
    )
    return jax.shard_map(shards, mesh=mesh, in_specs=in_specs, out_specs=out_specs, check_vma=False)
```

```python
import jax
import jax.numpy as jnp
from jax import lax
from jax.sharding import PartitionSpec as P

HEAD_DIM = 128


def in_one_piece(arrays, axis, dim, along):
    ends, at = ([], 0)
    for a in arrays[:-1]:
        at += a.shape[along]
        ends.append(at)
    both = jnp.concatenate(arrays, axis=along)
    return tuple(jnp.split(lax.all_gather(both, axis, axis=dim, tiled=True), ends, axis=along))


def from_everyone(x, axis):
    copies = jnp.broadcast_to(x, (lax.axis_size(axis), *x.shape))
    return lax.all_to_all(copies, axis, split_axis=0, concat_axis=0, tiled=True)


def all_in_one(x, axis):
    leaves = jax.tree.leaves(x)
    order = sorted(range(len(leaves)), key=lambda k: -leaves[k].size)
    width = (1, *leaves[order[0]].shape)[-1]
    lines = [
        jnp.pad(leaves[k].reshape(-1), (0, -leaves[k].size % width)).reshape(-1, width)
        for k in order
    ]
    both, at, found = (from_everyone(jnp.concatenate(lines), axis), 0, {})
    for k, line in zip(order, lines):
        section = both[:, at : at + len(line)].reshape(len(both), -1)
        found[k] = section[:, : leaves[k].size].reshape(-1, *leaves[k].shape)
        at += len(line)
    numbers = iter(range(len(leaves)))
    return jax.tree.map(lambda _: found[next(numbers)], x)


def joined_by_halves(pieces, combine):
    while len(jax.tree.leaves(pieces)[0]) > 1:
        pieces = jax.vmap(combine)(
            *(jax.tree.map(lambda part: part[side::2], pieces) for side in (0, 1))
        )
    return jax.tree.map(lambda part: part[0], pieces)


def merged(x, axis, combine):
    pieces = all_in_one(x, axis)
    return joined_by_halves(pieces, combine)


def split_up(x, dim, size):
    before, after = (x.shape[:dim], x.shape[dim + 1 :])
    return jnp.moveaxis(x.reshape(*before, size, -1, *after), dim, 0)


def sum_at_owner(x, axis, dim):
    size = lax.axis_size(axis)
    parts = lax.all_to_all(split_up(x, dim, size), axis, 0, 0, tiled=True)
    return jnp.sum(parts, axis=0)


def joined_along(parts, dim):
    lengths = list(parts.shape[1:])
    lengths[dim] *= parts.shape[0]
    return jnp.moveaxis(parts, 0, dim).reshape(lengths)


def gathered_copies(x, axis, dim):
    return joined_along(from_everyone(x, axis), dim)


def merge_stats(left_stats, right_stats):
    row_max = jnp.maximum(left_stats[0], right_stats[0])
    row_sum = left_stats[1] * jnp.exp(left_stats[0] - row_max) + right_stats[1] * jnp.exp(
        right_stats[0] - row_max
    )
    return (row_max, row_sum)


def head_scores(queries, key_rows, score_scale):
    return (
        jnp.einsum("qhd,khd->hqk", queries, key_rows, preferred_element_type=jnp.float32)
        * score_scale
    )


def scores_grad(weights, grad_rows, value_rows, row_dot, score_scale):
    grad_probs = jnp.einsum(
        "qhd,khd->hqk", grad_rows, value_rows, preferred_element_type=jnp.float32
    )
    return (weights * (grad_probs - jnp.transpose(row_dot)[:, :, None]) * score_scale).astype(
        jnp.bfloat16
    )


def contract_rows(left_rows, right_rows):
    return jnp.einsum("hqk,qhd->khd", left_rows, right_rows, preferred_element_type=jnp.float32)


def contract_cols(left_rows, right_rows):
    return jnp.einsum("hqk,khd->qhd", left_rows, right_rows, preferred_element_type=jnp.float32)


SEQ_PARTS = ("c", "x", "zh", "y")


GATHER_ORDER = ("zh", "c", "x", "y")


def gather_seq(x, axes):
    x = from_everyone(x, axes)
    x = x.reshape(*[lax.axis_size(axis) for axis in axes], *x.shape[1:])
    stacked = (*axes, *GATHER_ORDER[: 4 - len(axes)][::-1])
    order = [stacked.index(axis) for axis in SEQ_AXES]
    x = jnp.transpose(x, (*order, *range(4, x.ndim)))
    return x.reshape(-1, *x.shape[5:])


MERGE_GROUPS = ("y", "zh", ("x", "c"))


def merged_with_dq(row_max, row_sum, partial_dq):
    rows = partial_dq.shape[0]
    width = partial_dq[0].size
    start = 0
    for axis in MERGE_GROUPS:
        size = lax.axis_size(axis)
        rows //= size
        stats = jnp.stack([row_max, row_sum]).reshape(1, -1)
        send = jnp.concatenate(
            [partial_dq.reshape(size, -1), jnp.broadcast_to(stats, (size, stats.shape[1]))], axis=1
        )
        got = lax.all_to_all(send, axis, 0, 0, tiled=True)
        got_dq = got[:, : rows * width].reshape(size, rows, *partial_dq.shape[1:])
        got_stats = got[:, rows * width :].reshape(size, 2, *row_max.shape)
        top = jnp.max(got_stats[:, 0], axis=0)
        rescale = jnp.exp(got_stats[:, 0] - top)
        row_sum = jnp.sum(got_stats[:, 1] * rescale, axis=0)
        row_max = top
        start = start + lax.axis_index(axis) * rows
        dq_rescale = jnp.transpose(lax.dynamic_slice_in_dim(rescale, start, rows, 2), (0, 2, 1))
        partial_dq = jnp.sum(dq_rescale[..., None] * got_dq, axis=0)
    own_sum = jnp.transpose(lax.dynamic_slice_in_dim(row_sum, start, rows, 1))
    return row_max, row_sum, partial_dq / own_sum[..., None]


def shards(
    cross_q,
    cross_out,
    cross_grad,
    prefix_k,
    prefix_v,
    pad_counts,
    self_q,
    self_k,
    self_v,
    self_grad,
):
    score_scale = HEAD_DIM ** (-0.5)
    own_rows, feature_width = cross_q.shape
    local_heads = feature_width // HEAD_DIM
    tokens = prefix_k.shape[0]
    grad_own = cross_grad.reshape(own_rows, local_heads, HEAD_DIM).astype(jnp.float32)
    out_own = cross_out.reshape(own_rows, local_heads, HEAD_DIM).astype(jnp.float32)
    row_dot = jnp.sum(grad_own * out_own, axis=2).astype(jnp.bfloat16)
    head_groups = lax.axis_size("zl")
    far_pairs = lax.axis_size("zh")
    stacked = jnp.stack([self_q, self_k, self_v, self_grad]).reshape(4, head_groups, feature_width)
    self_chunks = jnp.transpose(stacked, (1, 0, 2)).reshape(head_groups, -1)
    cross_cols = jnp.concatenate((cross_q, cross_grad, row_dot), axis=1)
    cross_width = cross_cols.shape[1]
    self_width = self_chunks.shape[1]
    outgoing = jnp.concatenate(
        (
            self_chunks,
            jnp.broadcast_to(cross_cols.reshape(1, -1), (head_groups, cross_cols.size)),
        ),
        axis=1,
    )
    outgoing = jnp.broadcast_to(outgoing[None], (far_pairs, *outgoing.shape))
    incoming = lax.all_to_all(
        outgoing.reshape(far_pairs * head_groups, -1), ("zh", "zl"), 0, 0, tiled=True
    ).reshape(far_pairs, head_groups, -1)
    block_rows = head_groups
    self_cols = incoming[:, :, :self_width]
    far_cross = lax.dynamic_index_in_dim(incoming, lax.axis_index("zl"), 1, keepdims=False)
    far_cross = far_cross[:, self_width:].reshape(far_pairs, own_rows, cross_width)
    core = lax.axis_index("c")
    cores = lax.axis_size("c")
    self_heads = self_cols.reshape(far_pairs, head_groups, 4, local_heads, HEAD_DIM)
    per_core = jnp.moveaxis(self_heads, 3, 0).reshape(cores, far_pairs, head_groups, -1)
    chunks = jnp.concatenate(
        (jnp.broadcast_to(far_cross[None], (cores, *far_cross.shape)), per_core), axis=-1
    )
    plane = lax.axis_size("y") * lax.axis_size("x")
    sent = jnp.broadcast_to(chunks[None], (plane, *chunks.shape)).reshape(plane * cores, *chunks.shape[1:])
    got = lax.all_to_all(sent, ("y", "x", "c"), 0, 0, tiled=True)
    got = got.reshape(lax.axis_size("y"), lax.axis_size("x"), cores, *chunks.shape[1:])
    gathered = jnp.transpose(got, (0, 3, 1, 2, 4, 5)).reshape(-1, got.shape[-1])
    query_all = gathered[:, : cross_q.shape[1]]
    grad_all = gathered[:, cross_q.shape[1] : 2 * cross_q.shape[1]]
    dots_all = gathered[:, 2 * cross_q.shape[1] : cross_width]
    self_all = gathered[:, cross_width:]
    latents = query_all.shape[0]
    query_heads = query_all.reshape(latents, local_heads, HEAD_DIM)
    grad_heads = grad_all.reshape(latents, local_heads, HEAD_DIM)
    key_heads = prefix_k.reshape(tokens, local_heads, HEAD_DIM)
    value_heads = prefix_v.reshape(tokens, local_heads, HEAD_DIM)
    valid_keys = jnp.arange(tokens) < tokens - pad_counts[0]
    scores = head_scores(query_heads, key_heads, score_scale)
    scores = jnp.where(valid_keys[None, None, :], scores, -jnp.inf)
    row_max = jnp.max(scores, axis=2)
    shifted = jnp.exp(scores - row_max[:, :, None])
    row_sum = jnp.sum(shifted, axis=2)
    row_dots = dots_all.astype(jnp.float32)
    grad_probs = jnp.einsum(
        "qhd,khd->hqk", grad_heads, value_heads, preferred_element_type=jnp.float32
    )
    local_gs = shifted * (grad_probs - jnp.transpose(row_dots)[:, :, None]) * score_scale
    local_dq = jnp.einsum(
        "hqk,khd->qhd",
        local_gs,
        key_heads.astype(jnp.float32),
        precision=lax.Precision.HIGHEST,
        preferred_element_type=jnp.float32,
    )
    row_maxes, row_sums, own_dq = merged_with_dq(row_max, row_sum, local_dq)
    log_total = row_maxes + jnp.log(row_sums)
    weights = jnp.exp(scores - log_total[:, :, None])
    prefix_dv = (
        contract_rows(weights.astype(jnp.bfloat16), grad_heads)
        .reshape(tokens, feature_width)
        .astype(jnp.bfloat16)
    )
    grad_scores = scores_grad(weights, grad_heads, value_heads, row_dots, score_scale)
    prefix_dk = (
        contract_rows(grad_scores, query_heads).reshape(tokens, feature_width).astype(jnp.bfloat16)
    )
    cross_dq = own_dq.reshape(own_rows, feature_width).astype(jnp.bfloat16)
    everything = jnp.transpose(self_all.reshape(latents, 4, HEAD_DIM), (1, 0, 2))
    all_rows = everything.shape[1]
    query_every = everything[0].reshape(all_rows, 1, HEAD_DIM)
    key_every = everything[1].reshape(all_rows, 1, HEAD_DIM)
    value_every = everything[2].reshape(all_rows, 1, HEAD_DIM)
    grad_every = everything[3].reshape(all_rows, 1, HEAD_DIM)
    row_ids = jnp.arange(all_rows)
    causal_full = row_ids[:, None] >= row_ids[None, :]
    full_scores = head_scores(query_every, key_every, score_scale)
    full_scores = jnp.where(causal_full[None, :, :], full_scores, -jnp.inf)
    full_lse = jax.nn.logsumexp(full_scores, axis=2)
    full_weights = jnp.exp(full_scores - full_lse[:, :, None])
    full_half = full_weights.astype(jnp.bfloat16)
    full_out = contract_cols(full_half, value_every)
    full_dot = jnp.sum(grad_every.astype(jnp.float32) * full_out, axis=2)
    full_gs = scores_grad(full_weights, grad_every, value_every, full_dot, score_scale)
    cores = lax.axis_size("c")
    chip_rows = block_rows * cores
    chip_start = (lax.axis_index(SEQ_AXES) - core) * block_rows
    query_part = lax.dynamic_slice_in_dim(full_gs, chip_start, chip_rows, 1)
    key_part = lax.dynamic_slice_in_dim(full_gs, chip_start, chip_rows, 2)
    half_part = lax.dynamic_slice_in_dim(full_half, chip_start, chip_rows, 2)
    head_results = jnp.stack(
        [
            contract_cols(query_part, key_every),
            contract_rows(key_part, query_every),
            contract_rows(half_part, grad_every),
        ]
    ).astype(jnp.bfloat16)
    both = lax.all_gather(head_results.reshape(3, chip_rows, HEAD_DIM), "c", axis=0)
    mine = lax.dynamic_slice_in_dim(both, core * block_rows, block_rows, 2)
    mine = jnp.transpose(mine, (1, 2, 0, 3)).reshape(3, block_rows, feature_width)
    self_dq, self_dk, self_dv = mine[0], mine[1], mine[2]
    return (cross_dq, prefix_dk, prefix_dv, self_dq, self_dk, self_dv)


SEQ_AXES = ("y", "zh", "x", "c")


def solution(mesh):
    sizes = dict(mesh.shape)
    split = mesh.devices.reshape(4, 2, 4, 2, sizes["head"])
    mesh = jax.sharding.Mesh(split, (*SEQ_AXES, "zl"))
    in_specs = (
        P(SEQ_AXES, "zl"),
        P(SEQ_AXES, "zl"),
        P(SEQ_AXES, "zl"),
        P(SEQ_AXES, "zl"),
        P(SEQ_AXES, "zl"),
        P(SEQ_AXES),
        P((*SEQ_AXES, "zl"), None),
        P((*SEQ_AXES, "zl"), None),
        P((*SEQ_AXES, "zl"), None),
        P((*SEQ_AXES, "zl"), None),
    )
    out_specs = (
        P(SEQ_AXES, "zl"),
        P(SEQ_AXES, "zl"),
        P(SEQ_AXES, "zl"),
        P(SEQ_AXES, "zl"),
        P(SEQ_AXES, "zl"),
        P(SEQ_AXES, "zl"),
    )
    return jax.shard_map(shards, mesh=mesh, in_specs=in_specs, out_specs=out_specs, check_vma=False)
```
